32 devices in a mesh: fsdp: 8 (over z, y), dp: 4 (over x, core).
Axes of the slice: x: 2, y: 2, z: 4, core: 2. Of those that a mesh axis runs over, the one named last changes fastest.
Arguments:
- tokens: bfloat16 [32768, 768], P(('fsdp', 'dp')), may hold values from -6 to 6
- image_table: int32 [160, 3], P(('fsdp', 'dp')), may hold values from 0 to 996, as said below
- ln1_gain: bfloat16 [768], P('fsdp'), may hold values from 0.5 to 1.5
- ln1_bias: bfloat16 [768], P('fsdp'), may hold values from -3 to 3
- qkv_weight: bfloat16 [768, 2304], P('fsdp'), may hold values from -0.21875 to 0.21875
- qkv_bias: bfloat16 [2304], P('fsdp'), may hold values from -2 to 2
- out_weight: bfloat16 [768, 768], P('fsdp'), may hold values from -0.875 to 0.875
- out_bias: bfloat16 [768], P('fsdp'), may hold values from -2 to 2
- ln2_gain: bfloat16 [768], P('fsdp'), may hold values from 0.5 to 1.5
- ln2_bias: bfloat16 [768], P('fsdp'), may hold values from -3 to 3
- fc1_weight: bfloat16 [768, 3072], P('fsdp'), may hold values from -0.21875 to 0.21875
- fc1_bias: bfloat16 [3072], P('fsdp'), may hold values from -3 to 3
- fc2_weight: bfloat16 [3072, 768], P('fsdp'), may hold values from -0.109375 to 0.109375
- fc2_bias: bfloat16 [768], P('fsdp'), may hold values from -2 to 2
- frequencies: bfloat16 [768], P('fsdp'), may hold values from -0.796875 to 0.796875
- cotangent: bfloat16 [32768, 768], P(('fsdp', 'dp')), may hold values from -6 to 6
Outputs:
- block_out: bfloat16 [32768, 768], P(('fsdp', 'dp'))
- tokens_grad: bfloat16 [32768, 768], P(('fsdp', 'dp'))
- first_norm_gain_gradient: float32 [768], P('fsdp')
- ln1_bias_grad: float32 [768], P('fsdp')
- qkv_weight_grad: float32 [768, 2304], P('fsdp')
- qkv_bias_grad: float32 [2304], P('fsdp')
- out_weight_grad: float32 [768, 768], P('fsdp')
- out_bias_grad: float32 [768], P('fsdp')
- second_norm_gain_gradient: float32 [768], P('fsdp')
- ln2_bias_grad: float32 [768], P('fsdp')
- fc1_weight_grad: float32 [768, 3072], P('fsdp')
- fc1_bias_grad: float32 [3072], P('fsdp')
- fc2_weight_grad: float32 [3072, 768], P('fsdp')
- fc2_bias_grad: float32 [768], P('fsdp')
- frequencies_grad: float32 [768], P('fsdp')
- freq_grad_norm: float32 [], replicated
- other_grad_norm: float32 [], replicated
The draws below stay inside these ranges and needn't reach their ends.
Inputs may be any that keep to these rules, and one draw needn't show every extreme that they name: `image_table`: rows 5b to 5b+4 describe bin b: either a 24x24 and a 20x20 image, or 24x24 and two 14x14, or two 20x20 and one 14x14, or one 20x20 and three 14x14, or five 14x14, laid end to end from offset 0 in the listed order; unused rows have height and width 0 and the offset where the used rows end. Grids are square.
All inputs are finite; a program needn't handle non-finite values.
Results may differ from the reference program's by a relative error of at most 0.015.
Values may be sent and summed in bfloat16 or wider, within the bound.
No kernel may reach another device: no remote copies, remote signals or barrier semaphores. Data moves between devices by JAX's collectives and lax.ppermute only.
A program may use at most 192 MiB of HBM per device.

```python
import jax
import jax.numpy as jnp
from jax import lax

D = 768
H = 12
HD = 64
FF = 3072
S1 = 14
S2 = 20
S3 = 24
BIN = 1024
BINS_DEV = 1
TOKENS = 32768
N_FSDP = 8
N_DP = 4


def draw_image_table(key, part):
    bin_total = N_FSDP * N_DP * BINS_DEV
    combos = jnp.array([[S3, S2, 0, 0, 0], [S3, S1, S1, 0, 0], [S2, S2, S1, 0, 0], [S2, S1, S1, S1, 0], [S1, S1, S1, S1, S1]], jnp.int32)
    picks = jax.random.randint(key, (bin_total,), 0, 5)
    order = jnp.arange(bin_total, dtype=jnp.int32)
    picks = jnp.where(order < 5, order, picks)
    sides = combos[picks]
    counts = sides * sides
    offsets = jnp.cumsum(counts, axis=1) - counts
    table = jnp.stack([offsets, sides, sides], axis=-1)
    return table.reshape(bin_total * 5, 3).astype(jnp.int32)


def block_levels(stream_key, shape, pieces, least, largest):
    gain, own = 1.0, jax.random.fold_in(stream_key, 6)
    for dim, shards_of in pieces:
        steps = jnp.exp(jax.random.uniform(jax.random.fold_in(own, dim), (shards_of,), jnp.float32, least / len(pieces), largest / len(pieces)))
        gain = gain * jnp.repeat(steps, shape[dim] // shards_of).reshape([-1 if axis == dim else 1 for axis in range(len(shape))])
    return gain


def normal_values(key, dims, spread, reach, split=(), held_as=jnp.bfloat16):
    factor_of = block_levels(key, dims, split, -0.22, 0.18) if split else 1.0
    values = jax.random.normal(key, dims, jnp.float32) * spread * factor_of
    return jnp.minimum(jnp.maximum(values, -reach), reach).astype(held_as)


def setup_inputs(seed: int = 0) -> dict:
    splits = jax.random.split(jax.random.key(seed), 17)
    return {
        "tokens": normal_values(splits[0], (TOKENS, D), 1.0, 6.0, ((0, 32),)),
        "image_table": draw_image_table(jax.random.fold_in(splits[16], 71), 0),
        "ln1_gain": jnp.clip(1.0 + 0.1 * jax.random.normal(splits[2], (D,), jnp.float32), 0.5, 1.5).astype(jnp.bfloat16),
        "ln1_bias": normal_values(splits[3], (D,), 0.5, 3.0, ((0, 8),)),
        "qkv_weight": normal_values(splits[4], (D, 3 * D), D ** -0.5, 0.21875, ((0, 8),)),
        "qkv_bias": normal_values(splits[5], (3 * D,), 0.3, 2.0, ((0, 8),)),
        "out_weight": normal_values(splits[6], (D, D), (D // 16) ** -0.5, 0.875, ((0, 8),)),
        "out_bias": normal_values(splits[7], (D,), 0.3, 2.0, ((0, 8),)),
        "ln2_gain": jnp.clip(1.0 + 0.1 * jax.random.normal(splits[8], (D,), jnp.float32), 0.5, 1.5).astype(jnp.bfloat16),
        "ln2_bias": normal_values(splits[9], (D,), 0.5, 3.0, ((0, 8),)),
        "fc1_weight": normal_values(splits[10], (D, FF), D ** -0.5, 0.21875, ((0, 8),)),
        "fc1_bias": normal_values(splits[11], (FF,), 0.5, 3.0, ((0, 8),)),
        "fc2_weight": normal_values(splits[12], (FF, D), FF ** -0.5, 0.109375, ((0, 8),)),
        "fc2_bias": normal_values(splits[13], (D,), 0.3, 2.0, ((0, 8),)),
        "frequencies": jnp.clip(jax.random.uniform(splits[14], (D,), jnp.float32, -0.796875, 0.796875) * block_levels(splits[14], (D,), ((0, 8),), -0.4, 0.0), -0.796875, 0.796875).astype(jnp.bfloat16),
        "cotangent": normal_values(splits[15], (TOKENS, D), 1.0, 6.0, ((0, 32),)),
    }


@jax.custom_vjp
def low(v):
    return lax.optimization_barrier(v.astype(jnp.bfloat16)).astype(jnp.float32)

@jax.custom_vjp
def low_back(v):
    return v

def low_keep(v):
    return (low(v), None)

def low_pass(kept, grad):
    return (grad,)

def back_keep(v):
    return (v, None)

def back_low(kept, grad):
    return (low(grad),)
low.defvjp(low_keep, low_pass)
low_back.defvjp(back_keep, back_low)

def matmul(left, right):
    return jnp.dot(left, right, precision=lax.Precision.HIGHEST, preferred_element_type=jnp.float32)

def image_layout(image_table, bin_count, bin_rows):
    slot_count = image_table.shape[0] // bin_count
    table = image_table.reshape(bin_count, slot_count, 3)
    offset = table[:, :, 0:1]
    height = table[:, :, 1:2]
    width = table[:, :, 2:3]
    place = jnp.arange(bin_rows, dtype=jnp.int32)[None, None, :]
    inside = ((place >= offset) & (place < offset + height * width)).astype(jnp.int32)
    live = lax.optimization_barrier(jnp.sum(inside, axis=1))
    slot_ids = jnp.arange(slot_count, dtype=jnp.int32)[None, :, None]
    segment = lax.optimization_barrier(jnp.sum(inside * slot_ids, axis=1)) + slot_count * (1 - live)
    local_place = place[:, 0, :] - lax.optimization_barrier(jnp.sum(inside * offset, axis=1))
    grid_width = jnp.maximum(lax.optimization_barrier(jnp.sum(inside * width, axis=1)), 1)
    grid_row = local_place // grid_width * live
    grid_col = local_place % grid_width * live
    return (segment, grid_row.reshape(-1).astype(jnp.float32), grid_col.reshape(-1).astype(jnp.float32))

def rotary_tables(frequencies, grid_row, grid_col):
    half_width = frequencies.shape[0] // 2
    freq_row = frequencies[:half_width].reshape(H, HD // 2)
    freq_col = frequencies[half_width:].reshape(H, HD // 2)
    theta = grid_row[:, None, None] * freq_row[None] + grid_col[:, None, None] * freq_col[None]
    return (jnp.cos(theta), jnp.sin(theta))

def rotate(heads, cosine, sine):
    half_width = heads.shape[-1] // 2
    first = heads[..., :half_width]
    second = heads[..., half_width:]
    return jnp.concatenate([first * cosine - second * sine, first * sine + second * cosine], axis=-1)

def layer_norm_forward(values):
    center = values - lax.optimization_barrier(jnp.mean(values, axis=-1, keepdims=True))
    return center * lax.rsqrt(lax.optimization_barrier(jnp.mean(center * center, axis=-1, keepdims=True)) + 1e-06)

def attend_bin(packed):
    query, key_rows, value, segment = packed
    mask = segment[:, None] == segment[None, :]
    scores = low_back(jnp.einsum('qhd,khd->hqk', query, key_rows, precision=lax.Precision.HIGHEST) * HD ** (-0.5))
    scores = jnp.where(mask[None], scores, -1e+30)
    probs = low(jax.nn.softmax(scores, axis=-1))
    return jnp.einsum('hqk,khd->qhd', probs, value, precision=lax.Precision.HIGHEST)

def block_forward(block_parameters, input_single_precision, segment, grid_row, grid_col):
    ln1_gain, ln1_bias, qkv_weight, qkv_bias, out_weight, out_bias, ln2_gain, ln2_bias, fc1_weight, fc1_bias, fc2_weight, fc2_bias, frequencies = block_parameters
    row_count = input_single_precision.shape[0]
    bin_count = row_count // BIN
    first_activation = low(layer_norm_forward(input_single_precision) * ln1_gain + ln1_bias)
    qkv_full = low_back(matmul(first_activation, qkv_weight) + qkv_bias)
    cosine, sine = rotary_tables(frequencies, grid_row, grid_col)
    q_low = low(rotate(qkv_full[:, :D].reshape(row_count, H, HD), cosine, sine))
    k_low = low(rotate(qkv_full[:, D:2 * D].reshape(row_count, H, HD), cosine, sine))
    v_low = low(qkv_full[:, 2 * D:].reshape(row_count, H, HD))
    attended = lax.map(jax.checkpoint(attend_bin), (q_low.reshape(bin_count, BIN, H, HD), k_low.reshape(bin_count, BIN, H, HD), v_low.reshape(bin_count, BIN, H, HD), segment))
    mixed = low(low_back(attended.reshape(row_count, D)))
    residual_stream = input_single_precision + low_back(matmul(mixed, out_weight) + out_bias)
    second_activation = low(layer_norm_forward(residual_stream) * ln2_gain + ln2_bias)
    up_proj = low_back(matmul(second_activation, fc1_weight) + fc1_bias)
    gelu_low = low(jax.nn.gelu(up_proj, approximate=False))
    return residual_stream + low_back(matmul(gelu_low, fc2_weight) + fc2_bias)

def reference(tokens, image_table, ln1_gain, ln1_bias, qkv_weight, qkv_bias, out_weight, out_bias, ln2_gain, ln2_bias, fc1_weight, fc1_bias, fc2_weight, fc2_bias, frequencies, cotangent):
    bin_count = TOKENS // BIN
    segment, grid_row, grid_col = image_layout(image_table, bin_count, BIN)
    block_parameters = tuple((member.astype(jnp.float32) for member in (ln1_gain, ln1_bias, qkv_weight, qkv_bias, out_weight, out_bias, ln2_gain, ln2_bias, fc1_weight, fc1_bias, fc2_weight, fc2_bias, frequencies)))
    input_single_precision = tokens.astype(jnp.float32)

    def forward_only(param_set, inputs):
        return block_forward(param_set, inputs, segment, grid_row, grid_col)
    result, pullback = jax.vjp(forward_only, block_parameters, input_single_precision)
    param_grads, input_grad = pullback(cotangent.astype(jnp.float32))
    freq_norm = jnp.sqrt(jnp.sum(param_grads[12] * param_grads[12]))
    other_sq = jnp.float32(0.0)
    for member in param_grads[:12]:
        other_sq = other_sq + jnp.sum(member * member)
    return (result.astype(jnp.bfloat16), input_grad.astype(jnp.bfloat16), param_grads[0], param_grads[1], param_grads[2], param_grads[3], param_grads[4], param_grads[5], param_grads[6], param_grads[7], param_grads[8], param_grads[9], param_grads[10], param_grads[11], param_grads[12], freq_norm, jnp.sqrt(other_sq))
```

```python
import jax
import jax.numpy as jnp
from jax import lax
from jax.sharding import PartitionSpec as P


H = 12
HD = 64
BIN = 1024
PACK_ROWS = 16


norm_eps = 1e-06
masked_score = -1e30
inv_sqrt_two_pi = 0.3989422804014327


def matmul(left, right):
    return jnp.dot(left, right, preferred_element_type=jnp.float32)


def matmul_left_t(left, right):
    return lax.dot_general(
        left, right, (((0,), (0,)), ((), ())), preferred_element_type=jnp.float32
    )


def matmul_right_t(left, right):
    return lax.dot_general(
        left, right, (((1,), (1,)), ((), ())), preferred_element_type=jnp.float32
    )


def image_layout(image_table, bin_count, bin_rows):
    slot_count = image_table.shape[0] // bin_count
    table = image_table.reshape(bin_count, slot_count, 3)
    offset = table[:, :, 0:1]
    height = table[:, :, 1:2]
    width = table[:, :, 2:3]
    place = jnp.arange(bin_rows, dtype=jnp.int32)[None, None, :]
    inside = ((place >= offset) & (place < offset + height * width)).astype(jnp.int32)
    live = jnp.sum(inside, axis=1)
    slot_ids = jnp.arange(slot_count, dtype=jnp.int32)[None, :, None]
    segment = jnp.sum(inside * slot_ids, axis=1) + slot_count * (1 - live)
    local_place = place[:, 0, :] - jnp.sum(inside * offset, axis=1)
    grid_width = jnp.maximum(jnp.sum(inside * width, axis=1), 1)
    grid_row = local_place // grid_width * live
    grid_col = local_place % grid_width * live
    return (
        segment,
        grid_row.reshape(-1).astype(jnp.float32),
        grid_col.reshape(-1).astype(jnp.float32),
    )


def rotary_tables(frequencies, grid_row, grid_col):
    half_width = frequencies.shape[0] // 2
    freq_float = frequencies.astype(jnp.float32)
    freq_row = freq_float[:half_width].reshape(H, HD // 2)
    freq_col = freq_float[half_width:].reshape(H, HD // 2)
    theta = grid_row[:, None, None] * freq_row[None] + grid_col[:, None, None] * freq_col[None]
    return (jnp.cos(theta), jnp.sin(theta))


def rotate(heads, cosine, sine):
    half_width = heads.shape[-1] // 2
    first = heads[..., :half_width]
    second = heads[..., half_width:]
    return jnp.concatenate(
        [first * cosine - second * sine, first * sine + second * cosine], axis=-1
    )


def layer_norm_forward(values):
    center = values - jnp.mean(values, axis=-1, keepdims=True)
    inverse_deviation = lax.rsqrt(jnp.mean(center * center, axis=-1, keepdims=True) + norm_eps)
    return (center * inverse_deviation, inverse_deviation)


def layer_norm_backward(
    gradient_norm_total, centered_normalized, inverse_deviation, norm_gain_vector
):
    gain_scaled_output = gradient_norm_total * norm_gain_vector
    return inverse_deviation * (
        gain_scaled_output
        - jnp.mean(gain_scaled_output, axis=-1, keepdims=True)
        - centered_normalized
        * jnp.mean(gain_scaled_output * centered_normalized, axis=-1, keepdims=True)
    )


def gelu_slope(values):
    return (
        0.5 * (1.0 + lax.erf(values * 0.7071067811865476))
        + values * jnp.exp(-0.5 * values * values) * inv_sqrt_two_pi
    )


def join_heads(stacked):
    return jnp.transpose(stacked, (1, 0, 2)).reshape(stacked.shape[1], H * HD)


def head_slice(matrix, head_index):
    return lax.dynamic_slice_in_dim(matrix, head_index * HD, HD, 1)


def attend_bin(packed):
    query, key_rows, value, segment = packed
    mask = segment[:, None] == segment[None, :]
    scale = HD ** (-0.5)

    def one_head(head_index):
        q_head = head_slice(query, head_index)
        k_head = head_slice(key_rows, head_index)
        v_head = head_slice(value, head_index)
        scores = jnp.where(mask, matmul_right_t(q_head, k_head) * scale, masked_score)
        top = jnp.max(scores, axis=-1, keepdims=True)
        log_total = top + jnp.log(jnp.sum(jnp.exp(scores - top), axis=-1, keepdims=True))
        probs = jnp.exp(scores - log_total).astype(jnp.bfloat16)
        return (matmul(probs, v_head).astype(jnp.bfloat16), log_total[:, 0])

    mixed, log_total = lax.map(one_head, jnp.arange(H, dtype=jnp.int32))
    return (join_heads(mixed), log_total)


def attend_bin_back(packed):
    query, key_rows, value, d_mixed, log_total, segment = packed
    mask = segment[:, None] == segment[None, :]
    scale = HD ** (-0.5)

    def one_head(head_index):
        q_head = head_slice(query, head_index)
        k_head = head_slice(key_rows, head_index)
        v_head = head_slice(value, head_index)
        d_head = head_slice(d_mixed, head_index)
        total_head = lax.dynamic_index_in_dim(log_total, head_index, 0, keepdims=False)
        scores = jnp.where(mask, matmul_right_t(q_head, k_head) * scale, masked_score)
        probs = jnp.exp(scores - total_head[:, None])
        d_probs = matmul_right_t(d_head, v_head)
        d_value = matmul_left_t(probs.astype(jnp.bfloat16), d_head)
        inner = jnp.sum(probs * d_probs, axis=-1, keepdims=True)
        d_scores = (probs * (d_probs - inner)).astype(jnp.bfloat16)
        d_query = matmul(d_scores, k_head) * scale
        d_key = matmul_left_t(d_scores, q_head) * scale
        return (d_query, d_key, d_value)

    d_query, d_key, d_value = lax.map(one_head, jnp.arange(H, dtype=jnp.int32))
    return (join_heads(d_query), join_heads(d_key), join_heads(d_value))


def square_sums(pieces):
    freq_sq = jnp.sum(pieces[12] * pieces[12])
    other_sq = jnp.float32(0.0)
    for member in pieces[:12]:
        other_sq = other_sq + jnp.sum(member * member)
    return (freq_sq, other_sq)


def gather_weight(shard):
    pieces = lax.psum(1, "dp")
    part = shard.shape[0] // pieces
    mine = lax.dynamic_slice_in_dim(shard, lax.axis_index("dp") * part, part, 0)
    return lax.all_gather(mine, ("fsdp", "dp"), axis=0, tiled=True)


def gather_small(vectors):
    sizes = [v.shape[0] for v in vectors]
    packed = lax.all_gather(jnp.concatenate(vectors), "fsdp", axis=0, tiled=False)
    out, at = [], 0
    for n in sizes:
        out.append(packed[:, at : at + n].reshape(-1))
        at += n
    return out


def reduce_grads(grads):
    blocks = lax.psum(1, ("fsdp", "dp"))
    flats = [g.reshape(blocks, -1).astype(jnp.bfloat16) for g in grads]
    sizes = [f.shape[1] for f in flats]
    total = sum(sizes)
    padded = -(-total // (PACK_ROWS * 128)) * PACK_ROWS * 128
    if padded > total:
        flats.append(jnp.zeros((blocks, padded - total), jnp.bfloat16))
    packed = jnp.concatenate(flats, axis=1).reshape(blocks * PACK_ROWS, padded // PACK_ROWS)
    return packed, sizes


def finish_grads(packed, sizes, shapes):
    mine = lax.psum_scatter(packed, ("fsdp", "dp"), scatter_dimension=0, tiled=True)
    owned = lax.all_gather(mine, "dp", axis=0, tiled=True)
    owned = owned.reshape(lax.psum(1, "dp"), -1)
    out, at = [], 0
    for n, shape in zip(sizes, shapes):
        out.append(owned[:, at : at + n].reshape(shape).astype(jnp.float32))
        at += n
    return out


def shards(
    tokens,
    image_table,
    ln1_gain,
    ln1_bias,
    qkv_weight,
    qkv_bias,
    out_weight,
    out_bias,
    ln2_gain,
    ln2_bias,
    fc1_weight,
    fc1_bias,
    fc2_weight,
    fc2_bias,
    frequencies,
    cotangent,
):
    small_local = (ln1_gain, ln1_bias, qkv_bias, out_bias, ln2_gain, ln2_bias, fc1_bias, fc2_bias, frequencies)
    (g_ln1_gain, g_ln1_bias, g_qkv_bias, g_out_bias, g_ln2_gain, g_ln2_bias, g_fc1_bias, g_fc2_bias,
     g_frequencies) = gather_small(small_local)
    block_parameters = (
        g_ln1_gain,
        g_ln1_bias,
        gather_weight(qkv_weight),
        g_qkv_bias,
        gather_weight(out_weight),
        g_out_bias,
        g_ln2_gain,
        g_ln2_bias,
        gather_weight(fc1_weight),
        g_fc1_bias,
        gather_weight(fc2_weight),
        g_fc2_bias,
        g_frequencies,
    )
    row_count, width = tokens.shape
    bin_count = row_count // BIN
    half_head = HD // 2
    segment, grid_row, grid_col = image_layout(image_table, bin_count, BIN)
    cosine, sine = rotary_tables(block_parameters[12], grid_row, grid_col)
    input_single_precision = tokens.astype(jnp.float32)
    first_centered_normalized, first_inverse_deviation = layer_norm_forward(input_single_precision)
    first_activation = (
        first_centered_normalized * block_parameters[0].astype(jnp.float32)
        + block_parameters[1].astype(jnp.float32)
    ).astype(jnp.bfloat16)
    qkv_full = matmul(first_activation, block_parameters[2]) + block_parameters[3].astype(
        jnp.float32
    )
    q_rot = rotate(qkv_full[:, :width].reshape(row_count, H, HD), cosine, sine)
    k_rot = rotate(qkv_full[:, width : 2 * width].reshape(row_count, H, HD), cosine, sine)
    q_low = q_rot.reshape(row_count, width).astype(jnp.bfloat16)
    k_low = k_rot.reshape(row_count, width).astype(jnp.bfloat16)
    v_low = qkv_full[:, 2 * width :].astype(jnp.bfloat16)
    q_bins = q_low.reshape(bin_count, BIN, width)
    k_bins = k_low.reshape(bin_count, BIN, width)
    v_bins = v_low.reshape(bin_count, BIN, width)
    mixed, log_total = lax.map(attend_bin, (q_bins, k_bins, v_bins, segment))
    mixed = mixed.reshape(row_count, width)
    residual_stream = (
        input_single_precision
        + matmul(mixed, block_parameters[4])
        + block_parameters[5].astype(jnp.float32)
    )
    second_centered_normalized, second_inverse_deviation = layer_norm_forward(residual_stream)
    second_activation = (
        second_centered_normalized * block_parameters[6].astype(jnp.float32)
        + block_parameters[7].astype(jnp.float32)
    ).astype(jnp.bfloat16)
    up_proj = matmul(second_activation, block_parameters[8]) + block_parameters[9].astype(
        jnp.float32
    )
    gelu_low = jax.nn.gelu(up_proj, approximate=False).astype(jnp.bfloat16)
    block_out = (
        residual_stream
        + matmul(gelu_low, block_parameters[10])
        + block_parameters[11].astype(jnp.float32)
    ).astype(jnp.bfloat16)
    output_gradient = cotangent.astype(jnp.float32)
    fc2_bias_grad = jnp.sum(output_gradient, axis=0)
    fc2_weight_grad = matmul_left_t(gelu_low, cotangent)
    d_up = (matmul_right_t(cotangent, block_parameters[10]) * gelu_slope(up_proj)).astype(
        jnp.bfloat16
    )
    fc1_bias_grad = jnp.sum(d_up.astype(jnp.float32), axis=0)
    fc1_weight_grad = matmul_left_t(second_activation, d_up)
    second_activation_gradient = matmul_right_t(d_up, block_parameters[8])
    second_norm_gain_gradient = jnp.sum(
        second_activation_gradient * second_centered_normalized, axis=0
    )
    ln2_bias_grad = jnp.sum(second_activation_gradient, axis=0)
    residual_gradient = output_gradient + layer_norm_backward(
        second_activation_gradient,
        second_centered_normalized,
        second_inverse_deviation,
        block_parameters[6].astype(jnp.float32),
    )
    d_att = residual_gradient.astype(jnp.bfloat16)
    out_bias_grad = jnp.sum(d_att.astype(jnp.float32), axis=0)
    out_weight_grad = matmul_left_t(mixed, d_att)
    d_mixed = matmul_right_t(d_att, block_parameters[4]).astype(jnp.bfloat16)
    early_packed, early_sizes = reduce_grads(
        (fc2_weight_grad, fc1_weight_grad, out_weight_grad, fc2_bias_grad, fc1_bias_grad,
         out_bias_grad, second_norm_gain_gradient, ln2_bias_grad)
    )
    early_packed, d_mixed = lax.optimization_barrier((early_packed, d_mixed))
    early_owned = finish_grads(
        early_packed,
        early_sizes,
        (fc2_weight.shape, fc1_weight.shape, out_weight.shape, fc2_bias.shape, fc1_bias.shape,
         out_bias.shape, ln2_gain.shape, ln2_bias.shape),
    )
    d_qrot, d_krot, d_value = lax.map(
        attend_bin_back,
        (q_bins, k_bins, v_bins, d_mixed.reshape(bin_count, BIN, width), log_total, segment),
    )
    d_qrot = d_qrot.reshape(row_count, H, HD)
    d_krot = d_krot.reshape(row_count, H, HD)
    d_theta = (
        d_qrot[..., half_head:] * q_rot[..., :half_head]
        - d_qrot[..., :half_head] * q_rot[..., half_head:]
    )
    d_theta = (
        d_theta
        + d_krot[..., half_head:] * k_rot[..., :half_head]
        - d_krot[..., :half_head] * k_rot[..., half_head:]
    )
    frequencies_grad = jnp.concatenate(
        [
            jnp.sum(grid_row[:, None, None] * d_theta, axis=0).reshape(-1),
            jnp.sum(grid_col[:, None, None] * d_theta, axis=0).reshape(-1),
        ]
    )
    d_query = rotate(d_qrot, cosine, -sine).reshape(row_count, width)
    d_key = rotate(d_krot, cosine, -sine).reshape(row_count, width)
    d_qkv = jnp.concatenate([d_query, d_key, d_value.reshape(row_count, width)], axis=1).astype(
        jnp.bfloat16
    )
    qkv_bias_grad = jnp.sum(d_qkv.astype(jnp.float32), axis=0)
    qkv_weight_grad = matmul_left_t(first_activation, d_qkv)
    first_activation_gradient = matmul_right_t(d_qkv, block_parameters[2])
    first_norm_gain_gradient = jnp.sum(
        first_activation_gradient * first_centered_normalized, axis=0
    )
    ln1_bias_grad = jnp.sum(first_activation_gradient, axis=0)
    tokens_grad = (
        residual_gradient
        + layer_norm_backward(
            first_activation_gradient,
            first_centered_normalized,
            first_inverse_deviation,
            block_parameters[0].astype(jnp.float32),
        )
    ).astype(jnp.bfloat16)
    late_packed, late_sizes = reduce_grads(
        (qkv_weight_grad, qkv_bias_grad, first_norm_gain_gradient, ln1_bias_grad, frequencies_grad)
    )
    late_owned = finish_grads(
        late_packed,
        late_sizes,
        (qkv_weight.shape, qkv_bias.shape, ln1_gain.shape, ln1_bias.shape, frequencies.shape),
    )
    (fc2_weight_g, fc1_weight_g, out_weight_g, fc2_bias_g, fc1_bias_g, out_bias_g, ln2_gain_g,
     ln2_bias_g) = early_owned
    qkv_weight_g, qkv_bias_g, ln1_gain_g, ln1_bias_g, frequencies_g = late_owned
    pieces = (
        ln1_gain_g,
        ln1_bias_g,
        qkv_weight_g,
        qkv_bias_g,
        out_weight_g,
        out_bias_g,
        ln2_gain_g,
        ln2_bias_g,
        fc1_weight_g,
        fc1_bias_g,
        fc2_weight_g,
        fc2_bias_g,
        frequencies_g,
    )
    freq_sq, other_sq = square_sums(pieces)
    freq_sq, other_sq = lax.psum((freq_sq, other_sq), "fsdp")
    return (
        block_out,
        tokens_grad,
        *pieces,
        jnp.sqrt(freq_sq),
        jnp.sqrt(other_sq),
    )


def solution(mesh):
    placed = (
        P(("fsdp", "dp"), None),
        P(("fsdp", "dp"), None),
        P("fsdp"),
        P("fsdp"),
        P("fsdp", None),
        P("fsdp"),
        P("fsdp", None),
        P("fsdp"),
        P("fsdp"),
        P("fsdp"),
        P("fsdp", None),
        P("fsdp"),
        P("fsdp", None),
        P("fsdp"),
        P("fsdp"),
        P(("fsdp", "dp"), None),
    )
    return jax.shard_map(
        shards,
        mesh=mesh,
        in_specs=placed,
        out_specs=(
            P(("fsdp", "dp"), None),
            P(("fsdp", "dp"), None),
            P("fsdp"),
            P("fsdp"),
            P("fsdp", None),
            P("fsdp"),
            P("fsdp", None),
            P("fsdp"),
            P("fsdp"),
            P("fsdp"),
            P("fsdp", None),
            P("fsdp"),
            P("fsdp", None),
            P("fsdp"),
            P("fsdp"),
            P(),
            P(),
        ),
        check_vma=False,
    )
```

```python
import jax
import jax.numpy as jnp
from jax import lax
from jax.experimental import pallas as pl
from jax.sharding import PartitionSpec as P


H = 12
HD = 64
BIN = 1024
Q_BLOCK = 256
PACK_ROWS = 16


norm_eps = 1e-06
masked_score = -1e30
inv_sqrt_two_pi = 0.3989422804014327


def matmul(left, right):
    return jnp.dot(left, right, preferred_element_type=jnp.float32)


def matmul_left_t(left, right):
    return lax.dot_general(
        left, right, (((0,), (0,)), ((), ())), preferred_element_type=jnp.float32
    )


def matmul_right_t(left, right):
    return lax.dot_general(
        left, right, (((1,), (1,)), ((), ())), preferred_element_type=jnp.float32
    )


def image_layout(image_table, bin_count, bin_rows):
    slot_count = image_table.shape[0] // bin_count
    table = image_table.reshape(bin_count, slot_count, 3)
    offset = table[:, :, 0:1]
    height = table[:, :, 1:2]
    width = table[:, :, 2:3]
    place = jnp.arange(bin_rows, dtype=jnp.int32)[None, None, :]
    inside = ((place >= offset) & (place < offset + height * width)).astype(jnp.int32)
    live = jnp.sum(inside, axis=1)
    slot_ids = jnp.arange(slot_count, dtype=jnp.int32)[None, :, None]
    segment = jnp.sum(inside * slot_ids, axis=1) + slot_count * (1 - live)
    local_place = place[:, 0, :] - jnp.sum(inside * offset, axis=1)
    grid_width = jnp.maximum(jnp.sum(inside * width, axis=1), 1)
    grid_row = local_place // grid_width * live
    grid_col = local_place % grid_width * live
    return (
        segment,
        grid_row.reshape(-1).astype(jnp.float32),
        grid_col.reshape(-1).astype(jnp.float32),
    )


def rotary_tables(frequencies, grid_row, grid_col):
    half_width = frequencies.shape[0] // 2
    freq_float = frequencies.astype(jnp.float32)
    freq_row = freq_float[:half_width].reshape(H, HD // 2)
    freq_col = freq_float[half_width:].reshape(H, HD // 2)
    theta = grid_row[:, None, None] * freq_row[None] + grid_col[:, None, None] * freq_col[None]
    return (jnp.cos(theta), jnp.sin(theta))


def rotate(heads, cosine, sine):
    half_width = heads.shape[-1] // 2
    first = heads[..., :half_width]
    second = heads[..., half_width:]
    return jnp.concatenate(
        [first * cosine - second * sine, first * sine + second * cosine], axis=-1
    )


def layer_norm_forward(values):
    center = values - jnp.mean(values, axis=-1, keepdims=True)
    inverse_deviation = lax.rsqrt(jnp.mean(center * center, axis=-1, keepdims=True) + norm_eps)
    return (center * inverse_deviation, inverse_deviation)


def layer_norm_backward(
    gradient_norm_total, centered_normalized, inverse_deviation, norm_gain_vector
):
    gain_scaled_output = gradient_norm_total * norm_gain_vector
    return inverse_deviation * (
        gain_scaled_output
        - jnp.mean(gain_scaled_output, axis=-1, keepdims=True)
        - centered_normalized
        * jnp.mean(gain_scaled_output * centered_normalized, axis=-1, keepdims=True)
    )


def gelu_slope(values):
    return (
        0.5 * (1.0 + lax.erf(values * 0.7071067811865476))
        + values * jnp.exp(-0.5 * values * values) * inv_sqrt_two_pi
    )


def _nt(a, b):
    return lax.dot_general(a, b, (((1,), (1,)), ((), ())), preferred_element_type=jnp.float32)


def _tn(a, b):
    return lax.dot_general(a, b, (((0,), (0,)), ((), ())), preferred_element_type=jnp.float32)


def _nn(a, b):
    return lax.dot_general(a, b, (((1,), (0,)), ((), ())), preferred_element_type=jnp.float32)


def attention_forward_kernel(q_ref, k_ref, v_ref, seg_r_ref, seg_c_ref, o_ref, lse_ref):
    rows = q_ref.shape[0]
    seg_c = seg_c_ref[...]
    scale = HD ** (-0.5)
    for half in range(q_ref.shape[1] // HD):
        cols = slice(half * HD, (half + 1) * HD)
        k_h = k_ref[:, cols]
        v_h = v_ref[:, cols]

        def block(i, carry):
            at = pl.multiple_of(i * Q_BLOCK, Q_BLOCK)
            q_h = q_ref[pl.ds(at, Q_BLOCK), cols]
            mask = seg_r_ref[pl.ds(at, Q_BLOCK), :] == seg_c
            scores = jnp.where(mask, _nt(q_h, k_h) * scale, masked_score)
            top = jnp.max(scores, axis=-1, keepdims=True)
            log_total = top + jnp.log(jnp.sum(jnp.exp(scores - top), axis=-1, keepdims=True))
            probs = jnp.exp(scores - log_total).astype(jnp.bfloat16)
            o_ref[pl.ds(at, Q_BLOCK), cols] = _nn(probs, v_h).astype(o_ref.dtype)
            lse_ref[pl.ds(at, Q_BLOCK), cols] = jnp.broadcast_to(log_total, (Q_BLOCK, HD))
            return carry

        lax.fori_loop(0, rows // Q_BLOCK, block, 0)


def attention_backward_kernel(q_ref, k_ref, v_ref, d_ref, lse_ref, seg_r_ref, seg_c_ref, dq_ref, dk_ref, dv_ref):
    rows = q_ref.shape[0]
    seg_c = seg_c_ref[...]
    scale = HD ** (-0.5)
    for half in range(q_ref.shape[1] // HD):
        cols = slice(half * HD, (half + 1) * HD)
        k_h = k_ref[:, cols]
        v_h = v_ref[:, cols]

        def block(i, carry):
            dk_acc, dv_acc = carry
            at = pl.multiple_of(i * Q_BLOCK, Q_BLOCK)
            q_h = q_ref[pl.ds(at, Q_BLOCK), cols]
            d_h = d_ref[pl.ds(at, Q_BLOCK), cols]
            log_total = lse_ref[pl.ds(at, Q_BLOCK), pl.ds(half * HD, 1)]
            mask = seg_r_ref[pl.ds(at, Q_BLOCK), :] == seg_c
            scores = jnp.where(mask, _nt(q_h, k_h) * scale, masked_score)
            probs = jnp.exp(scores - log_total)
            d_probs = _nt(d_h, v_h)
            dv_acc = dv_acc + _tn(probs.astype(jnp.bfloat16), d_h)
            inner = jnp.sum(probs * d_probs, axis=-1, keepdims=True)
            d_scores = (probs * (d_probs - inner)).astype(jnp.bfloat16)
            dq_ref[pl.ds(at, Q_BLOCK), cols] = _nn(d_scores, k_h) * scale
            dk_acc = dk_acc + _tn(d_scores, q_h)
            return dk_acc, dv_acc

        zero = jnp.zeros((rows, HD), jnp.float32)
        dk_acc, dv_acc = lax.fori_loop(0, rows // Q_BLOCK, block, (zero, zero))
        dk_ref[:, cols] = dk_acc * scale
        dv_ref[:, cols] = dv_acc


def attention_forward(q, k, v, segment):
    rows, width = q.shape
    pair = 2 * HD
    seg_r = segment.reshape(rows, 1)
    seg_c = segment.reshape(1, rows)
    spec = pl.BlockSpec((rows, pair), lambda j: (0, j))
    return pl.pallas_call(
        attention_forward_kernel,
        grid=(width // pair,),
        in_specs=[spec, spec, spec, pl.BlockSpec((rows, 1), lambda j: (0, 0)), pl.BlockSpec((1, rows), lambda j: (0, 0))],
        out_specs=[spec, spec],
        out_shape=[jax.ShapeDtypeStruct((rows, width), jnp.bfloat16), jax.ShapeDtypeStruct((rows, width), jnp.float32)],
        cost_estimate=pl.CostEstimate(
            flops=4 * rows * rows * width, transcendentals=2 * rows * rows * (width // HD),
            bytes_accessed=rows * width * (2 * 4 + 4)),
        name="attention_forward",
    )(q, k, v, seg_r, seg_c)


def attention_backward(q, k, v, d_mixed, log_total, segment):
    rows, width = q.shape
    pair = 2 * HD
    seg_r = segment.reshape(rows, 1)
    seg_c = segment.reshape(1, rows)
    spec = pl.BlockSpec((rows, pair), lambda j: (0, j))
    f32 = jax.ShapeDtypeStruct((rows, width), jnp.float32)
    return pl.pallas_call(
        attention_backward_kernel,
        grid=(width // pair,),
        in_specs=[spec, spec, spec, spec, spec, pl.BlockSpec((rows, 1), lambda j: (0, 0)), pl.BlockSpec((1, rows), lambda j: (0, 0))],
        out_specs=[spec, spec, spec],
        out_shape=[f32, f32, f32],
        cost_estimate=pl.CostEstimate(
            flops=8 * rows * rows * width, transcendentals=rows * rows * (width // HD),
            bytes_accessed=rows * width * (2 * 4 + 4 + 12)),
        name="attention_backward",
    )(q, k, v, d_mixed, log_total, seg_r, seg_c)


def attention_bins(q_low, k_low, v_low, segment):
    outs = [attention_forward(q_low[b * BIN:(b + 1) * BIN], k_low[b * BIN:(b + 1) * BIN],
                              v_low[b * BIN:(b + 1) * BIN], segment[b]) for b in range(segment.shape[0])]
    return tuple(jnp.concatenate(parts, axis=0) for parts in zip(*outs))


def attention_bins_back(q_low, k_low, v_low, d_mixed, log_total, segment):
    outs = [attention_backward(q_low[b * BIN:(b + 1) * BIN], k_low[b * BIN:(b + 1) * BIN],
                               v_low[b * BIN:(b + 1) * BIN], d_mixed[b * BIN:(b + 1) * BIN],
                               log_total[b * BIN:(b + 1) * BIN], segment[b]) for b in range(segment.shape[0])]
    return tuple(jnp.concatenate(parts, axis=0) for parts in zip(*outs))


def square_sums(pieces):
    freq_sq = jnp.sum(pieces[12] * pieces[12])
    other_sq = jnp.float32(0.0)
    for member in pieces[:12]:
        other_sq = other_sq + jnp.sum(member * member)
    return (freq_sq, other_sq)


def gather_weight(shard):
    pieces = lax.psum(1, "dp")
    part = shard.shape[0] // pieces
    mine = lax.dynamic_slice_in_dim(shard, lax.axis_index("dp") * part, part, 0)
    return lax.all_gather(mine, ("fsdp", "dp"), axis=0, tiled=True)


def gather_small(vectors):
    sizes = [v.shape[0] for v in vectors]
    packed = lax.all_gather(jnp.concatenate(vectors), "fsdp", axis=0, tiled=False)
    out, at = [], 0
    for n in sizes:
        out.append(packed[:, at : at + n].reshape(-1))
        at += n
    return out


def reduce_grads(grads):
    blocks = lax.psum(1, ("fsdp", "dp"))
    flats = [g.reshape(blocks, -1).astype(jnp.bfloat16) for g in grads]
    sizes = [f.shape[1] for f in flats]
    total = sum(sizes)
    padded = -(-total // (PACK_ROWS * 128)) * PACK_ROWS * 128
    if padded > total:
        flats.append(jnp.zeros((blocks, padded - total), jnp.bfloat16))
    packed = jnp.concatenate(flats, axis=1).reshape(blocks * PACK_ROWS, padded // PACK_ROWS)
    return packed, sizes


def finish_grads(packed, sizes, shapes):
    mine = lax.psum_scatter(packed, ("fsdp", "dp"), scatter_dimension=0, tiled=True)
    owned = lax.all_gather(mine, "dp", axis=0, tiled=True)
    owned = owned.reshape(lax.psum(1, "dp"), -1)
    out, at = [], 0
    for n, shape in zip(sizes, shapes):
        out.append(owned[:, at : at + n].reshape(shape).astype(jnp.float32))
        at += n
    return out


def shards(
    tokens,
    image_table,
    ln1_gain,
    ln1_bias,
    qkv_weight,
    qkv_bias,
    out_weight,
    out_bias,
    ln2_gain,
    ln2_bias,
    fc1_weight,
    fc1_bias,
    fc2_weight,
    fc2_bias,
    frequencies,
    cotangent,
):
    small_local = (ln1_gain, ln1_bias, qkv_bias, out_bias, ln2_gain, ln2_bias, fc1_bias, fc2_bias, frequencies)
    (g_ln1_gain, g_ln1_bias, g_qkv_bias, g_out_bias, g_ln2_gain, g_ln2_bias, g_fc1_bias, g_fc2_bias,
     g_frequencies) = gather_small(small_local)
    block_parameters = (
        g_ln1_gain,
        g_ln1_bias,
        gather_weight(qkv_weight),
        g_qkv_bias,
        gather_weight(out_weight),
        g_out_bias,
        g_ln2_gain,
        g_ln2_bias,
        gather_weight(fc1_weight),
        g_fc1_bias,
        gather_weight(fc2_weight),
        g_fc2_bias,
        g_frequencies,
    )
    row_count, width = tokens.shape
    bin_count = row_count // BIN
    half_head = HD // 2
    segment, grid_row, grid_col = image_layout(image_table, bin_count, BIN)
    cosine, sine = rotary_tables(block_parameters[12], grid_row, grid_col)
    input_single_precision = tokens.astype(jnp.float32)
    first_centered_normalized, first_inverse_deviation = layer_norm_forward(input_single_precision)
    first_activation = (
        first_centered_normalized * block_parameters[0].astype(jnp.float32)
        + block_parameters[1].astype(jnp.float32)
    ).astype(jnp.bfloat16)
    qkv_full = matmul(first_activation, block_parameters[2]) + block_parameters[3].astype(
        jnp.float32
    )
    q_rot = rotate(qkv_full[:, :width].reshape(row_count, H, HD), cosine, sine)
    k_rot = rotate(qkv_full[:, width : 2 * width].reshape(row_count, H, HD), cosine, sine)
    q_low = q_rot.reshape(row_count, width).astype(jnp.bfloat16)
    k_low = k_rot.reshape(row_count, width).astype(jnp.bfloat16)
    v_low = qkv_full[:, 2 * width :].astype(jnp.bfloat16)
    mixed, log_total = attention_bins(q_low, k_low, v_low, segment)
    residual_stream = (
        input_single_precision
        + matmul(mixed, block_parameters[4])
        + block_parameters[5].astype(jnp.float32)
    )
    second_centered_normalized, second_inverse_deviation = layer_norm_forward(residual_stream)
    second_activation = (
        second_centered_normalized * block_parameters[6].astype(jnp.float32)
        + block_parameters[7].astype(jnp.float32)
    ).astype(jnp.bfloat16)
    up_proj = matmul(second_activation, block_parameters[8]) + block_parameters[9].astype(
        jnp.float32
    )
    gelu_low = jax.nn.gelu(up_proj, approximate=False).astype(jnp.bfloat16)
    block_out = (
        residual_stream
        + matmul(gelu_low, block_parameters[10])
        + block_parameters[11].astype(jnp.float32)
    ).astype(jnp.bfloat16)
    output_gradient = cotangent.astype(jnp.float32)
    fc2_bias_grad = jnp.sum(output_gradient, axis=0)
    fc2_weight_grad = matmul_left_t(gelu_low, cotangent)
    d_up = (matmul_right_t(cotangent, block_parameters[10]) * gelu_slope(up_proj)).astype(
        jnp.bfloat16
    )
    fc1_bias_grad = jnp.sum(d_up.astype(jnp.float32), axis=0)
    fc1_weight_grad = matmul_left_t(second_activation, d_up)
    second_activation_gradient = matmul_right_t(d_up, block_parameters[8])
    second_norm_gain_gradient = jnp.sum(
        second_activation_gradient * second_centered_normalized, axis=0
    )
    ln2_bias_grad = jnp.sum(second_activation_gradient, axis=0)
    residual_gradient = output_gradient + layer_norm_backward(
        second_activation_gradient,
        second_centered_normalized,
        second_inverse_deviation,
        block_parameters[6].astype(jnp.float32),
    )
    d_att = residual_gradient.astype(jnp.bfloat16)
    out_bias_grad = jnp.sum(d_att.astype(jnp.float32), axis=0)
    out_weight_grad = matmul_left_t(mixed, d_att)
    d_mixed = matmul_right_t(d_att, block_parameters[4]).astype(jnp.bfloat16)
    early_packed, early_sizes = reduce_grads(
        (fc2_weight_grad, fc1_weight_grad, out_weight_grad, fc2_bias_grad, fc1_bias_grad,
         out_bias_grad, second_norm_gain_gradient, ln2_bias_grad)
    )
    early_packed, d_mixed = lax.optimization_barrier((early_packed, d_mixed))
    early_owned = finish_grads(
        early_packed,
        early_sizes,
        (fc2_weight.shape, fc1_weight.shape, out_weight.shape, fc2_bias.shape, fc1_bias.shape,
         out_bias.shape, ln2_gain.shape, ln2_bias.shape),
    )
    d_qrot, d_krot, d_value = attention_bins_back(q_low, k_low, v_low, d_mixed, log_total, segment)
    d_qrot = d_qrot.reshape(row_count, H, HD)
    d_krot = d_krot.reshape(row_count, H, HD)
    d_theta = (
        d_qrot[..., half_head:] * q_rot[..., :half_head]
        - d_qrot[..., :half_head] * q_rot[..., half_head:]
    )
    d_theta = (
        d_theta
        + d_krot[..., half_head:] * k_rot[..., :half_head]
        - d_krot[..., :half_head] * k_rot[..., half_head:]
    )
    frequencies_grad = jnp.concatenate(
        [
            jnp.sum(grid_row[:, None, None] * d_theta, axis=0).reshape(-1),
            jnp.sum(grid_col[:, None, None] * d_theta, axis=0).reshape(-1),
        ]
    )
    d_query = rotate(d_qrot, cosine, -sine).reshape(row_count, width)
    d_key = rotate(d_krot, cosine, -sine).reshape(row_count, width)
    d_qkv = jnp.concatenate([d_query, d_key, d_value.reshape(row_count, width)], axis=1).astype(
        jnp.bfloat16
    )
    qkv_bias_grad = jnp.sum(d_qkv.astype(jnp.float32), axis=0)
    qkv_weight_grad = matmul_left_t(first_activation, d_qkv)
    first_activation_gradient = matmul_right_t(d_qkv, block_parameters[2])
    first_norm_gain_gradient = jnp.sum(
        first_activation_gradient * first_centered_normalized, axis=0
    )
    ln1_bias_grad = jnp.sum(first_activation_gradient, axis=0)
    tokens_grad = (
        residual_gradient
        + layer_norm_backward(
            first_activation_gradient,
            first_centered_normalized,
            first_inverse_deviation,
            block_parameters[0].astype(jnp.float32),
        )
    ).astype(jnp.bfloat16)
    late_packed, late_sizes = reduce_grads(
        (qkv_weight_grad, qkv_bias_grad, first_norm_gain_gradient, ln1_bias_grad, frequencies_grad)
    )
    late_owned = finish_grads(
        late_packed,
        late_sizes,
        (qkv_weight.shape, qkv_bias.shape, ln1_gain.shape, ln1_bias.shape, frequencies.shape),
    )
    (fc2_weight_g, fc1_weight_g, out_weight_g, fc2_bias_g, fc1_bias_g, out_bias_g, ln2_gain_g,
     ln2_bias_g) = early_owned
    qkv_weight_g, qkv_bias_g, ln1_gain_g, ln1_bias_g, frequencies_g = late_owned
    pieces = (
        ln1_gain_g,
        ln1_bias_g,
        qkv_weight_g,
        qkv_bias_g,
        out_weight_g,
        out_bias_g,
        ln2_gain_g,
        ln2_bias_g,
        fc1_weight_g,
        fc1_bias_g,
        fc2_weight_g,
        fc2_bias_g,
        frequencies_g,
    )
    freq_sq, other_sq = square_sums(pieces)
    freq_sq, other_sq = lax.psum((freq_sq, other_sq), "fsdp")
    return (
        block_out,
        tokens_grad,
        *pieces,
        jnp.sqrt(freq_sq),
        jnp.sqrt(other_sq),
    )


def solution(mesh):
    placed = (
        P(("fsdp", "dp"), None),
        P(("fsdp", "dp"), None),
        P("fsdp"),
        P("fsdp"),
        P("fsdp", None),
        P("fsdp"),
        P("fsdp", None),
        P("fsdp"),
        P("fsdp"),
        P("fsdp"),
        P("fsdp", None),
        P("fsdp"),
        P("fsdp", None),
        P("fsdp"),
        P("fsdp"),
        P(("fsdp", "dp"), None),
    )
    return jax.shard_map(
        shards,
        mesh=mesh,
        in_specs=placed,
        out_specs=(
            P(("fsdp", "dp"), None),
            P(("fsdp", "dp"), None),
            P("fsdp"),
            P("fsdp"),
            P("fsdp", None),
            P("fsdp"),
            P("fsdp", None),
            P("fsdp"),
            P("fsdp"),
            P("fsdp"),
            P("fsdp", None),
            P("fsdp"),
            P("fsdp", None),
            P("fsdp"),
            P("fsdp"),
            P(),
            P(),
        ),
        check_vma=False,
    )
```

```python
import jax
import jax.numpy as jnp
from jax import lax
from jax.experimental import pallas as pl
from jax.sharding import PartitionSpec as P


H = 12
HD = 64
BIN = 1024
Q_BLOCK = 256
PACK_ROWS = 16


norm_eps = 1e-06
masked_score = -1e30
inv_sqrt_two_pi = 0.3989422804014327


def matmul(left, right):
    return jnp.dot(left, right, preferred_element_type=jnp.float32)


def matmul_left_t(left, right):
    return lax.dot_general(
        left, right, (((0,), (0,)), ((), ())), preferred_element_type=jnp.float32
    )


def matmul_right_t(left, right):
    return lax.dot_general(
        left, right, (((1,), (1,)), ((), ())), preferred_element_type=jnp.float32
    )


def image_layout(image_table, bin_count, bin_rows):
    slot_count = image_table.shape[0] // bin_count
    table = image_table.reshape(bin_count, slot_count, 3)
    offset = table[:, :, 0:1]
    height = table[:, :, 1:2]
    width = table[:, :, 2:3]
    place = jnp.arange(bin_rows, dtype=jnp.int32)[None, None, :]
    inside = ((place >= offset) & (place < offset + height * width)).astype(jnp.int32)
    live = jnp.sum(inside, axis=1)
    slot_ids = jnp.arange(slot_count, dtype=jnp.int32)[None, :, None]
    segment = jnp.sum(inside * slot_ids, axis=1) + slot_count * (1 - live)
    local_place = place[:, 0, :] - jnp.sum(inside * offset, axis=1)
    grid_width = jnp.maximum(jnp.sum(inside * width, axis=1), 1)
    grid_row = local_place // grid_width * live
    grid_col = local_place % grid_width * live
    return (
        segment,
        grid_row.reshape(-1).astype(jnp.float32),
        grid_col.reshape(-1).astype(jnp.float32),
    )


def rotary_tables(frequencies, grid_row, grid_col):
    half_width = frequencies.shape[0] // 2
    freq_float = frequencies.astype(jnp.float32)
    freq_row = freq_float[:half_width].reshape(H, HD // 2)
    freq_col = freq_float[half_width:].reshape(H, HD // 2)
    theta = grid_row[:, None, None] * freq_row[None] + grid_col[:, None, None] * freq_col[None]
    return (jnp.cos(theta), jnp.sin(theta))


def rotate(heads, cosine, sine):
    half_width = heads.shape[-1] // 2
    first = heads[..., :half_width]
    second = heads[..., half_width:]
    return jnp.concatenate(
        [first * cosine - second * sine, first * sine + second * cosine], axis=-1
    )


def layer_norm_forward(values):
    center = values - jnp.mean(values, axis=-1, keepdims=True)
    inverse_deviation = lax.rsqrt(jnp.mean(center * center, axis=-1, keepdims=True) + norm_eps)
    return (center * inverse_deviation, inverse_deviation)


def layer_norm_backward(
    gradient_norm_total, centered_normalized, inverse_deviation, norm_gain_vector
):
    gain_scaled_output = gradient_norm_total * norm_gain_vector
    return inverse_deviation * (
        gain_scaled_output
        - jnp.mean(gain_scaled_output, axis=-1, keepdims=True)
        - centered_normalized
        * jnp.mean(gain_scaled_output * centered_normalized, axis=-1, keepdims=True)
    )


def gelu_slope(values):
    return (
        0.5 * (1.0 + lax.erf(values * 0.7071067811865476))
        + values * jnp.exp(-0.5 * values * values) * inv_sqrt_two_pi
    )


def _nt(a, b):
    return lax.dot_general(a, b, (((1,), (1,)), ((), ())), preferred_element_type=jnp.float32)


def _tn(a, b):
    return lax.dot_general(a, b, (((0,), (0,)), ((), ())), preferred_element_type=jnp.float32)


def _nn(a, b):
    return lax.dot_general(a, b, (((1,), (0,)), ((), ())), preferred_element_type=jnp.float32)


def attention_forward_kernel(q_ref, k_ref, v_ref, seg_r_ref, seg_c_ref, o_ref, lse_ref):
    rows = q_ref.shape[0]
    seg_c = seg_c_ref[...]
    scale = HD ** (-0.5)
    for half in range(q_ref.shape[1] // HD):
        cols = slice(half * HD, (half + 1) * HD)
        k_h = k_ref[:, cols]
        v_h = v_ref[:, cols]

        def block(i, carry):
            at = pl.multiple_of(i * Q_BLOCK, Q_BLOCK)
            q_h = q_ref[pl.ds(at, Q_BLOCK), cols]
            mask = seg_r_ref[pl.ds(at, Q_BLOCK), :] == seg_c
            scores = jnp.where(mask, _nt(q_h, k_h) * scale, masked_score)
            top = jnp.max(scores, axis=-1, keepdims=True)
            log_total = top + jnp.log(jnp.sum(jnp.exp(scores - top), axis=-1, keepdims=True))
            probs = jnp.exp(scores - log_total).astype(jnp.bfloat16)
            o_ref[pl.ds(at, Q_BLOCK), cols] = _nn(probs, v_h).astype(o_ref.dtype)
            lse_ref[pl.ds(at, Q_BLOCK), cols] = jnp.broadcast_to(log_total, (Q_BLOCK, HD))
            return carry

        lax.fori_loop(0, rows // Q_BLOCK, block, 0)


def attention_backward_kernel(q_ref, k_ref, v_ref, d_ref, lse_ref, seg_r_ref, seg_c_ref, dq_ref, dk_ref, dv_ref):
    rows = q_ref.shape[0]
    seg_c = seg_c_ref[...]
    scale = HD ** (-0.5)
    for half in range(q_ref.shape[1] // HD):
        cols = slice(half * HD, (half + 1) * HD)
        k_h = k_ref[:, cols]
        v_h = v_ref[:, cols]

        def block(i, carry):
            dk_acc, dv_acc = carry
            at = pl.multiple_of(i * Q_BLOCK, Q_BLOCK)
            q_h = q_ref[pl.ds(at, Q_BLOCK), cols]
            d_h = d_ref[pl.ds(at, Q_BLOCK), cols]
            log_total = lse_ref[pl.ds(at, Q_BLOCK), pl.ds(half * HD, 1)]
            mask = seg_r_ref[pl.ds(at, Q_BLOCK), :] == seg_c
            scores = jnp.where(mask, _nt(q_h, k_h) * scale, masked_score)
            probs = jnp.exp(scores - log_total)
            d_probs = _nt(d_h, v_h)
            dv_acc = dv_acc + _tn(probs.astype(jnp.bfloat16), d_h)
            inner = jnp.sum(probs * d_probs, axis=-1, keepdims=True)
            d_scores = (probs * (d_probs - inner)).astype(jnp.bfloat16)
            dq_ref[pl.ds(at, Q_BLOCK), cols] = _nn(d_scores, k_h) * scale
            dk_acc = dk_acc + _tn(d_scores, q_h)
            return dk_acc, dv_acc

        zero = jnp.zeros((rows, HD), jnp.float32)
        dk_acc, dv_acc = lax.fori_loop(0, rows // Q_BLOCK, block, (zero, zero))
        dk_ref[:, cols] = dk_acc * scale
        dv_ref[:, cols] = dv_acc


def attention_forward(q, k, v, segment):
    rows, width = q.shape
    pair = 2 * HD
    seg_r = segment.reshape(rows, 1)
    seg_c = segment.reshape(1, rows)
    spec = pl.BlockSpec((rows, pair), lambda j: (0, j))
    return pl.pallas_call(
        attention_forward_kernel,
        grid=(width // pair,),
        in_specs=[spec, spec, spec, pl.BlockSpec((rows, 1), lambda j: (0, 0)), pl.BlockSpec((1, rows), lambda j: (0, 0))],
        out_specs=[spec, spec],
        out_shape=[jax.ShapeDtypeStruct((rows, width), jnp.bfloat16), jax.ShapeDtypeStruct((rows, width), jnp.float32)],
        cost_estimate=pl.CostEstimate(
            flops=4 * rows * rows * width, transcendentals=2 * rows * rows * (width // HD),
            bytes_accessed=rows * width * (2 * 4 + 4)),
        name="attention_forward",
    )(q, k, v, seg_r, seg_c)


def attention_backward(q, k, v, d_mixed, log_total, segment):
    rows, width = q.shape
    pair = 2 * HD
    seg_r = segment.reshape(rows, 1)
    seg_c = segment.reshape(1, rows)
    spec = pl.BlockSpec((rows, pair), lambda j: (0, j))
    f32 = jax.ShapeDtypeStruct((rows, width), jnp.float32)
    return pl.pallas_call(
        attention_backward_kernel,
        grid=(width // pair,),
        in_specs=[spec, spec, spec, spec, spec, pl.BlockSpec((rows, 1), lambda j: (0, 0)), pl.BlockSpec((1, rows), lambda j: (0, 0))],
        out_specs=[spec, spec, spec],
        out_shape=[f32, f32, f32],
        cost_estimate=pl.CostEstimate(
            flops=8 * rows * rows * width, transcendentals=rows * rows * (width // HD),
            bytes_accessed=rows * width * (2 * 4 + 4 + 12)),
        name="attention_backward",
    )(q, k, v, d_mixed, log_total, seg_r, seg_c)


def attention_bins(q_low, k_low, v_low, segment):
    outs = [attention_forward(q_low[b * BIN:(b + 1) * BIN], k_low[b * BIN:(b + 1) * BIN],
                              v_low[b * BIN:(b + 1) * BIN], segment[b]) for b in range(segment.shape[0])]
    return tuple(jnp.concatenate(parts, axis=0) for parts in zip(*outs))


def attention_bins_back(q_low, k_low, v_low, d_mixed, log_total, segment):
    outs = [attention_backward(q_low[b * BIN:(b + 1) * BIN], k_low[b * BIN:(b + 1) * BIN],
                               v_low[b * BIN:(b + 1) * BIN], d_mixed[b * BIN:(b + 1) * BIN],
                               log_total[b * BIN:(b + 1) * BIN], segment[b]) for b in range(segment.shape[0])]
    return tuple(jnp.concatenate(parts, axis=0) for parts in zip(*outs))


def square_sums(pieces):
    freq_sq = jnp.sum(pieces[12] * pieces[12])
    other_sq = jnp.float32(0.0)
    for member in pieces[:12]:
        other_sq = other_sq + jnp.sum(member * member)
    return (freq_sq, other_sq)


def gather_weight(shard):
    pieces = lax.psum(1, "dp")
    part = shard.shape[0] // pieces
    mine = lax.dynamic_slice_in_dim(shard, lax.axis_index("dp") * part, part, 0)
    return lax.all_gather(mine, ("fsdp", "dp"), axis=0, tiled=True)


def gather_small(vectors):
    sizes = [v.shape[0] for v in vectors]
    packed = lax.all_gather(jnp.concatenate(vectors), "fsdp", axis=0, tiled=False)
    out, at = [], 0
    for n in sizes:
        out.append(packed[:, at : at + n].reshape(-1))
        at += n
    return out


def column_chunks(matrix, width):
    return [matrix[:, j * width : (j + 1) * width] for j in range(matrix.shape[1] // width)]


def pack_rows(matrices, vectors):
    blocks = lax.psum(1, ("fsdp", "dp"))
    width = matrices[0].shape[1]
    parts = [m.reshape(blocks, m.shape[0] // blocks, width).astype(jnp.bfloat16) for m in matrices]
    flat = jnp.concatenate([v.reshape(blocks, -1) for v in vectors], axis=1)
    small = flat.shape[1]
    small_rows = -(-small // width)
    flat = jnp.pad(flat, ((0, 0), (0, small_rows * width - small)))
    parts.append(flat.reshape(blocks, small_rows, width).astype(jnp.bfloat16))
    rows = [p.shape[1] for p in parts]
    total = sum(rows)
    padded = -(-total // PACK_ROWS) * PACK_ROWS
    if padded > total:
        parts.append(jnp.zeros((blocks, padded - total, width), jnp.bfloat16))
    layout = (rows, [v.shape[0] // blocks for v in vectors])
    return jnp.concatenate(parts, axis=1), layout


def unpack_rows(owned, layout):
    rows, vector_sizes = layout
    groups = owned.shape[0]
    out, at = [], 0
    for r in rows[:-1]:
        out.append(owned[:, at : at + r, :].reshape(groups * r, owned.shape[2]).astype(jnp.float32))
        at += r
    flat = owned[:, at : at + rows[-1], :].reshape(groups, -1)
    vectors, at = [], 0
    for n in vector_sizes:
        vectors.append(flat[:, at : at + n].reshape(-1).astype(jnp.float32))
        at += n
    return out, vectors


def sum_on_sparse_core(packed, layout):
    blocks, padded, width = packed.shape
    mine = lax.psum_scatter(
        packed.reshape(blocks * padded, width), ("fsdp", "dp"), scatter_dimension=0, tiled=True
    )
    owned = lax.all_gather(mine, "dp", axis=0, tiled=True)
    return unpack_rows(owned.reshape(-1, padded, width), layout)


def sum_by_exchange(packed, layout):
    _, padded, width = packed.shape
    received = lax.all_to_all(packed, ("fsdp", "dp"), 0, 0, tiled=False)
    mine = jnp.sum(received.astype(jnp.float32), axis=0)
    owned = lax.all_gather(mine, "dp", axis=0, tiled=True)
    return unpack_rows(owned.reshape(-1, padded, width), layout)


def shards(
    tokens,
    image_table,
    ln1_gain,
    ln1_bias,
    qkv_weight,
    qkv_bias,
    out_weight,
    out_bias,
    ln2_gain,
    ln2_bias,
    fc1_weight,
    fc1_bias,
    fc2_weight,
    fc2_bias,
    frequencies,
    cotangent,
):
    small_local = (ln1_gain, ln1_bias, qkv_bias, out_bias, ln2_gain, ln2_bias, fc1_bias, fc2_bias, frequencies)
    (g_ln1_gain, g_ln1_bias, g_qkv_bias, g_out_bias, g_ln2_gain, g_ln2_bias, g_fc1_bias, g_fc2_bias,
     g_frequencies) = gather_small(small_local)
    block_parameters = (
        g_ln1_gain,
        g_ln1_bias,
        gather_weight(qkv_weight),
        g_qkv_bias,
        gather_weight(out_weight),
        g_out_bias,
        g_ln2_gain,
        g_ln2_bias,
        gather_weight(fc1_weight),
        g_fc1_bias,
        gather_weight(fc2_weight),
        g_fc2_bias,
        g_frequencies,
    )
    row_count, width = tokens.shape
    bin_count = row_count // BIN
    half_head = HD // 2
    segment, grid_row, grid_col = image_layout(image_table, bin_count, BIN)
    cosine, sine = rotary_tables(block_parameters[12], grid_row, grid_col)
    input_single_precision = tokens.astype(jnp.float32)
    first_centered_normalized, first_inverse_deviation = layer_norm_forward(input_single_precision)
    first_activation = (
        first_centered_normalized * block_parameters[0].astype(jnp.float32)
        + block_parameters[1].astype(jnp.float32)
    ).astype(jnp.bfloat16)
    qkv_full = matmul(first_activation, block_parameters[2]) + block_parameters[3].astype(
        jnp.float32
    )
    q_rot = rotate(qkv_full[:, :width].reshape(row_count, H, HD), cosine, sine)
    k_rot = rotate(qkv_full[:, width : 2 * width].reshape(row_count, H, HD), cosine, sine)
    q_low = q_rot.reshape(row_count, width).astype(jnp.bfloat16)
    k_low = k_rot.reshape(row_count, width).astype(jnp.bfloat16)
    v_low = qkv_full[:, 2 * width :].astype(jnp.bfloat16)
    mixed, log_total = attention_bins(q_low, k_low, v_low, segment)
    residual_stream = (
        input_single_precision
        + matmul(mixed, block_parameters[4])
        + block_parameters[5].astype(jnp.float32)
    )
    second_centered_normalized, second_inverse_deviation = layer_norm_forward(residual_stream)
    second_activation = (
        second_centered_normalized * block_parameters[6].astype(jnp.float32)
        + block_parameters[7].astype(jnp.float32)
    ).astype(jnp.bfloat16)
    up_proj = matmul(second_activation, block_parameters[8]) + block_parameters[9].astype(
        jnp.float32
    )
    gelu_low = jax.nn.gelu(up_proj, approximate=False).astype(jnp.bfloat16)
    block_out = (
        residual_stream
        + matmul(gelu_low, block_parameters[10])
        + block_parameters[11].astype(jnp.float32)
    ).astype(jnp.bfloat16)
    output_gradient = cotangent.astype(jnp.float32)
    fc2_bias_grad = jnp.sum(output_gradient, axis=0)
    fc2_weight_grad = matmul_left_t(gelu_low, cotangent)
    d_up = (matmul_right_t(cotangent, block_parameters[10]) * gelu_slope(up_proj)).astype(
        jnp.bfloat16
    )
    fc1_bias_grad = jnp.sum(d_up.astype(jnp.float32), axis=0)
    fc1_weight_grad = matmul_left_t(second_activation, d_up)
    second_activation_gradient = matmul_right_t(d_up, block_parameters[8])
    second_norm_gain_gradient = jnp.sum(
        second_activation_gradient * second_centered_normalized, axis=0
    )
    ln2_bias_grad = jnp.sum(second_activation_gradient, axis=0)
    residual_gradient = output_gradient + layer_norm_backward(
        second_activation_gradient,
        second_centered_normalized,
        second_inverse_deviation,
        block_parameters[6].astype(jnp.float32),
    )
    d_att = residual_gradient.astype(jnp.bfloat16)
    out_bias_grad = jnp.sum(d_att.astype(jnp.float32), axis=0)
    out_weight_grad = matmul_left_t(mixed, d_att)
    d_mixed = matmul_right_t(d_att, block_parameters[4]).astype(jnp.bfloat16)
    width = out_weight_grad.shape[1]
    early_packed, early_layout = pack_rows(
        [fc2_weight_grad, *column_chunks(fc1_weight_grad, width), out_weight_grad],
        [fc2_bias_grad, fc1_bias_grad, out_bias_grad, second_norm_gain_gradient, ln2_bias_grad],
    )
    early_packed, d_mixed = lax.optimization_barrier((early_packed, d_mixed))
    early_mats, early_vecs = sum_on_sparse_core(early_packed, early_layout)
    d_qrot, d_krot, d_value = attention_bins_back(q_low, k_low, v_low, d_mixed, log_total, segment)
    d_qrot = d_qrot.reshape(row_count, H, HD)
    d_krot = d_krot.reshape(row_count, H, HD)
    d_theta = (
        d_qrot[..., half_head:] * q_rot[..., :half_head]
        - d_qrot[..., :half_head] * q_rot[..., half_head:]
    )
    d_theta = (
        d_theta
        + d_krot[..., half_head:] * k_rot[..., :half_head]
        - d_krot[..., :half_head] * k_rot[..., half_head:]
    )
    frequencies_grad = jnp.concatenate(
        [
            jnp.sum(grid_row[:, None, None] * d_theta, axis=0).reshape(-1),
            jnp.sum(grid_col[:, None, None] * d_theta, axis=0).reshape(-1),
        ]
    )
    d_query = rotate(d_qrot, cosine, -sine).reshape(row_count, width)
    d_key = rotate(d_krot, cosine, -sine).reshape(row_count, width)
    d_qkv = jnp.concatenate([d_query, d_key, d_value.reshape(row_count, width)], axis=1).astype(
        jnp.bfloat16
    )
    qkv_bias_grad = jnp.sum(d_qkv.astype(jnp.float32), axis=0)
    qkv_weight_grad = matmul_left_t(first_activation, d_qkv)
    first_activation_gradient = matmul_right_t(d_qkv, block_parameters[2])
    first_norm_gain_gradient = jnp.sum(
        first_activation_gradient * first_centered_normalized, axis=0
    )
    ln1_bias_grad = jnp.sum(first_activation_gradient, axis=0)
    tokens_grad = (
        residual_gradient
        + layer_norm_backward(
            first_activation_gradient,
            first_centered_normalized,
            first_inverse_deviation,
            block_parameters[0].astype(jnp.float32),
        )
    ).astype(jnp.bfloat16)
    late_packed, late_layout = pack_rows(
        column_chunks(qkv_weight_grad, width),
        [qkv_bias_grad, first_norm_gain_gradient, ln1_bias_grad, frequencies_grad],
    )
    late_mats, late_vecs = sum_by_exchange(late_packed, late_layout)
    fc2_weight_g = early_mats[0]
    fc1_weight_g = jnp.concatenate(early_mats[1:-1], axis=1)
    out_weight_g = early_mats[-1]
    fc2_bias_g, fc1_bias_g, out_bias_g, ln2_gain_g, ln2_bias_g = early_vecs
    qkv_weight_g = jnp.concatenate(late_mats, axis=1)
    qkv_bias_g, ln1_gain_g, ln1_bias_g, frequencies_g = late_vecs
    pieces = (
        ln1_gain_g,
        ln1_bias_g,
        qkv_weight_g,
        qkv_bias_g,
        out_weight_g,
        out_bias_g,
        ln2_gain_g,
        ln2_bias_g,
        fc1_weight_g,
        fc1_bias_g,
        fc2_weight_g,
        fc2_bias_g,
        frequencies_g,
    )
    freq_sq, other_sq = square_sums(pieces)
    freq_sq, other_sq = lax.psum((freq_sq, other_sq), "fsdp")
    return (
        block_out,
        tokens_grad,
        *pieces,
        jnp.sqrt(freq_sq),
        jnp.sqrt(other_sq),
    )


def solution(mesh):
    placed = (
        P(("fsdp", "dp"), None),
        P(("fsdp", "dp"), None),
        P("fsdp"),
        P("fsdp"),
        P("fsdp", None),
        P("fsdp"),
        P("fsdp", None),
        P("fsdp"),
        P("fsdp"),
        P("fsdp"),
        P("fsdp", None),
        P("fsdp"),
        P("fsdp", None),
        P("fsdp"),
        P("fsdp"),
        P(("fsdp", "dp"), None),
    )
    return jax.shard_map(
        shards,
        mesh=mesh,
        in_specs=placed,
        out_specs=(
            P(("fsdp", "dp"), None),
            P(("fsdp", "dp"), None),
            P("fsdp"),
            P("fsdp"),
            P("fsdp", None),
            P("fsdp"),
            P("fsdp", None),
            P("fsdp"),
            P("fsdp"),
            P("fsdp"),
            P("fsdp", None),
            P("fsdp"),
            P("fsdp", None),
            P("fsdp"),
            P("fsdp"),
            P(),
            P(),
        ),
        check_vma=False,
    )
```

```python
import jax
import jax.numpy as jnp
from jax import lax
from jax.experimental import pallas as pl
from jax.sharding import PartitionSpec as P


H = 12
HD = 64
BIN = 1024
Q_BLOCK = 256
PACK_ROWS = 16


norm_eps = 1e-06
masked_score = -1e30
inv_sqrt_two_pi = 0.3989422804014327


def matmul(left, right):
    return jnp.dot(left, right, preferred_element_type=jnp.float32)


def matmul_left_t(left, right):
    return lax.dot_general(
        left, right, (((0,), (0,)), ((), ())), preferred_element_type=jnp.float32
    )


def matmul_right_t(left, right):
    return lax.dot_general(
        left, right, (((1,), (1,)), ((), ())), preferred_element_type=jnp.float32
    )


def image_layout(image_table, bin_count, bin_rows):
    slot_count = image_table.shape[0] // bin_count
    table = image_table.reshape(bin_count, slot_count, 3)
    offset = table[:, :, 0:1]
    height = table[:, :, 1:2]
    width = table[:, :, 2:3]
    place = jnp.arange(bin_rows, dtype=jnp.int32)[None, None, :]
    inside = ((place >= offset) & (place < offset + height * width)).astype(jnp.int32)
    live = jnp.sum(inside, axis=1)
    slot_ids = jnp.arange(slot_count, dtype=jnp.int32)[None, :, None]
    segment = jnp.sum(inside * slot_ids, axis=1) + slot_count * (1 - live)
    local_place = place[:, 0, :] - jnp.sum(inside * offset, axis=1)
    grid_width = jnp.maximum(jnp.sum(inside * width, axis=1), 1)
    grid_row = local_place // grid_width * live
    grid_col = local_place % grid_width * live
    return (
        segment,
        grid_row.reshape(-1).astype(jnp.float32),
        grid_col.reshape(-1).astype(jnp.float32),
    )


def rotary_tables(frequencies, grid_row, grid_col):
    half_width = frequencies.shape[0] // 2
    freq_float = frequencies.astype(jnp.float32)
    freq_row = freq_float[:half_width].reshape(H, HD // 2)
    freq_col = freq_float[half_width:].reshape(H, HD // 2)
    theta = grid_row[:, None, None] * freq_row[None] + grid_col[:, None, None] * freq_col[None]
    return (jnp.cos(theta), jnp.sin(theta))


def rotate(heads, cosine, sine):
    half_width = heads.shape[-1] // 2
    first = heads[..., :half_width]
    second = heads[..., half_width:]
    return jnp.concatenate(
        [first * cosine - second * sine, first * sine + second * cosine], axis=-1
    )


def layer_norm_forward(values):
    center = values - jnp.mean(values, axis=-1, keepdims=True)
    inverse_deviation = lax.rsqrt(jnp.mean(center * center, axis=-1, keepdims=True) + norm_eps)
    return (center * inverse_deviation, inverse_deviation)


def layer_norm_backward(
    gradient_norm_total, centered_normalized, inverse_deviation, norm_gain_vector
):
    gain_scaled_output = gradient_norm_total * norm_gain_vector
    return inverse_deviation * (
        gain_scaled_output
        - jnp.mean(gain_scaled_output, axis=-1, keepdims=True)
        - centered_normalized
        * jnp.mean(gain_scaled_output * centered_normalized, axis=-1, keepdims=True)
    )


def gelu_slope(values):
    return (
        0.5 * (1.0 + lax.erf(values * 0.7071067811865476))
        + values * jnp.exp(-0.5 * values * values) * inv_sqrt_two_pi
    )


def _nt(a, b):
    return lax.dot_general(a, b, (((1,), (1,)), ((), ())), preferred_element_type=jnp.float32)


def _tn(a, b):
    return lax.dot_general(a, b, (((0,), (0,)), ((), ())), preferred_element_type=jnp.float32)


def _nn(a, b):
    return lax.dot_general(a, b, (((1,), (0,)), ((), ())), preferred_element_type=jnp.float32)


def attention_forward_kernel(q_ref, k_ref, v_ref, seg_r_ref, seg_c_ref, o_ref, lse_ref):
    rows = q_ref.shape[0]
    seg_c = seg_c_ref[...]
    scale = HD ** (-0.5)
    for half in range(q_ref.shape[1] // HD):
        cols = slice(half * HD, (half + 1) * HD)
        k_h = k_ref[:, cols]
        v_h = v_ref[:, cols]

        def block(i, carry):
            at = pl.multiple_of(i * Q_BLOCK, Q_BLOCK)
            q_h = q_ref[pl.ds(at, Q_BLOCK), cols]
            mask = seg_r_ref[pl.ds(at, Q_BLOCK), :] == seg_c
            scores = jnp.where(mask, _nt(q_h, k_h) * scale, masked_score)
            top = jnp.max(scores, axis=-1, keepdims=True)
            log_total = top + jnp.log(jnp.sum(jnp.exp(scores - top), axis=-1, keepdims=True))
            probs = jnp.exp(scores - log_total).astype(jnp.bfloat16)
            o_ref[pl.ds(at, Q_BLOCK), cols] = _nn(probs, v_h).astype(o_ref.dtype)
            lse_ref[pl.ds(at, Q_BLOCK), cols] = jnp.broadcast_to(log_total, (Q_BLOCK, HD))
            return carry

        lax.fori_loop(0, rows // Q_BLOCK, block, 0)


def attention_backward_kernel(q_ref, k_ref, v_ref, d_ref, lse_ref, seg_r_ref, seg_c_ref, dq_ref, dk_ref, dv_ref):
    rows = q_ref.shape[0]
    seg_c = seg_c_ref[...]
    scale = HD ** (-0.5)
    for half in range(q_ref.shape[1] // HD):
        cols = slice(half * HD, (half + 1) * HD)
        k_h = k_ref[:, cols]
        v_h = v_ref[:, cols]

        def block(i, carry):
            dk_acc, dv_acc = carry
            at = pl.multiple_of(i * Q_BLOCK, Q_BLOCK)
            q_h = q_ref[pl.ds(at, Q_BLOCK), cols]
            d_h = d_ref[pl.ds(at, Q_BLOCK), cols]
            log_total = lse_ref[pl.ds(at, Q_BLOCK), pl.ds(half * HD, 1)]
            mask = seg_r_ref[pl.ds(at, Q_BLOCK), :] == seg_c
            scores = jnp.where(mask, _nt(q_h, k_h) * scale, masked_score)
            probs = jnp.exp(scores - log_total)
            d_probs = _nt(d_h, v_h)
            dv_acc = dv_acc + _tn(probs.astype(jnp.bfloat16), d_h)
            inner = jnp.sum(probs * d_probs, axis=-1, keepdims=True)
            d_scores = (probs * (d_probs - inner)).astype(jnp.bfloat16)
            dq_ref[pl.ds(at, Q_BLOCK), cols] = _nn(d_scores, k_h) * scale
            dk_acc = dk_acc + _tn(d_scores, q_h)
            return dk_acc, dv_acc

        zero = jnp.zeros((rows, HD), jnp.float32)
        dk_acc, dv_acc = lax.fori_loop(0, rows // Q_BLOCK, block, (zero, zero))
        dk_ref[:, cols] = dk_acc * scale
        dv_ref[:, cols] = dv_acc


def attention_forward(q, k, v, segment):
    rows, width = q.shape
    pair = 2 * HD
    seg_r = segment.reshape(rows, 1)
    seg_c = segment.reshape(1, rows)
    spec = pl.BlockSpec((rows, pair), lambda j: (0, j))
    return pl.pallas_call(
        attention_forward_kernel,
        grid=(width // pair,),
        in_specs=[spec, spec, spec, pl.BlockSpec((rows, 1), lambda j: (0, 0)), pl.BlockSpec((1, rows), lambda j: (0, 0))],
        out_specs=[spec, spec],
        out_shape=[jax.ShapeDtypeStruct((rows, width), jnp.bfloat16), jax.ShapeDtypeStruct((rows, width), jnp.float32)],
        cost_estimate=pl.CostEstimate(
            flops=4 * rows * rows * width, transcendentals=2 * rows * rows * (width // HD),
            bytes_accessed=rows * width * (2 * 4 + 4)),
        name="attention_forward",
    )(q, k, v, seg_r, seg_c)


def attention_backward(q, k, v, d_mixed, log_total, segment):
    rows, width = q.shape
    pair = 2 * HD
    seg_r = segment.reshape(rows, 1)
    seg_c = segment.reshape(1, rows)
    spec = pl.BlockSpec((rows, pair), lambda j: (0, j))
    f32 = jax.ShapeDtypeStruct((rows, width), jnp.float32)
    return pl.pallas_call(
        attention_backward_kernel,
        grid=(width // pair,),
        in_specs=[spec, spec, spec, spec, spec, pl.BlockSpec((rows, 1), lambda j: (0, 0)), pl.BlockSpec((1, rows), lambda j: (0, 0))],
        out_specs=[spec, spec, spec],
        out_shape=[f32, f32, f32],
        cost_estimate=pl.CostEstimate(
            flops=8 * rows * rows * width, transcendentals=rows * rows * (width // HD),
            bytes_accessed=rows * width * (2 * 4 + 4 + 12)),
        name="attention_backward",
    )(q, k, v, d_mixed, log_total, seg_r, seg_c)


def attention_bins(q_low, k_low, v_low, segment):
    outs = [attention_forward(q_low[b * BIN:(b + 1) * BIN], k_low[b * BIN:(b + 1) * BIN],
                              v_low[b * BIN:(b + 1) * BIN], segment[b]) for b in range(segment.shape[0])]
    return tuple(jnp.concatenate(parts, axis=0) for parts in zip(*outs))


def attention_bins_back(q_low, k_low, v_low, d_mixed, log_total, segment):
    outs = [attention_backward(q_low[b * BIN:(b + 1) * BIN], k_low[b * BIN:(b + 1) * BIN],
                               v_low[b * BIN:(b + 1) * BIN], d_mixed[b * BIN:(b + 1) * BIN],
                               log_total[b * BIN:(b + 1) * BIN], segment[b]) for b in range(segment.shape[0])]
    return tuple(jnp.concatenate(parts, axis=0) for parts in zip(*outs))


def quarter(shard):
    part = shard.shape[0] // lax.psum(1, "dp")
    return lax.dynamic_slice_in_dim(shard, lax.axis_index("dp") * part, part, 0)


def gather_side_by_side(left, right):
    joined = jnp.concatenate([quarter(left), quarter(right)], axis=1)
    whole = lax.all_gather(joined, ("fsdp", "dp"), axis=0, tiled=True)
    return whole[:, : left.shape[1]], whole[:, left.shape[1] :]


def gather_stacked(top, bottom):
    upper = quarter(top)
    lower = quarter(bottom).reshape(-1, top.shape[1])
    whole = lax.all_gather(jnp.concatenate([upper, lower], axis=0)[None], ("fsdp", "dp"), axis=0, tiled=True)
    first = whole[:, : upper.shape[0]].reshape(-1, top.shape[1])
    second = whole[:, upper.shape[0] :].reshape(-1, bottom.shape[1])
    return first, second


def gather_small(vectors):
    sizes = [v.shape[0] for v in vectors]
    packed = lax.all_gather(jnp.concatenate(vectors), "fsdp", axis=0, tiled=False)
    out, at = [], 0
    for n in sizes:
        out.append(packed[:, at : at + n].reshape(-1))
        at += n
    return out


def column_chunks(matrix, width):
    return [matrix[:, j * width : (j + 1) * width] for j in range(matrix.shape[1] // width)]


def pack_rows(matrices, vectors):
    blocks = lax.psum(1, ("fsdp", "dp"))
    width = matrices[0].shape[1]
    parts = [m.reshape(blocks, m.shape[0] // blocks, width).astype(jnp.bfloat16) for m in matrices]
    flat = jnp.concatenate([v.reshape(blocks, -1) for v in vectors], axis=1)
    small = flat.shape[1]
    small_rows = -(-small // width)
    flat = jnp.pad(flat, ((0, 0), (0, small_rows * width - small)))
    parts.append(flat.reshape(blocks, small_rows, width).astype(jnp.bfloat16))
    rows = [p.shape[1] for p in parts]
    spans = [-(-r // PACK_ROWS) * PACK_ROWS if r >= PACK_ROWS else r for r in rows]
    spans[-1] += -sum(spans) % PACK_ROWS
    parts = [jnp.pad(p, ((0, 0), (0, s - r), (0, 0))) if s > r else p for p, r, s in zip(parts, rows, spans)]
    layout = (rows, spans, [v.shape[0] // blocks for v in vectors])
    return jnp.concatenate(parts, axis=1), layout


def unpack_rows(owned, layout):
    rows, spans, vector_sizes = layout
    groups = owned.shape[0]
    out, at = [], 0
    for r, s in zip(rows[:-1], spans[:-1]):
        out.append(owned[:, at : at + r, :].reshape(groups * r, owned.shape[2]).astype(jnp.float32))
        at += s
    flat = owned[:, at : at + rows[-1], :].reshape(groups, -1)
    vectors, at = [], 0
    for n in vector_sizes:
        vectors.append(flat[:, at : at + n].reshape(-1).astype(jnp.float32))
        at += n
    return out, vectors


def sum_on_sparse_core(packed, layout):
    blocks, padded, width = packed.shape
    mine = lax.psum_scatter(
        packed.reshape(blocks * padded, width), ("fsdp", "dp"), scatter_dimension=0, tiled=True
    )
    owned = lax.all_gather(mine, "dp", axis=0, tiled=True)
    return unpack_rows(owned.reshape(-1, padded, width), layout), mine


def sum_by_exchange(packed, layout):
    _, padded, width = packed.shape
    received = lax.all_to_all(packed, ("fsdp", "dp"), 0, 0, tiled=False)
    mine = jnp.sum(received.astype(jnp.float32), axis=0)
    owned = lax.all_gather(mine, "dp", axis=0, tiled=True)
    return unpack_rows(owned.reshape(-1, padded, width), layout), mine


def square_sums_of_block(mine, layout, last_vectors):
    rows, spans, vector_sizes = layout
    values = mine.astype(jnp.float32)
    small_at = sum(spans[:-1])
    flat = values[small_at : small_at + rows[-1]].reshape(-1)
    split = sum(vector_sizes[: len(vector_sizes) - last_vectors])
    end = sum(vector_sizes)
    last = jnp.sum(flat[split:end] * flat[split:end])
    rest = jnp.sum(values[:small_at] * values[:small_at]) + jnp.sum(flat[:split] * flat[:split])
    return last, rest


def shards(
    tokens,
    image_table,
    ln1_gain,
    ln1_bias,
    qkv_weight,
    qkv_bias,
    out_weight,
    out_bias,
    ln2_gain,
    ln2_bias,
    fc1_weight,
    fc1_bias,
    fc2_weight,
    fc2_bias,
    frequencies,
    cotangent,
):
    small_local = (ln1_gain, ln1_bias, qkv_bias, out_bias, ln2_gain, ln2_bias, fc1_bias, fc2_bias, frequencies)
    (g_ln1_gain, g_ln1_bias, g_qkv_bias, g_out_bias, g_ln2_gain, g_ln2_bias, g_fc1_bias, g_fc2_bias,
     g_frequencies) = gather_small(small_local)
    g_qkv_weight, g_out_weight = gather_side_by_side(qkv_weight, out_weight)
    g_fc1_weight, g_fc2_weight = gather_stacked(fc1_weight, fc2_weight)
    block_parameters = (
        g_ln1_gain,
        g_ln1_bias,
        g_qkv_weight,
        g_qkv_bias,
        g_out_weight,
        g_out_bias,
        g_ln2_gain,
        g_ln2_bias,
        g_fc1_weight,
        g_fc1_bias,
        g_fc2_weight,
        g_fc2_bias,
        g_frequencies,
    )
    row_count, width = tokens.shape
    bin_count = row_count // BIN
    half_head = HD // 2
    segment, grid_row, grid_col = image_layout(image_table, bin_count, BIN)
    cosine, sine = rotary_tables(block_parameters[12], grid_row, grid_col)
    input_single_precision = tokens.astype(jnp.float32)
    first_centered_normalized, first_inverse_deviation = layer_norm_forward(input_single_precision)
    first_activation = (
        first_centered_normalized * block_parameters[0].astype(jnp.float32)
        + block_parameters[1].astype(jnp.float32)
    ).astype(jnp.bfloat16)
    qkv_full = matmul(first_activation, block_parameters[2]) + block_parameters[3].astype(
        jnp.float32
    )
    q_rot = rotate(qkv_full[:, :width].reshape(row_count, H, HD), cosine, sine)
    k_rot = rotate(qkv_full[:, width : 2 * width].reshape(row_count, H, HD), cosine, sine)
    q_low = q_rot.reshape(row_count, width).astype(jnp.bfloat16)
    k_low = k_rot.reshape(row_count, width).astype(jnp.bfloat16)
    v_low = qkv_full[:, 2 * width :].astype(jnp.bfloat16)
    mixed, log_total = attention_bins(q_low, k_low, v_low, segment)
    residual_stream = (
        input_single_precision
        + matmul(mixed, block_parameters[4])
        + block_parameters[5].astype(jnp.float32)
    )
    second_centered_normalized, second_inverse_deviation = layer_norm_forward(residual_stream)
    second_activation = (
        second_centered_normalized * block_parameters[6].astype(jnp.float32)
        + block_parameters[7].astype(jnp.float32)
    ).astype(jnp.bfloat16)
    up_proj = matmul(second_activation, block_parameters[8]) + block_parameters[9].astype(
        jnp.float32
    )
    gelu_low = jax.nn.gelu(up_proj, approximate=False).astype(jnp.bfloat16)
    block_out = (
        residual_stream
        + matmul(gelu_low, block_parameters[10])
        + block_parameters[11].astype(jnp.float32)
    ).astype(jnp.bfloat16)
    output_gradient = cotangent.astype(jnp.float32)
    fc2_bias_grad = jnp.sum(output_gradient, axis=0)
    fc2_weight_grad = matmul_left_t(gelu_low, cotangent)
    d_up = (matmul_right_t(cotangent, block_parameters[10]) * gelu_slope(up_proj)).astype(
        jnp.bfloat16
    )
    fc1_bias_grad = jnp.sum(d_up.astype(jnp.float32), axis=0)
    fc1_weight_grad = matmul_left_t(second_activation, d_up)
    second_activation_gradient = matmul_right_t(d_up, block_parameters[8])
    second_norm_gain_gradient = jnp.sum(
        second_activation_gradient * second_centered_normalized, axis=0
    )
    ln2_bias_grad = jnp.sum(second_activation_gradient, axis=0)
    residual_gradient = output_gradient + layer_norm_backward(
        second_activation_gradient,
        second_centered_normalized,
        second_inverse_deviation,
        block_parameters[6].astype(jnp.float32),
    )
    d_att = residual_gradient.astype(jnp.bfloat16)
    out_bias_grad = jnp.sum(d_att.astype(jnp.float32), axis=0)
    out_weight_grad = matmul_left_t(mixed, d_att)
    d_mixed = matmul_right_t(d_att, block_parameters[4]).astype(jnp.bfloat16)
    width = out_weight_grad.shape[1]
    early_packed, early_layout = pack_rows(
        [fc2_weight_grad, *column_chunks(fc1_weight_grad, width), out_weight_grad],
        [fc2_bias_grad, fc1_bias_grad, out_bias_grad, second_norm_gain_gradient, ln2_bias_grad],
    )
    early_packed, d_mixed = lax.optimization_barrier((early_packed, d_mixed))
    (early_mats, early_vecs), early_mine = sum_on_sparse_core(early_packed, early_layout)
    d_qrot, d_krot, d_value = attention_bins_back(q_low, k_low, v_low, d_mixed, log_total, segment)
    d_qrot = d_qrot.reshape(row_count, H, HD)
    d_krot = d_krot.reshape(row_count, H, HD)
    d_theta = (
        d_qrot[..., half_head:] * q_rot[..., :half_head]
        - d_qrot[..., :half_head] * q_rot[..., half_head:]
    )
    d_theta = (
        d_theta
        + d_krot[..., half_head:] * k_rot[..., :half_head]
        - d_krot[..., :half_head] * k_rot[..., half_head:]
    )
    frequencies_grad = jnp.concatenate(
        [
            jnp.sum(grid_row[:, None, None] * d_theta, axis=0).reshape(-1),
            jnp.sum(grid_col[:, None, None] * d_theta, axis=0).reshape(-1),
        ]
    )
    d_query = rotate(d_qrot, cosine, -sine).reshape(row_count, width)
    d_key = rotate(d_krot, cosine, -sine).reshape(row_count, width)
    d_qkv = jnp.concatenate([d_query, d_key, d_value.reshape(row_count, width)], axis=1).astype(
        jnp.bfloat16
    )
    qkv_bias_grad = jnp.sum(d_qkv.astype(jnp.float32), axis=0)
    qkv_weight_grad = matmul_left_t(first_activation, d_qkv)
    first_activation_gradient = matmul_right_t(d_qkv, block_parameters[2])
    first_norm_gain_gradient = jnp.sum(
        first_activation_gradient * first_centered_normalized, axis=0
    )
    ln1_bias_grad = jnp.sum(first_activation_gradient, axis=0)
    tokens_grad = (
        residual_gradient
        + layer_norm_backward(
            first_activation_gradient,
            first_centered_normalized,
            first_inverse_deviation,
            block_parameters[0].astype(jnp.float32),
        )
    ).astype(jnp.bfloat16)
    late_packed, late_layout = pack_rows(
        column_chunks(qkv_weight_grad, width),
        [qkv_bias_grad, first_norm_gain_gradient, ln1_bias_grad, frequencies_grad],
    )
    (late_mats, late_vecs), late_mine = sum_by_exchange(late_packed, late_layout)
    _, early_sq = square_sums_of_block(early_mine, early_layout, 0)
    freq_sq, late_sq = square_sums_of_block(late_mine, late_layout, 1)
    freq_sq, other_sq = lax.psum((freq_sq, early_sq + late_sq), ("fsdp", "dp"))
    fc2_weight_g = early_mats[0]
    fc1_weight_g = jnp.concatenate(early_mats[1:-1], axis=1)
    out_weight_g = early_mats[-1]
    fc2_bias_g, fc1_bias_g, out_bias_g, ln2_gain_g, ln2_bias_g = early_vecs
    qkv_weight_g = jnp.concatenate(late_mats, axis=1)
    qkv_bias_g, ln1_gain_g, ln1_bias_g, frequencies_g = late_vecs
    pieces = (
        ln1_gain_g,
        ln1_bias_g,
        qkv_weight_g,
        qkv_bias_g,
        out_weight_g,
        out_bias_g,
        ln2_gain_g,
        ln2_bias_g,
        fc1_weight_g,
        fc1_bias_g,
        fc2_weight_g,
        fc2_bias_g,
        frequencies_g,
    )
    return (
        block_out,
        tokens_grad,
        *pieces,
        jnp.sqrt(freq_sq),
        jnp.sqrt(other_sq),
    )


def solution(mesh):
    placed = (
        P(("fsdp", "dp"), None),
        P(("fsdp", "dp"), None),
        P("fsdp"),
        P("fsdp"),
        P("fsdp", None),
        P("fsdp"),
        P("fsdp", None),
        P("fsdp"),
        P("fsdp"),
        P("fsdp"),
        P("fsdp", None),
        P("fsdp"),
        P("fsdp", None),
        P("fsdp"),
        P("fsdp"),
        P(("fsdp", "dp"), None),
    )
    return jax.shard_map(
        shards,
        mesh=mesh,
        in_specs=placed,
        out_specs=(
            P(("fsdp", "dp"), None),
            P(("fsdp", "dp"), None),
            P("fsdp"),
            P("fsdp"),
            P("fsdp", None),
            P("fsdp"),
            P("fsdp", None),
            P("fsdp"),
            P("fsdp"),
            P("fsdp"),
            P("fsdp", None),
            P("fsdp"),
            P("fsdp", None),
            P("fsdp"),
            P("fsdp"),
            P(),
            P(),
        ),
        check_vma=False,
    )
```

```python
import jax
import jax.numpy as jnp
from jax import lax
from jax.experimental import pallas as pl
from jax.sharding import PartitionSpec as P


H = 12
HD = 64
BIN = 1024
Q_BLOCK = 256


norm_eps = 1e-06
masked_score = -1e30
inv_sqrt_two_pi = 0.3989422804014327


def matmul(left, right):
    return jnp.dot(left, right, preferred_element_type=jnp.float32)


def matmul_left_t(left, right):
    return lax.dot_general(
        left, right, (((0,), (0,)), ((), ())), preferred_element_type=jnp.float32
    )


def matmul_right_t(left, right):
    return lax.dot_general(
        left, right, (((1,), (1,)), ((), ())), preferred_element_type=jnp.float32
    )


def image_layout(image_table, bin_count, bin_rows):
    slot_count = image_table.shape[0] // bin_count
    table = image_table.reshape(bin_count, slot_count, 3)
    offset = table[:, :, 0:1]
    height = table[:, :, 1:2]
    width = table[:, :, 2:3]
    place = jnp.arange(bin_rows, dtype=jnp.int32)[None, None, :]
    inside = ((place >= offset) & (place < offset + height * width)).astype(jnp.int32)
    live = jnp.sum(inside, axis=1)
    slot_ids = jnp.arange(slot_count, dtype=jnp.int32)[None, :, None]
    segment = jnp.sum(inside * slot_ids, axis=1) + slot_count * (1 - live)
    local_place = place[:, 0, :] - jnp.sum(inside * offset, axis=1)
    grid_width = jnp.maximum(jnp.sum(inside * width, axis=1), 1)
    grid_row = local_place // grid_width * live
    grid_col = local_place % grid_width * live
    return (
        segment,
        grid_row.reshape(-1).astype(jnp.float32),
        grid_col.reshape(-1).astype(jnp.float32),
    )


def rotary_tables(frequencies, grid_row, grid_col):
    half_width = frequencies.shape[0] // 2
    freq_float = frequencies.astype(jnp.float32)
    freq_row = freq_float[:half_width].reshape(H, HD // 2)
    freq_col = freq_float[half_width:].reshape(H, HD // 2)
    theta = grid_row[:, None, None] * freq_row[None] + grid_col[:, None, None] * freq_col[None]
    return (jnp.cos(theta), jnp.sin(theta))


def rotate(heads, cosine, sine):
    half_width = heads.shape[-1] // 2
    first = heads[..., :half_width]
    second = heads[..., half_width:]
    return jnp.concatenate(
        [first * cosine - second * sine, first * sine + second * cosine], axis=-1
    )


def layer_norm_forward(values):
    center = values - jnp.mean(values, axis=-1, keepdims=True)
    inverse_deviation = lax.rsqrt(jnp.mean(center * center, axis=-1, keepdims=True) + norm_eps)
    return (center * inverse_deviation, inverse_deviation)


def layer_norm_backward(
    gradient_norm_total, centered_normalized, inverse_deviation, norm_gain_vector
):
    gain_scaled_output = gradient_norm_total * norm_gain_vector
    return inverse_deviation * (
        gain_scaled_output
        - jnp.mean(gain_scaled_output, axis=-1, keepdims=True)
        - centered_normalized
        * jnp.mean(gain_scaled_output * centered_normalized, axis=-1, keepdims=True)
    )


def gelu_slope(values):
    return (
        0.5 * (1.0 + lax.erf(values * 0.7071067811865476))
        + values * jnp.exp(-0.5 * values * values) * inv_sqrt_two_pi
    )


def _nt(a, b):
    return lax.dot_general(a, b, (((1,), (1,)), ((), ())), preferred_element_type=jnp.float32)


def _tn(a, b):
    return lax.dot_general(a, b, (((0,), (0,)), ((), ())), preferred_element_type=jnp.float32)


def _nn(a, b):
    return lax.dot_general(a, b, (((1,), (0,)), ((), ())), preferred_element_type=jnp.float32)


def attention_forward_kernel(q_ref, k_ref, v_ref, seg_r_ref, seg_c_ref, o_ref, lse_ref):
    rows = q_ref.shape[0]
    seg_c = seg_c_ref[...]
    scale = HD ** (-0.5)
    for half in range(q_ref.shape[1] // HD):
        cols = slice(half * HD, (half + 1) * HD)
        k_h = k_ref[:, cols]
        v_h = v_ref[:, cols]

        def block(i, carry):
            at = pl.multiple_of(i * Q_BLOCK, Q_BLOCK)
            q_h = q_ref[pl.ds(at, Q_BLOCK), cols]
            mask = seg_r_ref[pl.ds(at, Q_BLOCK), :] == seg_c
            scores = jnp.where(mask, _nt(q_h, k_h) * scale, masked_score)
            top = jnp.max(scores, axis=-1, keepdims=True)
            log_total = top + jnp.log(jnp.sum(jnp.exp(scores - top), axis=-1, keepdims=True))
            probs = jnp.exp(scores - log_total).astype(jnp.bfloat16)
            o_ref[pl.ds(at, Q_BLOCK), cols] = _nn(probs, v_h).astype(o_ref.dtype)
            lse_ref[pl.ds(at, Q_BLOCK), cols] = jnp.broadcast_to(log_total, (Q_BLOCK, HD))
            return carry

        lax.fori_loop(0, rows // Q_BLOCK, block, 0)


def attention_backward_kernel(q_ref, k_ref, v_ref, d_ref, lse_ref, seg_r_ref, seg_c_ref, dq_ref, dk_ref, dv_ref):
    rows = q_ref.shape[0]
    seg_c = seg_c_ref[...]
    scale = HD ** (-0.5)
    for half in range(q_ref.shape[1] // HD):
        cols = slice(half * HD, (half + 1) * HD)
        k_h = k_ref[:, cols]
        v_h = v_ref[:, cols]

        def block(i, carry):
            dk_acc, dv_acc = carry
            at = pl.multiple_of(i * Q_BLOCK, Q_BLOCK)
            q_h = q_ref[pl.ds(at, Q_BLOCK), cols]
            d_h = d_ref[pl.ds(at, Q_BLOCK), cols]
            log_total = lse_ref[pl.ds(at, Q_BLOCK), pl.ds(half * HD, 1)]
            mask = seg_r_ref[pl.ds(at, Q_BLOCK), :] == seg_c
            scores = jnp.where(mask, _nt(q_h, k_h) * scale, masked_score)
            probs = jnp.exp(scores - log_total)
            d_probs = _nt(d_h, v_h)
            dv_acc = dv_acc + _tn(probs.astype(jnp.bfloat16), d_h)
            inner = jnp.sum(probs * d_probs, axis=-1, keepdims=True)
            d_scores = (probs * (d_probs - inner)).astype(jnp.bfloat16)
            dq_ref[pl.ds(at, Q_BLOCK), cols] = _nn(d_scores, k_h) * scale
            dk_acc = dk_acc + _tn(d_scores, q_h)
            return dk_acc, dv_acc

        zero = jnp.zeros((rows, HD), jnp.float32)
        dk_acc, dv_acc = lax.fori_loop(0, rows // Q_BLOCK, block, (zero, zero))
        dk_ref[:, cols] = dk_acc * scale
        dv_ref[:, cols] = dv_acc


def attention_forward(q, k, v, segment):
    rows, width = q.shape
    pair = 2 * HD
    seg_r = segment.reshape(rows, 1)
    seg_c = segment.reshape(1, rows)
    spec = pl.BlockSpec((rows, pair), lambda j: (0, j))
    return pl.pallas_call(
        attention_forward_kernel,
        grid=(width // pair,),
        in_specs=[spec, spec, spec, pl.BlockSpec((rows, 1), lambda j: (0, 0)), pl.BlockSpec((1, rows), lambda j: (0, 0))],
        out_specs=[spec, spec],
        out_shape=[jax.ShapeDtypeStruct((rows, width), jnp.bfloat16), jax.ShapeDtypeStruct((rows, width), jnp.float32)],
        cost_estimate=pl.CostEstimate(
            flops=4 * rows * rows * width, transcendentals=2 * rows * rows * (width // HD),
            bytes_accessed=rows * width * (2 * 4 + 4)),
        name="attention_forward",
    )(q, k, v, seg_r, seg_c)


def attention_backward(q, k, v, d_mixed, log_total, segment):
    rows, width = q.shape
    pair = 2 * HD
    seg_r = segment.reshape(rows, 1)
    seg_c = segment.reshape(1, rows)
    spec = pl.BlockSpec((rows, pair), lambda j: (0, j))
    f32 = jax.ShapeDtypeStruct((rows, width), jnp.float32)
    return pl.pallas_call(
        attention_backward_kernel,
        grid=(width // pair,),
        in_specs=[spec, spec, spec, spec, spec, pl.BlockSpec((rows, 1), lambda j: (0, 0)), pl.BlockSpec((1, rows), lambda j: (0, 0))],
        out_specs=[spec, spec, spec],
        out_shape=[f32, f32, f32],
        cost_estimate=pl.CostEstimate(
            flops=8 * rows * rows * width, transcendentals=rows * rows * (width // HD),
            bytes_accessed=rows * width * (2 * 4 + 4 + 12)),
        name="attention_backward",
    )(q, k, v, d_mixed, log_total, seg_r, seg_c)


def attention_bins(q_low, k_low, v_low, segment):
    outs = [attention_forward(q_low[b * BIN:(b + 1) * BIN], k_low[b * BIN:(b + 1) * BIN],
                              v_low[b * BIN:(b + 1) * BIN], segment[b]) for b in range(segment.shape[0])]
    return tuple(jnp.concatenate(parts, axis=0) for parts in zip(*outs))


def attention_bins_back(q_low, k_low, v_low, d_mixed, log_total, segment):
    outs = [attention_backward(q_low[b * BIN:(b + 1) * BIN], k_low[b * BIN:(b + 1) * BIN],
                               v_low[b * BIN:(b + 1) * BIN], d_mixed[b * BIN:(b + 1) * BIN],
                               log_total[b * BIN:(b + 1) * BIN], segment[b]) for b in range(segment.shape[0])]
    return tuple(jnp.concatenate(parts, axis=0) for parts in zip(*outs))


def quarter(shard):
    part = shard.shape[0] // lax.psum(1, "dp")
    return lax.dynamic_slice_in_dim(shard, lax.axis_index("dp") * part, part, 0)


def gather_side_by_side(left, right):
    joined = jnp.concatenate([quarter(left), quarter(right)], axis=1)
    whole = lax.all_gather(joined, ("fsdp", "dp"), axis=0, tiled=True)
    return whole[:, : left.shape[1]], whole[:, left.shape[1] :]


def gather_stacked(top, bottom):
    upper = quarter(top)
    lower = quarter(bottom).reshape(-1, top.shape[1])
    whole = lax.all_gather(jnp.concatenate([upper, lower], axis=0)[None], ("fsdp", "dp"), axis=0, tiled=True)
    first = whole[:, : upper.shape[0]].reshape(-1, top.shape[1])
    second = whole[:, upper.shape[0] :].reshape(-1, bottom.shape[1])
    return first, second


def gather_small(vectors):
    sizes = [v.shape[0] for v in vectors]
    packed = lax.all_gather(jnp.concatenate(vectors), "fsdp", axis=0, tiled=False)
    out, at = [], 0
    for n in sizes:
        out.append(packed[:, at : at + n].reshape(-1))
        at += n
    return out


def pack_columns(matrices, vectors):
    blocks = lax.psum(1, ("fsdp", "dp"))
    rows = matrices[0].shape[0]
    per_block = rows // blocks
    flat = jnp.concatenate([v.reshape(blocks, -1) for v in vectors], axis=1)
    small = flat.shape[1]
    small_cols = -(-small // per_block)
    flat = jnp.pad(flat, ((0, 0), (0, small_cols * per_block - small)))
    flat = flat.reshape(rows, small_cols)
    padded_cols = -(-small_cols // 128) * 128
    flat = jnp.pad(flat, ((0, 0), (0, padded_cols - small_cols)))
    parts = [m.astype(jnp.bfloat16) for m in matrices] + [flat.astype(jnp.bfloat16)]
    layout = ([m.shape[1] for m in matrices], small_cols, padded_cols, [v.shape[0] // blocks for v in vectors])
    return jnp.concatenate(parts, axis=1), layout


def unpack_columns(owned, layout):
    widths, small_cols, _, vector_sizes = layout
    groups = lax.psum(1, "dp")
    out, at = [], 0
    for w in widths:
        out.append(owned[:, at : at + w].astype(jnp.float32))
        at += w
    flat = owned[:, at : at + small_cols].reshape(groups, -1)
    vectors, at = [], 0
    for n in vector_sizes:
        vectors.append(flat[:, at : at + n].reshape(-1).astype(jnp.float32))
        at += n
    return out, vectors


def square_sums_of_block(mine, layout, last_vectors):
    widths, small_cols, _, vector_sizes = layout
    values = mine.astype(jnp.float32)
    at = sum(widths)
    flat = values[:, at : at + small_cols].reshape(-1)
    split = sum(vector_sizes[: len(vector_sizes) - last_vectors])
    end = sum(vector_sizes)
    last = jnp.sum(flat[split:end] * flat[split:end])
    rest = jnp.sum(values[:, :at] * values[:, :at]) + jnp.sum(flat[:split] * flat[:split])
    return last, rest


def sum_on_sparse_core(packed, layout):
    mine = lax.psum_scatter(packed, ("fsdp", "dp"), scatter_dimension=0, tiled=True)
    owned = lax.all_gather(mine, "dp", axis=0, tiled=True)
    return unpack_columns(owned, layout), mine


def sum_by_exchange(packed, layout, carried):
    blocks = lax.psum(1, ("fsdp", "dp"))
    received = lax.all_to_all(packed, ("fsdp", "dp"), 0, 0, tiled=True)
    mine = jnp.sum(received.reshape(blocks, -1, packed.shape[1]).astype(jnp.float32), axis=0)
    freq_part, rest_part = square_sums_of_block(mine, layout, 1)
    rest_part = rest_part + carried
    extra = jnp.zeros((mine.shape[0], 128), jnp.float32).at[0, 0].set(freq_part).at[0, 1].set(rest_part)
    owned = lax.all_gather(jnp.concatenate([mine, extra], axis=1), "dp", axis=0, tiled=True)
    partials = jnp.sum(owned[:: mine.shape[0], packed.shape[1] : packed.shape[1] + 2], axis=0)
    return unpack_columns(owned[:, : packed.shape[1]], layout), partials


def shards(
    tokens,
    image_table,
    ln1_gain,
    ln1_bias,
    qkv_weight,
    qkv_bias,
    out_weight,
    out_bias,
    ln2_gain,
    ln2_bias,
    fc1_weight,
    fc1_bias,
    fc2_weight,
    fc2_bias,
    frequencies,
    cotangent,
):
    small_local = (ln1_gain, ln1_bias, qkv_bias, out_bias, ln2_gain, ln2_bias, fc1_bias, fc2_bias, frequencies)
    (g_ln1_gain, g_ln1_bias, g_qkv_bias, g_out_bias, g_ln2_gain, g_ln2_bias, g_fc1_bias, g_fc2_bias,
     g_frequencies) = gather_small(small_local)
    g_qkv_weight, g_out_weight = gather_side_by_side(qkv_weight, out_weight)
    g_fc1_weight, g_fc2_weight = gather_stacked(fc1_weight, fc2_weight)
    block_parameters = (
        g_ln1_gain,
        g_ln1_bias,
        g_qkv_weight,
        g_qkv_bias,
        g_out_weight,
        g_out_bias,
        g_ln2_gain,
        g_ln2_bias,
        g_fc1_weight,
        g_fc1_bias,
        g_fc2_weight,
        g_fc2_bias,
        g_frequencies,
    )
    row_count, width = tokens.shape
    bin_count = row_count // BIN
    half_head = HD // 2
    segment, grid_row, grid_col = image_layout(image_table, bin_count, BIN)
    cosine, sine = rotary_tables(block_parameters[12], grid_row, grid_col)
    input_single_precision = tokens.astype(jnp.float32)
    first_centered_normalized, first_inverse_deviation = layer_norm_forward(input_single_precision)
    first_activation = (
        first_centered_normalized * block_parameters[0].astype(jnp.float32)
        + block_parameters[1].astype(jnp.float32)
    ).astype(jnp.bfloat16)
    qkv_full = matmul(first_activation, block_parameters[2]) + block_parameters[3].astype(
        jnp.float32
    )
    q_rot = rotate(qkv_full[:, :width].reshape(row_count, H, HD), cosine, sine)
    k_rot = rotate(qkv_full[:, width : 2 * width].reshape(row_count, H, HD), cosine, sine)
    q_low = q_rot.reshape(row_count, width).astype(jnp.bfloat16)
    k_low = k_rot.reshape(row_count, width).astype(jnp.bfloat16)
    v_low = qkv_full[:, 2 * width :].astype(jnp.bfloat16)
    mixed, log_total = attention_bins(q_low, k_low, v_low, segment)
    residual_stream = (
        input_single_precision
        + matmul(mixed, block_parameters[4])
        + block_parameters[5].astype(jnp.float32)
    )
    second_centered_normalized, second_inverse_deviation = layer_norm_forward(residual_stream)
    second_activation = (
        second_centered_normalized * block_parameters[6].astype(jnp.float32)
        + block_parameters[7].astype(jnp.float32)
    ).astype(jnp.bfloat16)
    up_proj = matmul(second_activation, block_parameters[8]) + block_parameters[9].astype(
        jnp.float32
    )
    gelu_low = jax.nn.gelu(up_proj, approximate=False).astype(jnp.bfloat16)
    block_out = (
        residual_stream
        + matmul(gelu_low, block_parameters[10])
        + block_parameters[11].astype(jnp.float32)
    ).astype(jnp.bfloat16)
    output_gradient = cotangent.astype(jnp.float32)
    fc2_bias_grad = jnp.sum(output_gradient, axis=0)
    fc2_weight_grad = matmul_left_t(gelu_low, cotangent)
    d_up = (matmul_right_t(cotangent, block_parameters[10]) * gelu_slope(up_proj)).astype(
        jnp.bfloat16
    )
    fc1_bias_grad = jnp.sum(d_up.astype(jnp.float32), axis=0)
    fc1_weight_grad = matmul_left_t(second_activation, d_up)
    second_activation_gradient = matmul_right_t(d_up, block_parameters[8])
    second_norm_gain_gradient = jnp.sum(
        second_activation_gradient * second_centered_normalized, axis=0
    )
    ln2_bias_grad = jnp.sum(second_activation_gradient, axis=0)
    residual_gradient = output_gradient + layer_norm_backward(
        second_activation_gradient,
        second_centered_normalized,
        second_inverse_deviation,
        block_parameters[6].astype(jnp.float32),
    )
    d_att = residual_gradient.astype(jnp.bfloat16)
    out_bias_grad = jnp.sum(d_att.astype(jnp.float32), axis=0)
    out_weight_grad = matmul_left_t(mixed, d_att)
    d_mixed = matmul_right_t(d_att, block_parameters[4]).astype(jnp.bfloat16)
    early_packed, early_layout = pack_columns(
        [fc2_weight_grad.reshape(fc1_weight_grad.shape[0], -1), fc1_weight_grad, out_weight_grad],
        [fc2_bias_grad, fc1_bias_grad, out_bias_grad, second_norm_gain_gradient, ln2_bias_grad],
    )
    early_packed, d_mixed = lax.optimization_barrier((early_packed, d_mixed))
    (early_mats, early_vecs), early_mine = sum_on_sparse_core(early_packed, early_layout)
    d_qrot, d_krot, d_value = attention_bins_back(q_low, k_low, v_low, d_mixed, log_total, segment)
    d_qrot = d_qrot.reshape(row_count, H, HD)
    d_krot = d_krot.reshape(row_count, H, HD)
    d_theta = (
        d_qrot[..., half_head:] * q_rot[..., :half_head]
        - d_qrot[..., :half_head] * q_rot[..., half_head:]
    )
    d_theta = (
        d_theta
        + d_krot[..., half_head:] * k_rot[..., :half_head]
        - d_krot[..., :half_head] * k_rot[..., half_head:]
    )
    frequencies_grad = jnp.concatenate(
        [
            jnp.sum(grid_row[:, None, None] * d_theta, axis=0).reshape(-1),
            jnp.sum(grid_col[:, None, None] * d_theta, axis=0).reshape(-1),
        ]
    )
    d_query = rotate(d_qrot, cosine, -sine).reshape(row_count, width)
    d_key = rotate(d_krot, cosine, -sine).reshape(row_count, width)
    d_qkv = jnp.concatenate([d_query, d_key, d_value.reshape(row_count, width)], axis=1).astype(
        jnp.bfloat16
    )
    qkv_bias_grad = jnp.sum(d_qkv.astype(jnp.float32), axis=0)
    qkv_weight_grad = matmul_left_t(first_activation, d_qkv)
    first_activation_gradient = matmul_right_t(d_qkv, block_parameters[2])
    first_norm_gain_gradient = jnp.sum(
        first_activation_gradient * first_centered_normalized, axis=0
    )
    ln1_bias_grad = jnp.sum(first_activation_gradient, axis=0)
    tokens_grad = (
        residual_gradient
        + layer_norm_backward(
            first_activation_gradient,
            first_centered_normalized,
            first_inverse_deviation,
            block_parameters[0].astype(jnp.float32),
        )
    ).astype(jnp.bfloat16)
    late_packed, late_layout = pack_columns(
        [qkv_weight_grad],
        [qkv_bias_grad, first_norm_gain_gradient, ln1_bias_grad, frequencies_grad],
    )
    late_packed, tokens_grad = lax.optimization_barrier((late_packed, tokens_grad))
    _, early_sq = square_sums_of_block(early_mine, early_layout, 0)
    (late_mats, late_vecs), partials = sum_by_exchange(late_packed, late_layout, early_sq)
    freq_sq, other_sq = lax.psum((partials[0], partials[1]), "fsdp")
    fc2_weight_g = early_mats[0].reshape(fc2_weight.shape)
    fc1_weight_g = early_mats[1]
    out_weight_g = early_mats[2]
    fc2_bias_g, fc1_bias_g, out_bias_g, ln2_gain_g, ln2_bias_g = early_vecs
    qkv_weight_g = late_mats[0]
    qkv_bias_g, ln1_gain_g, ln1_bias_g, frequencies_g = late_vecs
    pieces = (
        ln1_gain_g,
        ln1_bias_g,
        qkv_weight_g,
        qkv_bias_g,
        out_weight_g,
        out_bias_g,
        ln2_gain_g,
        ln2_bias_g,
        fc1_weight_g,
        fc1_bias_g,
        fc2_weight_g,
        fc2_bias_g,
        frequencies_g,
    )
    return (
        block_out,
        tokens_grad,
        *pieces,
        jnp.sqrt(freq_sq),
        jnp.sqrt(other_sq),
    )


def solution(mesh):
    placed = (
        P(("fsdp", "dp"), None),
        P(("fsdp", "dp"), None),
        P("fsdp"),
        P("fsdp"),
        P("fsdp", None),
        P("fsdp"),
        P("fsdp", None),
        P("fsdp"),
        P("fsdp"),
        P("fsdp"),
        P("fsdp", None),
        P("fsdp"),
        P("fsdp", None),
        P("fsdp"),
        P("fsdp"),
        P(("fsdp", "dp"), None),
    )
    return jax.shard_map(
        shards,
        mesh=mesh,
        in_specs=placed,
        out_specs=(
            P(("fsdp", "dp"), None),
            P(("fsdp", "dp"), None),
            P("fsdp"),
            P("fsdp"),
            P("fsdp", None),
            P("fsdp"),
            P("fsdp", None),
            P("fsdp"),
            P("fsdp"),
            P("fsdp"),
            P("fsdp", None),
            P("fsdp"),
            P("fsdp", None),
            P("fsdp"),
            P("fsdp"),
            P(),
            P(),
        ),
        check_vma=False,
    )
```

```python
import jax
import jax.numpy as jnp
from jax import lax
from jax.experimental import pallas as pl
from jax.sharding import PartitionSpec as P


H = 12
HD = 64
BIN = 1024
Q_BLOCK = 256


norm_eps = 1e-06
masked_score = -1e30
inv_sqrt_two_pi = 0.3989422804014327


def matmul(left, right):
    return jnp.dot(left, right, preferred_element_type=jnp.float32)


def matmul_left_t(left, right):
    return lax.dot_general(
        left, right, (((0,), (0,)), ((), ())), preferred_element_type=jnp.float32
    )


def matmul_right_t(left, right):
    return lax.dot_general(
        left, right, (((1,), (1,)), ((), ())), preferred_element_type=jnp.float32
    )


def image_layout(image_table, bin_count, bin_rows):
    slot_count = image_table.shape[0] // bin_count
    table = image_table.reshape(bin_count, slot_count, 3)
    offset = table[:, :, 0:1]
    height = table[:, :, 1:2]
    width = table[:, :, 2:3]
    place = jnp.arange(bin_rows, dtype=jnp.int32)[None, None, :]
    inside = ((place >= offset) & (place < offset + height * width)).astype(jnp.int32)
    live = jnp.sum(inside, axis=1)
    slot_ids = jnp.arange(slot_count, dtype=jnp.int32)[None, :, None]
    segment = jnp.sum(inside * slot_ids, axis=1) + slot_count * (1 - live)
    local_place = place[:, 0, :] - jnp.sum(inside * offset, axis=1)
    grid_width = jnp.maximum(jnp.sum(inside * width, axis=1), 1)
    grid_row = local_place // grid_width * live
    grid_col = local_place % grid_width * live
    return (
        segment,
        grid_row.reshape(-1).astype(jnp.float32),
        grid_col.reshape(-1).astype(jnp.float32),
    )


def rotary_tables(frequencies, grid_row, grid_col):
    half_width = frequencies.shape[0] // 2
    freq_float = frequencies.astype(jnp.float32)
    freq_row = freq_float[:half_width].reshape(H, HD // 2)
    freq_col = freq_float[half_width:].reshape(H, HD // 2)
    theta = grid_row[:, None, None] * freq_row[None] + grid_col[:, None, None] * freq_col[None]
    return (jnp.cos(theta), jnp.sin(theta))


def rotate(heads, cosine, sine):
    half_width = heads.shape[-1] // 2
    first = heads[..., :half_width]
    second = heads[..., half_width:]
    return jnp.concatenate(
        [first * cosine - second * sine, first * sine + second * cosine], axis=-1
    )


def layer_norm_forward(values):
    center = values - jnp.mean(values, axis=-1, keepdims=True)
    inverse_deviation = lax.rsqrt(jnp.mean(center * center, axis=-1, keepdims=True) + norm_eps)
    return (center * inverse_deviation, inverse_deviation)


def layer_norm_backward(
    gradient_norm_total, centered_normalized, inverse_deviation, norm_gain_vector
):
    gain_scaled_output = gradient_norm_total * norm_gain_vector
    return inverse_deviation * (
        gain_scaled_output
        - jnp.mean(gain_scaled_output, axis=-1, keepdims=True)
        - centered_normalized
        * jnp.mean(gain_scaled_output * centered_normalized, axis=-1, keepdims=True)
    )


def gelu_slope(values):
    return (
        0.5 * (1.0 + lax.erf(values * 0.7071067811865476))
        + values * jnp.exp(-0.5 * values * values) * inv_sqrt_two_pi
    )


def _nt(a, b):
    return lax.dot_general(a, b, (((1,), (1,)), ((), ())), preferred_element_type=jnp.float32)


def _tn(a, b):
    return lax.dot_general(a, b, (((0,), (0,)), ((), ())), preferred_element_type=jnp.float32)


def _nn(a, b):
    return lax.dot_general(a, b, (((1,), (0,)), ((), ())), preferred_element_type=jnp.float32)


def attention_forward_kernel(q_ref, k_ref, v_ref, seg_r_ref, seg_c_ref, o_ref, lse_ref):
    rows = q_ref.shape[0]
    seg_c = seg_c_ref[...]
    scale = HD ** (-0.5)
    for half in range(q_ref.shape[1] // HD):
        cols = slice(half * HD, (half + 1) * HD)
        k_h = k_ref[:, cols]
        v_h = v_ref[:, cols]

        def block(i, carry):
            at = pl.multiple_of(i * Q_BLOCK, Q_BLOCK)
            q_h = q_ref[pl.ds(at, Q_BLOCK), cols]
            mask = seg_r_ref[pl.ds(at, Q_BLOCK), :] == seg_c
            scores = jnp.where(mask, _nt(q_h, k_h) * scale, masked_score)
            top = jnp.max(scores, axis=-1, keepdims=True)
            shifted = jnp.exp(scores - top)
            total = jnp.sum(shifted, axis=-1, keepdims=True)
            log_total = top + jnp.log(total)
            probs = (shifted * (1.0 / total)).astype(jnp.bfloat16)
            o_ref[pl.ds(at, Q_BLOCK), cols] = _nn(probs, v_h).astype(o_ref.dtype)
            lse_ref[pl.ds(at, Q_BLOCK), cols] = jnp.broadcast_to(log_total, (Q_BLOCK, HD))
            return carry

        lax.fori_loop(0, rows // Q_BLOCK, block, 0)


def attention_backward_kernel(q_ref, k_ref, v_ref, d_ref, lse_ref, seg_r_ref, seg_c_ref, dq_ref, dk_ref, dv_ref):
    rows = q_ref.shape[0]
    seg_c = seg_c_ref[...]
    scale = HD ** (-0.5)
    for half in range(q_ref.shape[1] // HD):
        cols = slice(half * HD, (half + 1) * HD)
        k_h = k_ref[:, cols]
        v_h = v_ref[:, cols]

        def block(i, carry):
            dk_acc, dv_acc = carry
            at = pl.multiple_of(i * Q_BLOCK, Q_BLOCK)
            q_h = q_ref[pl.ds(at, Q_BLOCK), cols]
            d_h = d_ref[pl.ds(at, Q_BLOCK), cols]
            log_total = lse_ref[pl.ds(at, Q_BLOCK), pl.ds(half * HD, 1)]
            mask = seg_r_ref[pl.ds(at, Q_BLOCK), :] == seg_c
            scores = jnp.where(mask, _nt(q_h, k_h) * scale, masked_score)
            probs = jnp.exp(scores - log_total)
            d_probs = _nt(d_h, v_h)
            dv_acc = dv_acc + _tn(probs.astype(jnp.bfloat16), d_h)
            inner = jnp.sum(probs * d_probs, axis=-1, keepdims=True)
            d_scores = (probs * (d_probs - inner)).astype(jnp.bfloat16)
            dq_ref[pl.ds(at, Q_BLOCK), cols] = _nn(d_scores, k_h) * scale
            dk_acc = dk_acc + _tn(d_scores, q_h)
            return dk_acc, dv_acc

        zero = jnp.zeros((rows, HD), jnp.float32)
        dk_acc, dv_acc = lax.fori_loop(0, rows // Q_BLOCK, block, (zero, zero))
        dk_ref[:, cols] = dk_acc * scale
        dv_ref[:, cols] = dv_acc


def attention_forward(q, k, v, segment):
    rows, width = q.shape
    pair = 2 * HD
    seg_r = segment.reshape(rows, 1)
    seg_c = segment.reshape(1, rows)
    spec = pl.BlockSpec((rows, pair), lambda j: (0, j))
    return pl.pallas_call(
        attention_forward_kernel,
        grid=(width // pair,),
        in_specs=[spec, spec, spec, pl.BlockSpec((rows, 1), lambda j: (0, 0)), pl.BlockSpec((1, rows), lambda j: (0, 0))],
        out_specs=[spec, spec],
        out_shape=[jax.ShapeDtypeStruct((rows, width), jnp.bfloat16), jax.ShapeDtypeStruct((rows, width), jnp.float32)],
        cost_estimate=pl.CostEstimate(
            flops=4 * rows * rows * width, transcendentals=2 * rows * rows * (width // HD),
            bytes_accessed=rows * width * (2 * 4 + 4)),
        name="attention_forward",
    )(q, k, v, seg_r, seg_c)


def attention_backward(q, k, v, d_mixed, log_total, segment):
    rows, width = q.shape
    pair = 2 * HD
    seg_r = segment.reshape(rows, 1)
    seg_c = segment.reshape(1, rows)
    spec = pl.BlockSpec((rows, pair), lambda j: (0, j))
    f32 = jax.ShapeDtypeStruct((rows, width), jnp.float32)
    return pl.pallas_call(
        attention_backward_kernel,
        grid=(width // pair,),
        in_specs=[spec, spec, spec, spec, spec, pl.BlockSpec((rows, 1), lambda j: (0, 0)), pl.BlockSpec((1, rows), lambda j: (0, 0))],
        out_specs=[spec, spec, spec],
        out_shape=[f32, f32, f32],
        cost_estimate=pl.CostEstimate(
            flops=8 * rows * rows * width, transcendentals=rows * rows * (width // HD),
            bytes_accessed=rows * width * (2 * 4 + 4 + 12)),
        name="attention_backward",
    )(q, k, v, d_mixed, log_total, seg_r, seg_c)


def attention_bins(q_low, k_low, v_low, segment):
    outs = [attention_forward(q_low[b * BIN:(b + 1) * BIN], k_low[b * BIN:(b + 1) * BIN],
                              v_low[b * BIN:(b + 1) * BIN], segment[b]) for b in range(segment.shape[0])]
    return tuple(jnp.concatenate(parts, axis=0) for parts in zip(*outs))


def attention_bins_back(q_low, k_low, v_low, d_mixed, log_total, segment):
    outs = [attention_backward(q_low[b * BIN:(b + 1) * BIN], k_low[b * BIN:(b + 1) * BIN],
                               v_low[b * BIN:(b + 1) * BIN], d_mixed[b * BIN:(b + 1) * BIN],
                               log_total[b * BIN:(b + 1) * BIN], segment[b]) for b in range(segment.shape[0])]
    return tuple(jnp.concatenate(parts, axis=0) for parts in zip(*outs))


def quarter(shard):
    part = shard.shape[0] // lax.psum(1, "dp")
    return lax.dynamic_slice_in_dim(shard, lax.axis_index("dp") * part, part, 0)


def gather_with_small(left, right, vectors):
    rows = quarter(left).shape[0]
    flat = quarter(jnp.concatenate(vectors))
    cols = -(-flat.shape[0] // rows)
    tile = jnp.pad(flat, (0, rows * cols - flat.shape[0])).reshape(rows, cols)
    tile = jnp.pad(tile, ((0, 0), (0, -cols % 128)))
    joined = jnp.concatenate([quarter(left), quarter(right), tile], axis=1)
    whole = lax.all_gather(joined, ("fsdp", "dp"), axis=0, tiled=True)
    split = left.shape[1] + right.shape[1]
    groups = lax.psum(1, "fsdp")
    small = whole[:, split : split + cols].reshape(lax.psum(1, ("fsdp", "dp")), -1)[:, : flat.shape[0]]
    small = small.reshape(groups, -1)
    out, at = [], 0
    for v in vectors:
        out.append(small[:, at : at + v.shape[0]].reshape(-1))
        at += v.shape[0]
    return whole[:, : left.shape[1]], whole[:, left.shape[1] : split], out


def gather_alone(shard):
    return lax.all_gather(quarter(shard), ("fsdp", "dp"), axis=0, tiled=True)


def pack_columns(matrices, vectors):
    blocks = lax.psum(1, ("fsdp", "dp"))
    rows = matrices[0].shape[0]
    per_block = rows // blocks
    flat = jnp.concatenate([v.reshape(blocks, -1) for v in vectors], axis=1)
    small = flat.shape[1]
    small_cols = -(-small // per_block)
    flat = jnp.pad(flat, ((0, 0), (0, small_cols * per_block - small)))
    flat = flat.reshape(rows, small_cols)
    padded_cols = -(-small_cols // 128) * 128
    flat = jnp.pad(flat, ((0, 0), (0, padded_cols - small_cols)))
    parts = [m.astype(jnp.bfloat16) for m in matrices] + [flat.astype(jnp.bfloat16)]
    layout = ([m.shape[1] for m in matrices], small_cols, padded_cols, [v.shape[0] // blocks for v in vectors])
    return jnp.concatenate(parts, axis=1), layout


def unpack_columns(owned, layout):
    widths, small_cols, _, vector_sizes = layout
    groups = lax.psum(1, "dp")
    out, at = [], 0
    for w in widths:
        out.append(owned[:, at : at + w].astype(jnp.float32))
        at += w
    flat = owned[:, at : at + small_cols].reshape(groups, -1)
    vectors, at = [], 0
    for n in vector_sizes:
        vectors.append(flat[:, at : at + n].reshape(-1).astype(jnp.float32))
        at += n
    return out, vectors


def square_sums_of_block(mine, layout, last_vectors):
    widths, small_cols, _, vector_sizes = layout
    values = mine.astype(jnp.float32)
    at = sum(widths)
    flat = values[:, at : at + small_cols].reshape(-1)
    split = sum(vector_sizes[: len(vector_sizes) - last_vectors])
    end = sum(vector_sizes)
    last = jnp.sum(flat[split:end] * flat[split:end])
    rest = jnp.sum(values[:, :at] * values[:, :at]) + jnp.sum(flat[:split] * flat[:split])
    return last, rest


def sum_on_sparse_core(packed, layout):
    mine = lax.psum_scatter(packed, ("fsdp", "dp"), scatter_dimension=0, tiled=True)
    owned = lax.all_gather(mine, "dp", axis=0, tiled=True)
    return unpack_columns(owned, layout), mine


def sum_by_exchange(packed, layout, carried):
    blocks = lax.psum(1, ("fsdp", "dp"))
    received = lax.all_to_all(packed, ("fsdp", "dp"), 0, 0, tiled=True)
    mine = jnp.sum(received.reshape(blocks, -1, packed.shape[1]).astype(jnp.float32), axis=0)
    freq_part, rest_part = square_sums_of_block(mine, layout, 1)
    rest_part = rest_part + carried
    extra = jnp.zeros((mine.shape[0], 128), jnp.float32).at[0, 0].set(freq_part).at[0, 1].set(rest_part)
    owned = lax.all_gather(jnp.concatenate([mine, extra], axis=1), "dp", axis=0, tiled=True)
    partials = jnp.sum(owned[:: mine.shape[0], packed.shape[1] : packed.shape[1] + 2], axis=0)
    return unpack_columns(owned[:, : packed.shape[1]], layout), partials


def shards(
    tokens,
    image_table,
    ln1_gain,
    ln1_bias,
    qkv_weight,
    qkv_bias,
    out_weight,
    out_bias,
    ln2_gain,
    ln2_bias,
    fc1_weight,
    fc1_bias,
    fc2_weight,
    fc2_bias,
    frequencies,
    cotangent,
):
    small_local = [ln1_gain, ln1_bias, qkv_bias, out_bias, ln2_gain, ln2_bias, fc1_bias, fc2_bias, frequencies]
    g_qkv_weight, g_out_weight, small_whole = gather_with_small(qkv_weight, out_weight, small_local)
    (g_ln1_gain, g_ln1_bias, g_qkv_bias, g_out_bias, g_ln2_gain, g_ln2_bias, g_fc1_bias, g_fc2_bias,
     g_frequencies) = small_whole
    g_fc1_weight = gather_alone(fc1_weight)
    g_fc2_weight = gather_alone(fc2_weight)
    block_parameters = (
        g_ln1_gain,
        g_ln1_bias,
        g_qkv_weight,
        g_qkv_bias,
        g_out_weight,
        g_out_bias,
        g_ln2_gain,
        g_ln2_bias,
        g_fc1_weight,
        g_fc1_bias,
        g_fc2_weight,
        g_fc2_bias,
        g_frequencies,
    )
    row_count, width = tokens.shape
    bin_count = row_count // BIN
    half_head = HD // 2
    segment, grid_row, grid_col = image_layout(image_table, bin_count, BIN)
    cosine, sine = rotary_tables(block_parameters[12], grid_row, grid_col)
    input_single_precision = tokens.astype(jnp.float32)
    first_centered_normalized, first_inverse_deviation = layer_norm_forward(input_single_precision)
    first_activation = (
        first_centered_normalized * block_parameters[0].astype(jnp.float32)
        + block_parameters[1].astype(jnp.float32)
    ).astype(jnp.bfloat16)
    qkv_full = matmul(first_activation, block_parameters[2]) + block_parameters[3].astype(
        jnp.float32
    )
    q_rot = rotate(qkv_full[:, :width].reshape(row_count, H, HD), cosine, sine)
    k_rot = rotate(qkv_full[:, width : 2 * width].reshape(row_count, H, HD), cosine, sine)
    q_low = q_rot.reshape(row_count, width).astype(jnp.bfloat16)
    k_low = k_rot.reshape(row_count, width).astype(jnp.bfloat16)
    v_low = qkv_full[:, 2 * width :].astype(jnp.bfloat16)
    mixed, log_total = attention_bins(q_low, k_low, v_low, segment)
    residual_stream = (
        input_single_precision
        + matmul(mixed, block_parameters[4])
        + block_parameters[5].astype(jnp.float32)
    )
    second_centered_normalized, second_inverse_deviation = layer_norm_forward(residual_stream)
    second_activation = (
        second_centered_normalized * block_parameters[6].astype(jnp.float32)
        + block_parameters[7].astype(jnp.float32)
    ).astype(jnp.bfloat16)
    up_proj = matmul(second_activation, block_parameters[8]) + block_parameters[9].astype(
        jnp.float32
    )
    gelu_low = jax.nn.gelu(up_proj, approximate=False).astype(jnp.bfloat16)
    block_out = (
        residual_stream
        + matmul(gelu_low, block_parameters[10])
        + block_parameters[11].astype(jnp.float32)
    ).astype(jnp.bfloat16)
    output_gradient = cotangent.astype(jnp.float32)
    fc2_bias_grad = jnp.sum(output_gradient, axis=0)
    fc2_weight_grad = matmul_left_t(gelu_low, cotangent)
    d_up = (matmul_right_t(cotangent, block_parameters[10]) * gelu_slope(up_proj)).astype(
        jnp.bfloat16
    )
    fc1_bias_grad = jnp.sum(d_up.astype(jnp.float32), axis=0)
    fc1_weight_grad = matmul_left_t(second_activation, d_up)
    second_activation_gradient = matmul_right_t(d_up, block_parameters[8])
    second_norm_gain_gradient = jnp.sum(
        second_activation_gradient * second_centered_normalized, axis=0
    )
    ln2_bias_grad = jnp.sum(second_activation_gradient, axis=0)
    residual_gradient = output_gradient + layer_norm_backward(
        second_activation_gradient,
        second_centered_normalized,
        second_inverse_deviation,
        block_parameters[6].astype(jnp.float32),
    )
    d_att = residual_gradient.astype(jnp.bfloat16)
    out_bias_grad = jnp.sum(d_att.astype(jnp.float32), axis=0)
    out_weight_grad = matmul_left_t(mixed, d_att)
    d_mixed = matmul_right_t(d_att, block_parameters[4]).astype(jnp.bfloat16)
    early_packed, early_layout = pack_columns(
        [fc2_weight_grad.reshape(fc1_weight_grad.shape[0], -1), fc1_weight_grad, out_weight_grad],
        [fc2_bias_grad, fc1_bias_grad, out_bias_grad, second_norm_gain_gradient, ln2_bias_grad],
    )
    early_packed, d_mixed = lax.optimization_barrier((early_packed, d_mixed))
    (early_mats, early_vecs), early_mine = sum_on_sparse_core(early_packed, early_layout)
    d_qrot, d_krot, d_value = attention_bins_back(q_low, k_low, v_low, d_mixed, log_total, segment)
    d_qrot = d_qrot.reshape(row_count, H, HD)
    d_krot = d_krot.reshape(row_count, H, HD)
    d_theta = (
        d_qrot[..., half_head:] * q_rot[..., :half_head]
        - d_qrot[..., :half_head] * q_rot[..., half_head:]
    )
    d_theta = (
        d_theta
        + d_krot[..., half_head:] * k_rot[..., :half_head]
        - d_krot[..., :half_head] * k_rot[..., half_head:]
    )
    frequencies_grad = jnp.concatenate(
        [
            jnp.sum(grid_row[:, None, None] * d_theta, axis=0).reshape(-1),
            jnp.sum(grid_col[:, None, None] * d_theta, axis=0).reshape(-1),
        ]
    )
    d_query = rotate(d_qrot, cosine, -sine).reshape(row_count, width)
    d_key = rotate(d_krot, cosine, -sine).reshape(row_count, width)
    d_qkv = jnp.concatenate([d_query, d_key, d_value.reshape(row_count, width)], axis=1).astype(
        jnp.bfloat16
    )
    qkv_bias_grad = jnp.sum(d_qkv.astype(jnp.float32), axis=0)
    qkv_weight_grad = matmul_left_t(first_activation, d_qkv)
    first_activation_gradient = matmul_right_t(d_qkv, block_parameters[2])
    first_norm_gain_gradient = jnp.sum(
        first_activation_gradient * first_centered_normalized, axis=0
    )
    ln1_bias_grad = jnp.sum(first_activation_gradient, axis=0)
    tokens_grad = (
        residual_gradient
        + layer_norm_backward(
            first_activation_gradient,
            first_centered_normalized,
            first_inverse_deviation,
            block_parameters[0].astype(jnp.float32),
        )
    ).astype(jnp.bfloat16)
    late_packed, late_layout = pack_columns(
        [qkv_weight_grad],
        [qkv_bias_grad, first_norm_gain_gradient, ln1_bias_grad, frequencies_grad],
    )
    late_packed, tokens_grad = lax.optimization_barrier((late_packed, tokens_grad))
    _, early_sq = square_sums_of_block(early_mine, early_layout, 0)
    (late_mats, late_vecs), partials = sum_by_exchange(late_packed, late_layout, early_sq)
    freq_sq, other_sq = lax.psum((partials[0], partials[1]), "fsdp")
    fc2_weight_g = early_mats[0].reshape(fc2_weight.shape)
    fc1_weight_g = early_mats[1]
    out_weight_g = early_mats[2]
    fc2_bias_g, fc1_bias_g, out_bias_g, ln2_gain_g, ln2_bias_g = early_vecs
    qkv_weight_g = late_mats[0]
    qkv_bias_g, ln1_gain_g, ln1_bias_g, frequencies_g = late_vecs
    pieces = (
        ln1_gain_g,
        ln1_bias_g,
        qkv_weight_g,
        qkv_bias_g,
        out_weight_g,
        out_bias_g,
        ln2_gain_g,
        ln2_bias_g,
        fc1_weight_g,
        fc1_bias_g,
        fc2_weight_g,
        fc2_bias_g,
        frequencies_g,
    )
    return (
        block_out,
        tokens_grad,
        *pieces,
        jnp.sqrt(freq_sq),
        jnp.sqrt(other_sq),
    )


def solution(mesh):
    placed = (
        P(("fsdp", "dp"), None),
        P(("fsdp", "dp"), None),
        P("fsdp"),
        P("fsdp"),
        P("fsdp", None),
        P("fsdp"),
        P("fsdp", None),
        P("fsdp"),
        P("fsdp"),
        P("fsdp"),
        P("fsdp", None),
        P("fsdp"),
        P("fsdp", None),
        P("fsdp"),
        P("fsdp"),
        P(("fsdp", "dp"), None),
    )
    return jax.shard_map(
        shards,
        mesh=mesh,
        in_specs=placed,
        out_specs=(
            P(("fsdp", "dp"), None),
            P(("fsdp", "dp"), None),
            P("fsdp"),
            P("fsdp"),
            P("fsdp", None),
            P("fsdp"),
            P("fsdp", None),
            P("fsdp"),
            P("fsdp"),
            P("fsdp"),
            P("fsdp", None),
            P("fsdp"),
            P("fsdp", None),
            P("fsdp"),
            P("fsdp"),
            P(),
            P(),
        ),
        check_vma=False,
    )
```

```python
import jax
import jax.numpy as jnp
from jax import lax
from jax.experimental import pallas as pl
from jax.sharding import PartitionSpec as P


H = 12
HD = 64
BIN = 1024
Q_BLOCK = 256


norm_eps = 1e-06
masked_score = -1e30
inv_sqrt_two_pi = 0.3989422804014327


def matmul(left, right):
    return jnp.dot(left, right, preferred_element_type=jnp.float32)


def matmul_left_t(left, right):
    return lax.dot_general(
        left, right, (((0,), (0,)), ((), ())), preferred_element_type=jnp.float32
    )


def matmul_right_t(left, right):
    return lax.dot_general(
        left, right, (((1,), (1,)), ((), ())), preferred_element_type=jnp.float32
    )


def image_layout(image_table, bin_count, bin_rows):
    slot_count = image_table.shape[0] // bin_count
    table = image_table.reshape(bin_count, slot_count, 3)
    offset = table[:, :, 0:1]
    height = table[:, :, 1:2]
    width = table[:, :, 2:3]
    place = jnp.arange(bin_rows, dtype=jnp.int32)[None, None, :]
    inside = ((place >= offset) & (place < offset + height * width)).astype(jnp.int32)
    live = jnp.sum(inside, axis=1)
    slot_ids = jnp.arange(slot_count, dtype=jnp.int32)[None, :, None]
    segment = jnp.sum(inside * slot_ids, axis=1) + slot_count * (1 - live)
    local_place = place[:, 0, :] - jnp.sum(inside * offset, axis=1)
    grid_width = jnp.maximum(jnp.sum(inside * width, axis=1), 1)
    grid_row = local_place // grid_width * live
    grid_col = local_place % grid_width * live
    return (
        segment,
        grid_row.reshape(-1).astype(jnp.float32),
        grid_col.reshape(-1).astype(jnp.float32),
    )


def lane_tables(frequencies, grid_row, grid_col, width):
    half_width = frequencies.shape[0] // 2
    freq_float = frequencies.astype(jnp.float32)
    freq_row = freq_float[:half_width].reshape(H, HD // 2)
    freq_col = freq_float[half_width:].reshape(H, HD // 2)
    lane_row = jnp.concatenate([freq_row, freq_row], axis=1).reshape(width)
    lane_col = jnp.concatenate([freq_col, freq_col], axis=1).reshape(width)
    theta = grid_row[:, None] * lane_row[None] + grid_col[:, None] * lane_col[None]
    first = (jnp.arange(width, dtype=jnp.int32) % HD) < HD // 2
    sine = jnp.sin(theta)
    return jnp.cos(theta), jnp.where(first[None], -sine, sine), first


def swap_halves(values, first):
    return jnp.where(
        first[None], jnp.roll(values, -(HD // 2), axis=1), jnp.roll(values, HD // 2, axis=1)
    )


def layer_norm_forward(values):
    center = values - jnp.mean(values, axis=-1, keepdims=True)
    inverse_deviation = lax.rsqrt(jnp.mean(center * center, axis=-1, keepdims=True) + norm_eps)
    return (center * inverse_deviation, inverse_deviation)


def layer_norm_backward(
    gradient_norm_total, centered_normalized, inverse_deviation, norm_gain_vector
):
    gain_scaled_output = gradient_norm_total * norm_gain_vector
    return inverse_deviation * (
        gain_scaled_output
        - jnp.mean(gain_scaled_output, axis=-1, keepdims=True)
        - centered_normalized
        * jnp.mean(gain_scaled_output * centered_normalized, axis=-1, keepdims=True)
    )


def gelu_slope(values):
    return (
        0.5 * (1.0 + lax.erf(values * 0.7071067811865476))
        + values * jnp.exp(-0.5 * values * values) * inv_sqrt_two_pi
    )


def _nt(a, b):
    return lax.dot_general(a, b, (((1,), (1,)), ((), ())), preferred_element_type=jnp.float32)


def _tn(a, b):
    return lax.dot_general(a, b, (((0,), (0,)), ((), ())), preferred_element_type=jnp.float32)


def _nn(a, b):
    return lax.dot_general(a, b, (((1,), (0,)), ((), ())), preferred_element_type=jnp.float32)


def attention_forward_kernel(q_ref, k_ref, v_ref, seg_r_ref, seg_c_ref, o_ref, lse_ref):
    rows = q_ref.shape[0]
    seg_c = seg_c_ref[...]
    scale = HD ** (-0.5)
    for half in range(q_ref.shape[1] // HD):
        cols = slice(half * HD, (half + 1) * HD)
        k_h = k_ref[:, cols]
        v_h = v_ref[:, cols]

        def block(i, carry):
            at = pl.multiple_of(i * Q_BLOCK, Q_BLOCK)
            q_h = q_ref[pl.ds(at, Q_BLOCK), cols]
            mask = seg_r_ref[pl.ds(at, Q_BLOCK), :] == seg_c
            scores = jnp.where(mask, _nt(q_h, k_h) * scale, masked_score)
            top = jnp.max(scores, axis=-1, keepdims=True)
            log_total = top + jnp.log(jnp.sum(jnp.exp(scores - top), axis=-1, keepdims=True))
            probs = jnp.exp(scores - log_total).astype(jnp.bfloat16)
            o_ref[pl.ds(at, Q_BLOCK), cols] = _nn(probs, v_h).astype(o_ref.dtype)
            lse_ref[pl.ds(at, Q_BLOCK), cols] = jnp.broadcast_to(log_total, (Q_BLOCK, HD))
            return carry

        lax.fori_loop(0, rows // Q_BLOCK, block, 0)


def attention_backward_kernel(q_ref, k_ref, v_ref, d_ref, lse_ref, seg_r_ref, seg_c_ref, dq_ref, dk_ref, dv_ref):
    rows = q_ref.shape[0]
    seg_c = seg_c_ref[...]
    scale = HD ** (-0.5)
    for half in range(q_ref.shape[1] // HD):
        cols = slice(half * HD, (half + 1) * HD)
        k_h = k_ref[:, cols]
        v_h = v_ref[:, cols]

        def block(i, carry):
            dk_acc, dv_acc = carry
            at = pl.multiple_of(i * Q_BLOCK, Q_BLOCK)
            q_h = q_ref[pl.ds(at, Q_BLOCK), cols]
            d_h = d_ref[pl.ds(at, Q_BLOCK), cols]
            log_total = lse_ref[pl.ds(at, Q_BLOCK), pl.ds(half * HD, 1)]
            mask = seg_r_ref[pl.ds(at, Q_BLOCK), :] == seg_c
            scores = jnp.where(mask, _nt(q_h, k_h) * scale, masked_score)
            probs = jnp.exp(scores - log_total)
            d_probs = _nt(d_h, v_h)
            dv_acc = dv_acc + _tn(probs.astype(jnp.bfloat16), d_h)
            inner = jnp.sum(probs * d_probs, axis=-1, keepdims=True)
            d_scores = (probs * (d_probs - inner)).astype(jnp.bfloat16)
            dq_ref[pl.ds(at, Q_BLOCK), cols] = _nn(d_scores, k_h) * scale
            dk_acc = dk_acc + _tn(d_scores, q_h)
            return dk_acc, dv_acc

        zero = jnp.zeros((rows, HD), jnp.float32)
        dk_acc, dv_acc = lax.fori_loop(0, rows // Q_BLOCK, block, (zero, zero))
        dk_ref[:, cols] = dk_acc * scale
        dv_ref[:, cols] = dv_acc


def attention_forward(q, k, v, segment):
    rows, width = q.shape
    pair = 2 * HD
    seg_r = segment.reshape(rows, 1)
    seg_c = segment.reshape(1, rows)
    spec = pl.BlockSpec((rows, pair), lambda j: (0, j))
    return pl.pallas_call(
        attention_forward_kernel,
        grid=(width // pair,),
        in_specs=[spec, spec, spec, pl.BlockSpec((rows, 1), lambda j: (0, 0)), pl.BlockSpec((1, rows), lambda j: (0, 0))],
        out_specs=[spec, spec],
        out_shape=[jax.ShapeDtypeStruct((rows, width), jnp.bfloat16), jax.ShapeDtypeStruct((rows, width), jnp.float32)],
        cost_estimate=pl.CostEstimate(
            flops=4 * rows * rows * width, transcendentals=2 * rows * rows * (width // HD),
            bytes_accessed=rows * width * (2 * 4 + 4)),
        name="attention_forward",
    )(q, k, v, seg_r, seg_c)


def attention_backward(q, k, v, d_mixed, log_total, segment):
    rows, width = q.shape
    pair = 2 * HD
    seg_r = segment.reshape(rows, 1)
    seg_c = segment.reshape(1, rows)
    spec = pl.BlockSpec((rows, pair), lambda j: (0, j))
    f32 = jax.ShapeDtypeStruct((rows, width), jnp.float32)
    return pl.pallas_call(
        attention_backward_kernel,
        grid=(width // pair,),
        in_specs=[spec, spec, spec, spec, spec, pl.BlockSpec((rows, 1), lambda j: (0, 0)), pl.BlockSpec((1, rows), lambda j: (0, 0))],
        out_specs=[spec, spec, spec],
        out_shape=[f32, f32, f32],
        cost_estimate=pl.CostEstimate(
            flops=8 * rows * rows * width, transcendentals=rows * rows * (width // HD),
            bytes_accessed=rows * width * (2 * 4 + 4 + 12)),
        name="attention_backward",
    )(q, k, v, d_mixed, log_total, seg_r, seg_c)


def attention_bins(q_low, k_low, v_low, segment):
    outs = [attention_forward(q_low[b * BIN:(b + 1) * BIN], k_low[b * BIN:(b + 1) * BIN],
                              v_low[b * BIN:(b + 1) * BIN], segment[b]) for b in range(segment.shape[0])]
    return tuple(jnp.concatenate(parts, axis=0) for parts in zip(*outs))


def attention_bins_back(q_low, k_low, v_low, d_mixed, log_total, segment):
    outs = [attention_backward(q_low[b * BIN:(b + 1) * BIN], k_low[b * BIN:(b + 1) * BIN],
                               v_low[b * BIN:(b + 1) * BIN], d_mixed[b * BIN:(b + 1) * BIN],
                               log_total[b * BIN:(b + 1) * BIN], segment[b]) for b in range(segment.shape[0])]
    return tuple(jnp.concatenate(parts, axis=0) for parts in zip(*outs))


def quarter(shard):
    part = shard.shape[0] // lax.psum(1, "dp")
    return lax.dynamic_slice_in_dim(shard, lax.axis_index("dp") * part, part, 0)


def gather_with_small(left, right, vectors):
    rows = quarter(left).shape[0]
    flat = quarter(jnp.concatenate(vectors))
    cols = -(-flat.shape[0] // rows)
    tile = jnp.pad(flat, (0, rows * cols - flat.shape[0])).reshape(rows, cols)
    tile = jnp.pad(tile, ((0, 0), (0, -cols % 128)))
    joined = jnp.concatenate([quarter(left), quarter(right), tile], axis=1)
    whole = lax.all_gather(joined, ("fsdp", "dp"), axis=0, tiled=True)
    split = left.shape[1] + right.shape[1]
    groups = lax.psum(1, "fsdp")
    small = whole[:, split : split + cols].reshape(lax.psum(1, ("fsdp", "dp")), -1)[:, : flat.shape[0]]
    small = small.reshape(groups, -1)
    out, at = [], 0
    for v in vectors:
        out.append(small[:, at : at + v.shape[0]].reshape(-1))
        at += v.shape[0]
    return whole[:, : left.shape[1]], whole[:, left.shape[1] : split], out


def gather_alone(shard):
    return lax.all_gather(quarter(shard), ("fsdp", "dp"), axis=0, tiled=True)


def pack_columns(matrices, vectors):
    blocks = lax.psum(1, ("fsdp", "dp"))
    rows = matrices[0].shape[0]
    per_block = rows // blocks
    flat = jnp.concatenate([v.reshape(blocks, -1) for v in vectors], axis=1)
    small = flat.shape[1]
    small_cols = -(-small // per_block)
    flat = jnp.pad(flat, ((0, 0), (0, small_cols * per_block - small)))
    flat = flat.reshape(rows, small_cols)
    padded_cols = -(-small_cols // 128) * 128
    flat = jnp.pad(flat, ((0, 0), (0, padded_cols - small_cols)))
    parts = [m.astype(jnp.bfloat16) for m in matrices] + [flat.astype(jnp.bfloat16)]
    layout = ([m.shape[1] for m in matrices], small_cols, padded_cols, [v.shape[0] // blocks for v in vectors])
    return jnp.concatenate(parts, axis=1), layout


def unpack_columns(owned, layout):
    widths, small_cols, _, vector_sizes = layout
    groups = lax.psum(1, "dp")
    out, at = [], 0
    for w in widths:
        out.append(owned[:, at : at + w].astype(jnp.float32))
        at += w
    flat = owned[:, at : at + small_cols].reshape(groups, -1)
    vectors, at = [], 0
    for n in vector_sizes:
        vectors.append(flat[:, at : at + n].reshape(-1).astype(jnp.float32))
        at += n
    return out, vectors


def square_sums_of_block(mine, layout, last_vectors):
    widths, small_cols, _, vector_sizes = layout
    values = mine.astype(jnp.float32)
    at = sum(widths)
    flat = values[:, at : at + small_cols].reshape(-1)
    split = sum(vector_sizes[: len(vector_sizes) - last_vectors])
    end = sum(vector_sizes)
    last = jnp.sum(flat[split:end] * flat[split:end])
    rest = jnp.sum(values[:, :at] * values[:, :at]) + jnp.sum(flat[:split] * flat[:split])
    return last, rest


def sum_on_sparse_core(packed, layout):
    mine = lax.psum_scatter(packed, ("fsdp", "dp"), scatter_dimension=0, tiled=True)
    owned = lax.all_gather(mine, "dp", axis=0, tiled=True)
    return unpack_columns(owned, layout), mine


def sum_by_exchange(packed, layout, carried):
    blocks = lax.psum(1, ("fsdp", "dp"))
    received = lax.all_to_all(packed, ("fsdp", "dp"), 0, 0, tiled=True)
    mine = jnp.sum(received.reshape(blocks, -1, packed.shape[1]).astype(jnp.float32), axis=0)
    freq_part, rest_part = square_sums_of_block(mine, layout, 1)
    rest_part = rest_part + carried
    extra = jnp.zeros((mine.shape[0], 128), jnp.float32).at[0, 0].set(freq_part).at[0, 1].set(rest_part)
    owned = lax.all_gather(jnp.concatenate([mine, extra], axis=1), "dp", axis=0, tiled=True)
    partials = jnp.sum(owned[:: mine.shape[0], packed.shape[1] : packed.shape[1] + 2], axis=0)
    return unpack_columns(owned[:, : packed.shape[1]], layout), partials


def shards(
    tokens,
    image_table,
    ln1_gain,
    ln1_bias,
    qkv_weight,
    qkv_bias,
    out_weight,
    out_bias,
    ln2_gain,
    ln2_bias,
    fc1_weight,
    fc1_bias,
    fc2_weight,
    fc2_bias,
    frequencies,
    cotangent,
):
    small_local = [ln1_gain, ln1_bias, qkv_bias, out_bias, ln2_gain, ln2_bias, fc1_bias, fc2_bias, frequencies]
    g_qkv_weight, g_out_weight, small_whole = gather_with_small(qkv_weight, out_weight, small_local)
    (g_ln1_gain, g_ln1_bias, g_qkv_bias, g_out_bias, g_ln2_gain, g_ln2_bias, g_fc1_bias, g_fc2_bias,
     g_frequencies) = small_whole
    g_fc1_weight = gather_alone(fc1_weight)
    g_fc2_weight = gather_alone(fc2_weight)
    block_parameters = (
        g_ln1_gain,
        g_ln1_bias,
        g_qkv_weight,
        g_qkv_bias,
        g_out_weight,
        g_out_bias,
        g_ln2_gain,
        g_ln2_bias,
        g_fc1_weight,
        g_fc1_bias,
        g_fc2_weight,
        g_fc2_bias,
        g_frequencies,
    )
    row_count, width = tokens.shape
    bin_count = row_count // BIN
    segment, grid_row, grid_col = image_layout(image_table, bin_count, BIN)
    input_single_precision = tokens.astype(jnp.float32)
    first_centered_normalized, first_inverse_deviation = layer_norm_forward(input_single_precision)
    first_activation = (
        first_centered_normalized * block_parameters[0].astype(jnp.float32)
        + block_parameters[1].astype(jnp.float32)
    ).astype(jnp.bfloat16)
    qkv_full = matmul(first_activation, block_parameters[2]) + block_parameters[3].astype(
        jnp.float32
    )
    lane_cos, lane_sin, first_half = lane_tables(block_parameters[12], grid_row, grid_col, width)
    q_full = qkv_full[:, :width]
    k_full = qkv_full[:, width : 2 * width]
    q_rot = q_full * lane_cos + swap_halves(q_full, first_half) * lane_sin
    k_rot = k_full * lane_cos + swap_halves(k_full, first_half) * lane_sin
    q_low = q_rot.astype(jnp.bfloat16)
    k_low = k_rot.astype(jnp.bfloat16)
    v_low = qkv_full[:, 2 * width :].astype(jnp.bfloat16)
    mixed, log_total = attention_bins(q_low, k_low, v_low, segment)
    residual_stream = (
        input_single_precision
        + matmul(mixed, block_parameters[4])
        + block_parameters[5].astype(jnp.float32)
    )
    second_centered_normalized, second_inverse_deviation = layer_norm_forward(residual_stream)
    second_activation = (
        second_centered_normalized * block_parameters[6].astype(jnp.float32)
        + block_parameters[7].astype(jnp.float32)
    ).astype(jnp.bfloat16)
    up_proj = matmul(second_activation, block_parameters[8]) + block_parameters[9].astype(
        jnp.float32
    )
    gelu_low = jax.nn.gelu(up_proj, approximate=False).astype(jnp.bfloat16)
    block_out = (
        residual_stream
        + matmul(gelu_low, block_parameters[10])
        + block_parameters[11].astype(jnp.float32)
    ).astype(jnp.bfloat16)
    output_gradient = cotangent.astype(jnp.float32)
    fc2_bias_grad = jnp.sum(output_gradient, axis=0)
    fc2_weight_grad = matmul_left_t(gelu_low, cotangent)
    d_up = (matmul_right_t(cotangent, block_parameters[10]) * gelu_slope(up_proj)).astype(
        jnp.bfloat16
    )
    fc1_bias_grad = jnp.sum(d_up.astype(jnp.float32), axis=0)
    fc1_weight_grad = matmul_left_t(second_activation, d_up)
    second_activation_gradient = matmul_right_t(d_up, block_parameters[8])
    second_norm_gain_gradient = jnp.sum(
        second_activation_gradient * second_centered_normalized, axis=0
    )
    ln2_bias_grad = jnp.sum(second_activation_gradient, axis=0)
    residual_gradient = output_gradient + layer_norm_backward(
        second_activation_gradient,
        second_centered_normalized,
        second_inverse_deviation,
        block_parameters[6].astype(jnp.float32),
    )
    d_att = residual_gradient.astype(jnp.bfloat16)
    out_bias_grad = jnp.sum(d_att.astype(jnp.float32), axis=0)
    out_weight_grad = matmul_left_t(mixed, d_att)
    d_mixed = matmul_right_t(d_att, block_parameters[4]).astype(jnp.bfloat16)
    early_packed, early_layout = pack_columns(
        [fc2_weight_grad.reshape(fc1_weight_grad.shape[0], -1), fc1_weight_grad, out_weight_grad],
        [fc2_bias_grad, fc1_bias_grad, out_bias_grad, second_norm_gain_gradient, ln2_bias_grad],
    )
    early_packed, d_mixed = lax.optimization_barrier((early_packed, d_mixed))
    (early_mats, early_vecs), early_mine = sum_on_sparse_core(early_packed, early_layout)
    d_qrot, d_krot, d_value = attention_bins_back(q_low, k_low, v_low, d_mixed, log_total, segment)
    q_terms = d_qrot * swap_halves(q_rot, first_half)
    k_terms = d_krot * swap_halves(k_rot, first_half)
    d_theta = swap_halves(q_terms, first_half) - q_terms
    d_theta = d_theta + swap_halves(k_terms, first_half) - k_terms
    row_sums = jnp.sum(grid_row[:, None] * d_theta, axis=0).reshape(H, 2, HD // 2)[:, 0]
    col_sums = jnp.sum(grid_col[:, None] * d_theta, axis=0).reshape(H, 2, HD // 2)[:, 0]
    frequencies_grad = jnp.concatenate([row_sums.reshape(-1), col_sums.reshape(-1)])
    d_query = d_qrot * lane_cos + swap_halves(d_qrot * lane_sin, first_half)
    d_key = d_krot * lane_cos + swap_halves(d_krot * lane_sin, first_half)
    d_qkv = jnp.concatenate([d_query, d_key, d_value.reshape(row_count, width)], axis=1).astype(
        jnp.bfloat16
    )
    qkv_bias_grad = jnp.sum(d_qkv.astype(jnp.float32), axis=0)
    qkv_weight_grad = matmul_left_t(first_activation, d_qkv)
    first_activation_gradient = matmul_right_t(d_qkv, block_parameters[2])
    first_norm_gain_gradient = jnp.sum(
        first_activation_gradient * first_centered_normalized, axis=0
    )
    ln1_bias_grad = jnp.sum(first_activation_gradient, axis=0)
    tokens_grad = (
        residual_gradient
        + layer_norm_backward(
            first_activation_gradient,
            first_centered_normalized,
            first_inverse_deviation,
            block_parameters[0].astype(jnp.float32),
        )
    ).astype(jnp.bfloat16)
    late_packed, late_layout = pack_columns(
        [qkv_weight_grad],
        [qkv_bias_grad, first_norm_gain_gradient, ln1_bias_grad, frequencies_grad],
    )
    late_packed, tokens_grad = lax.optimization_barrier((late_packed, tokens_grad))
    _, early_sq = square_sums_of_block(early_mine, early_layout, 0)
    (late_mats, late_vecs), partials = sum_by_exchange(late_packed, late_layout, early_sq)
    freq_sq, other_sq = lax.psum((partials[0], partials[1]), "fsdp")
    fc2_weight_g = early_mats[0].reshape(fc2_weight.shape)
    fc1_weight_g = early_mats[1]
    out_weight_g = early_mats[2]
    fc2_bias_g, fc1_bias_g, out_bias_g, ln2_gain_g, ln2_bias_g = early_vecs
    qkv_weight_g = late_mats[0]
    qkv_bias_g, ln1_gain_g, ln1_bias_g, frequencies_g = late_vecs
    pieces = (
        ln1_gain_g,
        ln1_bias_g,
        qkv_weight_g,
        qkv_bias_g,
        out_weight_g,
        out_bias_g,
        ln2_gain_g,
        ln2_bias_g,
        fc1_weight_g,
        fc1_bias_g,
        fc2_weight_g,
        fc2_bias_g,
        frequencies_g,
    )
    return (
        block_out,
        tokens_grad,
        *pieces,
        jnp.sqrt(freq_sq),
        jnp.sqrt(other_sq),
    )


def solution(mesh):
    placed = (
        P(("fsdp", "dp"), None),
        P(("fsdp", "dp"), None),
        P("fsdp"),
        P("fsdp"),
        P("fsdp", None),
        P("fsdp"),
        P("fsdp", None),
        P("fsdp"),
        P("fsdp"),
        P("fsdp"),
        P("fsdp", None),
        P("fsdp"),
        P("fsdp", None),
        P("fsdp"),
        P("fsdp"),
        P(("fsdp", "dp"), None),
    )
    return jax.shard_map(
        shards,
        mesh=mesh,
        in_specs=placed,
        out_specs=(
            P(("fsdp", "dp"), None),
            P(("fsdp", "dp"), None),
            P("fsdp"),
            P("fsdp"),
            P("fsdp", None),
            P("fsdp"),
            P("fsdp", None),
            P("fsdp"),
            P("fsdp"),
            P("fsdp"),
            P("fsdp", None),
            P("fsdp"),
            P("fsdp", None),
            P("fsdp"),
            P("fsdp"),
            P(),
            P(),
        ),
        check_vma=False,
    )
```

```python
import jax
import jax.numpy as jnp
from jax import lax
from jax.experimental import pallas as pl
from jax.sharding import PartitionSpec as P


H = 12
HD = 64
BIN = 1024
Q_BLOCK = 1024


norm_eps = 1e-06
masked_score = -1e30
inv_sqrt_two_pi = 0.3989422804014327


def matmul(left, right):
    return jnp.dot(left, right, preferred_element_type=jnp.float32)


def matmul_left_t(left, right):
    return lax.dot_general(
        left, right, (((0,), (0,)), ((), ())), preferred_element_type=jnp.float32
    )


def matmul_right_t(left, right):
    return lax.dot_general(
        left, right, (((1,), (1,)), ((), ())), preferred_element_type=jnp.float32
    )


def image_layout(image_table, bin_count, bin_rows):
    slot_count = image_table.shape[0] // bin_count
    table = image_table.reshape(bin_count, slot_count, 3)
    offset = table[:, :, 0:1]
    height = table[:, :, 1:2]
    width = table[:, :, 2:3]
    place = jnp.arange(bin_rows, dtype=jnp.int32)[None, None, :]
    inside = ((place >= offset) & (place < offset + height * width)).astype(jnp.int32)
    live = jnp.sum(inside, axis=1)
    slot_ids = jnp.arange(slot_count, dtype=jnp.int32)[None, :, None]
    segment = jnp.sum(inside * slot_ids, axis=1) + slot_count * (1 - live)
    local_place = place[:, 0, :] - jnp.sum(inside * offset, axis=1)
    grid_width = jnp.maximum(jnp.sum(inside * width, axis=1), 1)
    grid_row = local_place // grid_width * live
    grid_col = local_place % grid_width * live
    return (
        segment,
        grid_row.reshape(-1).astype(jnp.float32),
        grid_col.reshape(-1).astype(jnp.float32),
    )


def rotary_tables(frequencies, grid_row, grid_col):
    half_width = frequencies.shape[0] // 2
    freq_float = frequencies.astype(jnp.float32)
    freq_row = freq_float[:half_width].reshape(H, HD // 2)
    freq_col = freq_float[half_width:].reshape(H, HD // 2)
    theta = grid_row[:, None, None] * freq_row[None] + grid_col[:, None, None] * freq_col[None]
    return (jnp.cos(theta), jnp.sin(theta))


def rotate(heads, cosine, sine):
    half_width = heads.shape[-1] // 2
    first = heads[..., :half_width]
    second = heads[..., half_width:]
    return jnp.concatenate(
        [first * cosine - second * sine, first * sine + second * cosine], axis=-1
    )


def layer_norm_forward(values):
    center = values - jnp.mean(values, axis=-1, keepdims=True)
    inverse_deviation = lax.rsqrt(jnp.mean(center * center, axis=-1, keepdims=True) + norm_eps)
    return (center * inverse_deviation, inverse_deviation)


def layer_norm_backward(
    gradient_norm_total, centered_normalized, inverse_deviation, norm_gain_vector
):
    gain_scaled_output = gradient_norm_total * norm_gain_vector
    return inverse_deviation * (
        gain_scaled_output
        - jnp.mean(gain_scaled_output, axis=-1, keepdims=True)
        - centered_normalized
        * jnp.mean(gain_scaled_output * centered_normalized, axis=-1, keepdims=True)
    )


def gelu_slope(values):
    return (
        0.5 * (1.0 + lax.erf(values * 0.7071067811865476))
        + values * jnp.exp(-0.5 * values * values) * inv_sqrt_two_pi
    )


def _nt(a, b):
    return lax.dot_general(a, b, (((1,), (1,)), ((), ())), preferred_element_type=jnp.float32)


def _tn(a, b):
    return lax.dot_general(a, b, (((0,), (0,)), ((), ())), preferred_element_type=jnp.float32)


def _nn(a, b):
    return lax.dot_general(a, b, (((1,), (0,)), ((), ())), preferred_element_type=jnp.float32)


def attention_forward_kernel(q_ref, k_ref, v_ref, seg_r_ref, seg_c_ref, o_ref, lse_ref):
    rows = q_ref.shape[0]
    seg_c = seg_c_ref[...]
    scale = HD ** (-0.5)
    for half in range(q_ref.shape[1] // HD):
        cols = slice(half * HD, (half + 1) * HD)
        k_h = k_ref[:, cols]
        v_h = v_ref[:, cols]

        def block(i, carry):
            at = pl.multiple_of(i * Q_BLOCK, Q_BLOCK)
            q_h = q_ref[pl.ds(at, Q_BLOCK), cols]
            mask = seg_r_ref[pl.ds(at, Q_BLOCK), :] == seg_c
            scores = jnp.where(mask, _nt(q_h, k_h) * scale, masked_score)
            top = jnp.max(scores, axis=-1, keepdims=True)
            log_total = top + jnp.log(jnp.sum(jnp.exp(scores - top), axis=-1, keepdims=True))
            probs = jnp.exp(scores - log_total).astype(jnp.bfloat16)
            o_ref[pl.ds(at, Q_BLOCK), cols] = _nn(probs, v_h).astype(o_ref.dtype)
            lse_ref[pl.ds(at, Q_BLOCK), cols] = jnp.broadcast_to(log_total, (Q_BLOCK, HD))
            return carry

        lax.fori_loop(0, rows // Q_BLOCK, block, 0)


def attention_backward_kernel(q_ref, k_ref, v_ref, d_ref, lse_ref, seg_r_ref, seg_c_ref, dq_ref, dk_ref, dv_ref):
    rows = q_ref.shape[0]
    seg_c = seg_c_ref[...]
    scale = HD ** (-0.5)
    for half in range(q_ref.shape[1] // HD):
        cols = slice(half * HD, (half + 1) * HD)
        k_h = k_ref[:, cols]
        v_h = v_ref[:, cols]

        def block(i, carry):
            dk_acc, dv_acc = carry
            at = pl.multiple_of(i * Q_BLOCK, Q_BLOCK)
            q_h = q_ref[pl.ds(at, Q_BLOCK), cols]
            d_h = d_ref[pl.ds(at, Q_BLOCK), cols]
            log_total = lse_ref[pl.ds(at, Q_BLOCK), pl.ds(half * HD, 1)]
            mask = seg_r_ref[pl.ds(at, Q_BLOCK), :] == seg_c
            scores = jnp.where(mask, _nt(q_h, k_h) * scale, masked_score)
            probs = jnp.exp(scores - log_total)
            d_probs = _nt(d_h, v_h)
            dv_acc = dv_acc + _tn(probs.astype(jnp.bfloat16), d_h)
            inner = jnp.sum(probs * d_probs, axis=-1, keepdims=True)
            d_scores = (probs * (d_probs - inner)).astype(jnp.bfloat16)
            dq_ref[pl.ds(at, Q_BLOCK), cols] = _nn(d_scores, k_h) * scale
            dk_acc = dk_acc + _tn(d_scores, q_h)
            return dk_acc, dv_acc

        zero = jnp.zeros((rows, HD), jnp.float32)
        dk_acc, dv_acc = lax.fori_loop(0, rows // Q_BLOCK, block, (zero, zero))
        dk_ref[:, cols] = dk_acc * scale
        dv_ref[:, cols] = dv_acc


def attention_forward(q, k, v, segment):
    rows, width = q.shape
    pair = 2 * HD
    seg_r = segment.reshape(rows, 1)
    seg_c = segment.reshape(1, rows)
    spec = pl.BlockSpec((rows, pair), lambda j: (0, j))
    return pl.pallas_call(
        attention_forward_kernel,
        grid=(width // pair,),
        in_specs=[spec, spec, spec, pl.BlockSpec((rows, 1), lambda j: (0, 0)), pl.BlockSpec((1, rows), lambda j: (0, 0))],
        out_specs=[spec, spec],
        out_shape=[jax.ShapeDtypeStruct((rows, width), jnp.bfloat16), jax.ShapeDtypeStruct((rows, width), jnp.float32)],
        cost_estimate=pl.CostEstimate(
            flops=4 * rows * rows * width, transcendentals=2 * rows * rows * (width // HD),
            bytes_accessed=rows * width * (2 * 4 + 4)),
        name="attention_forward",
    )(q, k, v, seg_r, seg_c)


def attention_backward(q, k, v, d_mixed, log_total, segment):
    rows, width = q.shape
    pair = 2 * HD
    seg_r = segment.reshape(rows, 1)
    seg_c = segment.reshape(1, rows)
    spec = pl.BlockSpec((rows, pair), lambda j: (0, j))
    f32 = jax.ShapeDtypeStruct((rows, width), jnp.float32)
    return pl.pallas_call(
        attention_backward_kernel,
        grid=(width // pair,),
        in_specs=[spec, spec, spec, spec, spec, pl.BlockSpec((rows, 1), lambda j: (0, 0)), pl.BlockSpec((1, rows), lambda j: (0, 0))],
        out_specs=[spec, spec, spec],
        out_shape=[f32, f32, f32],
        cost_estimate=pl.CostEstimate(
            flops=8 * rows * rows * width, transcendentals=rows * rows * (width // HD),
            bytes_accessed=rows * width * (2 * 4 + 4 + 12)),
        name="attention_backward",
    )(q, k, v, d_mixed, log_total, seg_r, seg_c)


def attention_bins(q_low, k_low, v_low, segment):
    outs = [attention_forward(q_low[b * BIN:(b + 1) * BIN], k_low[b * BIN:(b + 1) * BIN],
                              v_low[b * BIN:(b + 1) * BIN], segment[b]) for b in range(segment.shape[0])]
    return tuple(jnp.concatenate(parts, axis=0) for parts in zip(*outs))


def attention_bins_back(q_low, k_low, v_low, d_mixed, log_total, segment):
    outs = [attention_backward(q_low[b * BIN:(b + 1) * BIN], k_low[b * BIN:(b + 1) * BIN],
                               v_low[b * BIN:(b + 1) * BIN], d_mixed[b * BIN:(b + 1) * BIN],
                               log_total[b * BIN:(b + 1) * BIN], segment[b]) for b in range(segment.shape[0])]
    return tuple(jnp.concatenate(parts, axis=0) for parts in zip(*outs))


def quarter(shard):
    part = shard.shape[0] // lax.psum(1, "dp")
    return lax.dynamic_slice_in_dim(shard, lax.axis_index("dp") * part, part, 0)


def gather_with_small(left, right, vectors):
    rows = quarter(left).shape[0]
    flat = quarter(jnp.concatenate(vectors))
    cols = -(-flat.shape[0] // rows)
    tile = jnp.pad(flat, (0, rows * cols - flat.shape[0])).reshape(rows, cols)
    tile = jnp.pad(tile, ((0, 0), (0, -cols % 128)))
    joined = jnp.concatenate([quarter(left), quarter(right), tile], axis=1)
    whole = lax.all_gather(joined, ("fsdp", "dp"), axis=0, tiled=True)
    split = left.shape[1] + right.shape[1]
    groups = lax.psum(1, "fsdp")
    small = whole[:, split : split + cols].reshape(lax.psum(1, ("fsdp", "dp")), -1)[:, : flat.shape[0]]
    small = small.reshape(groups, -1)
    out, at = [], 0
    for v in vectors:
        out.append(small[:, at : at + v.shape[0]].reshape(-1))
        at += v.shape[0]
    return whole[:, : left.shape[1]], whole[:, left.shape[1] : split], out


def gather_alone(shard):
    return lax.all_gather(quarter(shard), ("fsdp", "dp"), axis=0, tiled=True)


def pack_columns(matrices, vectors):
    blocks = lax.psum(1, ("fsdp", "dp"))
    rows = matrices[0].shape[0]
    per_block = rows // blocks
    flat = jnp.concatenate([v.reshape(blocks, -1) for v in vectors], axis=1)
    small = flat.shape[1]
    small_cols = -(-small // per_block)
    flat = jnp.pad(flat, ((0, 0), (0, small_cols * per_block - small)))
    flat = flat.reshape(rows, small_cols)
    padded_cols = -(-small_cols // 128) * 128
    flat = jnp.pad(flat, ((0, 0), (0, padded_cols - small_cols)))
    parts = [m.astype(jnp.bfloat16) for m in matrices] + [flat.astype(jnp.bfloat16)]
    layout = ([m.shape[1] for m in matrices], small_cols, padded_cols, [v.shape[0] // blocks for v in vectors])
    return jnp.concatenate(parts, axis=1), layout


def unpack_columns(owned, layout):
    widths, small_cols, _, vector_sizes = layout
    groups = lax.psum(1, "dp")
    out, at = [], 0
    for w in widths:
        out.append(owned[:, at : at + w].astype(jnp.float32))
        at += w
    flat = owned[:, at : at + small_cols].reshape(groups, -1)
    vectors, at = [], 0
    for n in vector_sizes:
        vectors.append(flat[:, at : at + n].reshape(-1).astype(jnp.float32))
        at += n
    return out, vectors


def square_sums_of_block(mine, layout, last_vectors):
    widths, small_cols, _, vector_sizes = layout
    values = mine.astype(jnp.float32)
    at = sum(widths)
    flat = values[:, at : at + small_cols].reshape(-1)
    split = sum(vector_sizes[: len(vector_sizes) - last_vectors])
    end = sum(vector_sizes)
    last = jnp.sum(flat[split:end] * flat[split:end])
    rest = jnp.sum(values[:, :at] * values[:, :at]) + jnp.sum(flat[:split] * flat[:split])
    return last, rest


def sum_on_sparse_core(packed, layout):
    mine = lax.psum_scatter(packed, ("fsdp", "dp"), scatter_dimension=0, tiled=True)
    owned = lax.all_gather(mine, "dp", axis=0, tiled=True)
    return unpack_columns(owned, layout), mine


def sum_by_exchange(packed, layout, carried):
    blocks = lax.psum(1, ("fsdp", "dp"))
    received = lax.all_to_all(packed, ("fsdp", "dp"), 0, 0, tiled=True)
    mine = jnp.sum(received.reshape(blocks, -1, packed.shape[1]).astype(jnp.float32), axis=0)
    freq_part, rest_part = square_sums_of_block(mine, layout, 1)
    rest_part = rest_part + carried
    extra = jnp.zeros((mine.shape[0], 128), jnp.float32).at[0, 0].set(freq_part).at[0, 1].set(rest_part)
    owned = lax.all_gather(jnp.concatenate([mine, extra], axis=1), "dp", axis=0, tiled=True)
    partials = jnp.sum(owned[:: mine.shape[0], packed.shape[1] : packed.shape[1] + 2], axis=0)
    return unpack_columns(owned[:, : packed.shape[1]], layout), partials


def shards(
    tokens,
    image_table,
    ln1_gain,
    ln1_bias,
    qkv_weight,
    qkv_bias,
    out_weight,
    out_bias,
    ln2_gain,
    ln2_bias,
    fc1_weight,
    fc1_bias,
    fc2_weight,
    fc2_bias,
    frequencies,
    cotangent,
):
    small_local = [ln1_gain, ln1_bias, qkv_bias, out_bias, ln2_gain, ln2_bias, fc1_bias, fc2_bias, frequencies]
    g_qkv_weight, g_out_weight, small_whole = gather_with_small(qkv_weight, out_weight, small_local)
    (g_ln1_gain, g_ln1_bias, g_qkv_bias, g_out_bias, g_ln2_gain, g_ln2_bias, g_fc1_bias, g_fc2_bias,
     g_frequencies) = small_whole
    g_fc1_weight = gather_alone(fc1_weight)
    g_fc2_weight = gather_alone(fc2_weight)
    block_parameters = (
        g_ln1_gain,
        g_ln1_bias,
        g_qkv_weight,
        g_qkv_bias,
        g_out_weight,
        g_out_bias,
        g_ln2_gain,
        g_ln2_bias,
        g_fc1_weight,
        g_fc1_bias,
        g_fc2_weight,
        g_fc2_bias,
        g_frequencies,
    )
    row_count, width = tokens.shape
    bin_count = row_count // BIN
    half_head = HD // 2
    segment, grid_row, grid_col = image_layout(image_table, bin_count, BIN)
    cosine, sine = rotary_tables(block_parameters[12], grid_row, grid_col)
    input_single_precision = tokens.astype(jnp.float32)
    first_centered_normalized, first_inverse_deviation = layer_norm_forward(input_single_precision)
    first_activation = (
        first_centered_normalized * block_parameters[0].astype(jnp.float32)
        + block_parameters[1].astype(jnp.float32)
    ).astype(jnp.bfloat16)
    qkv_full = matmul(first_activation, block_parameters[2]) + block_parameters[3].astype(
        jnp.float32
    )
    q_rot = rotate(qkv_full[:, :width].reshape(row_count, H, HD), cosine, sine)
    k_rot = rotate(qkv_full[:, width : 2 * width].reshape(row_count, H, HD), cosine, sine)
    q_low = q_rot.reshape(row_count, width).astype(jnp.bfloat16)
    k_low = k_rot.reshape(row_count, width).astype(jnp.bfloat16)
    v_low = qkv_full[:, 2 * width :].astype(jnp.bfloat16)
    mixed, log_total = attention_bins(q_low, k_low, v_low, segment)
    residual_stream = (
        input_single_precision
        + matmul(mixed, block_parameters[4])
        + block_parameters[5].astype(jnp.float32)
    )
    second_centered_normalized, second_inverse_deviation = layer_norm_forward(residual_stream)
    second_activation = (
        second_centered_normalized * block_parameters[6].astype(jnp.float32)
        + block_parameters[7].astype(jnp.float32)
    ).astype(jnp.bfloat16)
    up_proj = matmul(second_activation, block_parameters[8]) + block_parameters[9].astype(
        jnp.float32
    )
    gelu_low = jax.nn.gelu(up_proj, approximate=False).astype(jnp.bfloat16)
    block_out = (
        residual_stream
        + matmul(gelu_low, block_parameters[10])
        + block_parameters[11].astype(jnp.float32)
    ).astype(jnp.bfloat16)
    output_gradient = cotangent.astype(jnp.float32)
    fc2_bias_grad = jnp.sum(output_gradient, axis=0)
    fc2_weight_grad = matmul_left_t(gelu_low, cotangent)
    d_up = (matmul_right_t(cotangent, block_parameters[10]) * gelu_slope(up_proj)).astype(
        jnp.bfloat16
    )
    fc1_bias_grad = jnp.sum(d_up.astype(jnp.float32), axis=0)
    fc1_weight_grad = matmul_left_t(second_activation, d_up)
    second_activation_gradient = matmul_right_t(d_up, block_parameters[8])
    second_norm_gain_gradient = jnp.sum(
        second_activation_gradient * second_centered_normalized, axis=0
    )
    ln2_bias_grad = jnp.sum(second_activation_gradient, axis=0)
    residual_gradient = output_gradient + layer_norm_backward(
        second_activation_gradient,
        second_centered_normalized,
        second_inverse_deviation,
        block_parameters[6].astype(jnp.float32),
    )
    d_att = residual_gradient.astype(jnp.bfloat16)
    out_bias_grad = jnp.sum(d_att.astype(jnp.float32), axis=0)
    out_weight_grad = matmul_left_t(mixed, d_att)
    d_mixed = matmul_right_t(d_att, block_parameters[4]).astype(jnp.bfloat16)
    early_packed, early_layout = pack_columns(
        [fc2_weight_grad.reshape(fc1_weight_grad.shape[0], -1), fc1_weight_grad, out_weight_grad],
        [fc2_bias_grad, fc1_bias_grad, out_bias_grad, second_norm_gain_gradient, ln2_bias_grad],
    )
    early_packed, d_mixed = lax.optimization_barrier((early_packed, d_mixed))
    (early_mats, early_vecs), early_mine = sum_on_sparse_core(early_packed, early_layout)
    d_qrot, d_krot, d_value = attention_bins_back(q_low, k_low, v_low, d_mixed, log_total, segment)
    d_qrot = d_qrot.reshape(row_count, H, HD)
    d_krot = d_krot.reshape(row_count, H, HD)
    d_theta = (
        d_qrot[..., half_head:] * q_rot[..., :half_head]
        - d_qrot[..., :half_head] * q_rot[..., half_head:]
    )
    d_theta = (
        d_theta
        + d_krot[..., half_head:] * k_rot[..., :half_head]
        - d_krot[..., :half_head] * k_rot[..., half_head:]
    )
    frequencies_grad = jnp.concatenate(
        [
            jnp.sum(grid_row[:, None, None] * d_theta, axis=0).reshape(-1),
            jnp.sum(grid_col[:, None, None] * d_theta, axis=0).reshape(-1),
        ]
    )
    d_query = rotate(d_qrot, cosine, -sine).reshape(row_count, width)
    d_key = rotate(d_krot, cosine, -sine).reshape(row_count, width)
    d_qkv = jnp.concatenate([d_query, d_key, d_value.reshape(row_count, width)], axis=1).astype(
        jnp.bfloat16
    )
    qkv_bias_grad = jnp.sum(d_qkv.astype(jnp.float32), axis=0)
    qkv_weight_grad = matmul_left_t(first_activation, d_qkv)
    first_activation_gradient = matmul_right_t(d_qkv, block_parameters[2])
    first_norm_gain_gradient = jnp.sum(
        first_activation_gradient * first_centered_normalized, axis=0
    )
    ln1_bias_grad = jnp.sum(first_activation_gradient, axis=0)
    tokens_grad = (
        residual_gradient
        + layer_norm_backward(
            first_activation_gradient,
            first_centered_normalized,
            first_inverse_deviation,
            block_parameters[0].astype(jnp.float32),
        )
    ).astype(jnp.bfloat16)
    late_packed, late_layout = pack_columns(
        [qkv_weight_grad],
        [qkv_bias_grad, first_norm_gain_gradient, ln1_bias_grad, frequencies_grad],
    )
    late_packed, tokens_grad = lax.optimization_barrier((late_packed, tokens_grad))
    _, early_sq = square_sums_of_block(early_mine, early_layout, 0)
    (late_mats, late_vecs), partials = sum_by_exchange(late_packed, late_layout, early_sq)
    freq_sq, other_sq = lax.psum((partials[0], partials[1]), "fsdp")
    fc2_weight_g = early_mats[0].reshape(fc2_weight.shape)
    fc1_weight_g = early_mats[1]
    out_weight_g = early_mats[2]
    fc2_bias_g, fc1_bias_g, out_bias_g, ln2_gain_g, ln2_bias_g = early_vecs
    qkv_weight_g = late_mats[0]
    qkv_bias_g, ln1_gain_g, ln1_bias_g, frequencies_g = late_vecs
    pieces = (
        ln1_gain_g,
        ln1_bias_g,
        qkv_weight_g,
        qkv_bias_g,
        out_weight_g,
        out_bias_g,
        ln2_gain_g,
        ln2_bias_g,
        fc1_weight_g,
        fc1_bias_g,
        fc2_weight_g,
        fc2_bias_g,
        frequencies_g,
    )
    return (
        block_out,
        tokens_grad,
        *pieces,
        jnp.sqrt(freq_sq),
        jnp.sqrt(other_sq),
    )


def solution(mesh):
    placed = (
        P(("fsdp", "dp"), None),
        P(("fsdp", "dp"), None),
        P("fsdp"),
        P("fsdp"),
        P("fsdp", None),
        P("fsdp"),
        P("fsdp", None),
        P("fsdp"),
        P("fsdp"),
        P("fsdp"),
        P("fsdp", None),
        P("fsdp"),
        P("fsdp", None),
        P("fsdp"),
        P("fsdp"),
        P(("fsdp", "dp"), None),
    )
    return jax.shard_map(
        shards,
        mesh=mesh,
        in_specs=placed,
        out_specs=(
            P(("fsdp", "dp"), None),
            P(("fsdp", "dp"), None),
            P("fsdp"),
            P("fsdp"),
            P("fsdp", None),
            P("fsdp"),
            P("fsdp", None),
            P("fsdp"),
            P("fsdp"),
            P("fsdp"),
            P("fsdp", None),
            P("fsdp"),
            P("fsdp", None),
            P("fsdp"),
            P("fsdp"),
            P(),
            P(),
        ),
        check_vma=False,
    )
```

```python
import jax
import jax.numpy as jnp
from jax import lax
from jax.experimental import pallas as pl
from jax.experimental.pallas import tpu as pltpu
from jax.sharding import PartitionSpec as P


H = 12
HD = 64
BIN = 1024
Q_BLOCK = 1024


norm_eps = 1e-06
masked_score = -1e30
inv_sqrt_two_pi = 0.3989422804014327


def matmul(left, right):
    return jnp.dot(left, right, preferred_element_type=jnp.float32)


def matmul_left_t(left, right):
    return lax.dot_general(
        left, right, (((0,), (0,)), ((), ())), preferred_element_type=jnp.float32
    )


def matmul_right_t(left, right):
    return lax.dot_general(
        left, right, (((1,), (1,)), ((), ())), preferred_element_type=jnp.float32
    )


def image_layout(image_table, bin_count, bin_rows):
    slot_count = image_table.shape[0] // bin_count
    table = image_table.reshape(bin_count, slot_count, 3)
    offset = table[:, :, 0:1]
    height = table[:, :, 1:2]
    width = table[:, :, 2:3]
    place = jnp.arange(bin_rows, dtype=jnp.int32)[None, None, :]
    inside = ((place >= offset) & (place < offset + height * width)).astype(jnp.int32)
    live = jnp.sum(inside, axis=1)
    slot_ids = jnp.arange(slot_count, dtype=jnp.int32)[None, :, None]
    segment = jnp.sum(inside * slot_ids, axis=1) + slot_count * (1 - live)
    local_place = place[:, 0, :] - jnp.sum(inside * offset, axis=1)
    grid_width = jnp.maximum(jnp.sum(inside * width, axis=1), 1)
    grid_row = local_place // grid_width * live
    grid_col = local_place % grid_width * live
    return (
        segment,
        grid_row.reshape(-1).astype(jnp.float32),
        grid_col.reshape(-1).astype(jnp.float32),
    )


def rotary_tables(frequencies, grid_row, grid_col):
    half_width = frequencies.shape[0] // 2
    freq_float = frequencies.astype(jnp.float32)
    freq_row = freq_float[:half_width].reshape(H, HD // 2)
    freq_col = freq_float[half_width:].reshape(H, HD // 2)
    theta = grid_row[:, None, None] * freq_row[None] + grid_col[:, None, None] * freq_col[None]
    return (jnp.cos(theta), jnp.sin(theta))


def rotate(heads, cosine, sine):
    half_width = heads.shape[-1] // 2
    first = heads[..., :half_width]
    second = heads[..., half_width:]
    return jnp.concatenate(
        [first * cosine - second * sine, first * sine + second * cosine], axis=-1
    )


def layer_norm_forward(values):
    center = values - jnp.mean(values, axis=-1, keepdims=True)
    inverse_deviation = lax.rsqrt(jnp.mean(center * center, axis=-1, keepdims=True) + norm_eps)
    return (center * inverse_deviation, inverse_deviation)


def layer_norm_backward(
    gradient_norm_total, centered_normalized, inverse_deviation, norm_gain_vector
):
    gain_scaled_output = gradient_norm_total * norm_gain_vector
    return inverse_deviation * (
        gain_scaled_output
        - jnp.mean(gain_scaled_output, axis=-1, keepdims=True)
        - centered_normalized
        * jnp.mean(gain_scaled_output * centered_normalized, axis=-1, keepdims=True)
    )


def gelu_slope(values):
    return (
        0.5 * (1.0 + lax.erf(values * 0.7071067811865476))
        + values * jnp.exp(-0.5 * values * values) * inv_sqrt_two_pi
    )


def _nt(a, b):
    return lax.dot_general(a, b, (((1,), (1,)), ((), ())), preferred_element_type=jnp.float32)


def _tn(a, b):
    return lax.dot_general(a, b, (((0,), (0,)), ((), ())), preferred_element_type=jnp.float32)


def _nn(a, b):
    return lax.dot_general(a, b, (((1,), (0,)), ((), ())), preferred_element_type=jnp.float32)


def build_bias(seg_r_ref, seg_c_ref, bias_ref):
    @pl.when(pl.program_id(0) == 0)
    def _():
        bias_ref[...] = jnp.where(seg_r_ref[...] == seg_c_ref[...], 0.0, masked_score).astype(jnp.float32)


def attention_forward_kernel(q_ref, k_ref, v_ref, seg_r_ref, seg_c_ref, o_ref, lse_ref, bias_ref):
    rows = q_ref.shape[0]
    scale = HD ** (-0.5)
    build_bias(seg_r_ref, seg_c_ref, bias_ref)
    for half in range(q_ref.shape[1] // HD):
        cols = slice(half * HD, (half + 1) * HD)
        k_h = k_ref[:, cols]
        v_h = v_ref[:, cols]

        def block(i, carry):
            at = pl.multiple_of(i * Q_BLOCK, Q_BLOCK)
            q_h = q_ref[pl.ds(at, Q_BLOCK), cols]
            scores = _nt(q_h, k_h) * scale + bias_ref[pl.ds(at, Q_BLOCK), :]
            top = jnp.max(scores, axis=-1, keepdims=True)
            log_total = top + jnp.log(jnp.sum(jnp.exp(scores - top), axis=-1, keepdims=True))
            probs = jnp.exp(scores - log_total).astype(jnp.bfloat16)
            o_ref[pl.ds(at, Q_BLOCK), cols] = _nn(probs, v_h).astype(o_ref.dtype)
            lse_ref[pl.ds(at, Q_BLOCK), cols] = jnp.broadcast_to(log_total, (Q_BLOCK, HD))
            return carry

        lax.fori_loop(0, rows // Q_BLOCK, block, 0)


def attention_backward_kernel(q_ref, k_ref, v_ref, d_ref, lse_ref, seg_r_ref, seg_c_ref, dq_ref, dk_ref, dv_ref, bias_ref):
    rows = q_ref.shape[0]
    scale = HD ** (-0.5)
    build_bias(seg_r_ref, seg_c_ref, bias_ref)
    for half in range(q_ref.shape[1] // HD):
        cols = slice(half * HD, (half + 1) * HD)
        k_h = k_ref[:, cols]
        v_h = v_ref[:, cols]

        def block(i, carry):
            dk_acc, dv_acc = carry
            at = pl.multiple_of(i * Q_BLOCK, Q_BLOCK)
            q_h = q_ref[pl.ds(at, Q_BLOCK), cols]
            d_h = d_ref[pl.ds(at, Q_BLOCK), cols]
            log_total = lse_ref[pl.ds(at, Q_BLOCK), pl.ds(half * HD, 1)]
            scores = _nt(q_h, k_h) * scale + bias_ref[pl.ds(at, Q_BLOCK), :]
            probs = jnp.exp(scores - log_total)
            d_probs = _nt(d_h, v_h)
            dv_acc = dv_acc + _tn(probs.astype(jnp.bfloat16), d_h)
            inner = jnp.sum(probs * d_probs, axis=-1, keepdims=True)
            d_scores = (probs * (d_probs - inner)).astype(jnp.bfloat16)
            dq_ref[pl.ds(at, Q_BLOCK), cols] = _nn(d_scores, k_h) * scale
            dk_acc = dk_acc + _tn(d_scores, q_h)
            return dk_acc, dv_acc

        zero = jnp.zeros((rows, HD), jnp.float32)
        dk_acc, dv_acc = lax.fori_loop(0, rows // Q_BLOCK, block, (zero, zero))
        dk_ref[:, cols] = dk_acc * scale
        dv_ref[:, cols] = dv_acc


def attention_forward(q, k, v, segment):
    rows, width = q.shape
    pair = 2 * HD
    seg_r = segment.reshape(rows, 1)
    seg_c = segment.reshape(1, rows)
    spec = pl.BlockSpec((rows, pair), lambda j: (0, j))
    return pl.pallas_call(
        attention_forward_kernel,
        grid=(width // pair,),
        in_specs=[spec, spec, spec, pl.BlockSpec((rows, 1), lambda j: (0, 0)), pl.BlockSpec((1, rows), lambda j: (0, 0))],
        out_specs=[spec, spec],
        out_shape=[jax.ShapeDtypeStruct((rows, width), jnp.bfloat16), jax.ShapeDtypeStruct((rows, width), jnp.float32)],
        scratch_shapes=[pltpu.VMEM((rows, rows), jnp.float32)],
        cost_estimate=pl.CostEstimate(
            flops=4 * rows * rows * width, transcendentals=2 * rows * rows * (width // HD),
            bytes_accessed=rows * width * (2 * 4 + 4)),
        name="attention_forward",
    )(q, k, v, seg_r, seg_c)


def attention_backward(q, k, v, d_mixed, log_total, segment):
    rows, width = q.shape
    pair = 2 * HD
    seg_r = segment.reshape(rows, 1)
    seg_c = segment.reshape(1, rows)
    spec = pl.BlockSpec((rows, pair), lambda j: (0, j))
    f32 = jax.ShapeDtypeStruct((rows, width), jnp.float32)
    return pl.pallas_call(
        attention_backward_kernel,
        grid=(width // pair,),
        in_specs=[spec, spec, spec, spec, spec, pl.BlockSpec((rows, 1), lambda j: (0, 0)), pl.BlockSpec((1, rows), lambda j: (0, 0))],
        out_specs=[spec, spec, spec],
        out_shape=[f32, f32, f32],
        scratch_shapes=[pltpu.VMEM((rows, rows), jnp.float32)],
        cost_estimate=pl.CostEstimate(
            flops=8 * rows * rows * width, transcendentals=rows * rows * (width // HD),
            bytes_accessed=rows * width * (2 * 4 + 4 + 12)),
        name="attention_backward",
    )(q, k, v, d_mixed, log_total, seg_r, seg_c)


def attention_bins(q_low, k_low, v_low, segment):
    outs = [attention_forward(q_low[b * BIN:(b + 1) * BIN], k_low[b * BIN:(b + 1) * BIN],
                              v_low[b * BIN:(b + 1) * BIN], segment[b]) for b in range(segment.shape[0])]
    return tuple(jnp.concatenate(parts, axis=0) for parts in zip(*outs))


def attention_bins_back(q_low, k_low, v_low, d_mixed, log_total, segment):
    outs = [attention_backward(q_low[b * BIN:(b + 1) * BIN], k_low[b * BIN:(b + 1) * BIN],
                               v_low[b * BIN:(b + 1) * BIN], d_mixed[b * BIN:(b + 1) * BIN],
                               log_total[b * BIN:(b + 1) * BIN], segment[b]) for b in range(segment.shape[0])]
    return tuple(jnp.concatenate(parts, axis=0) for parts in zip(*outs))


def quarter(shard):
    part = shard.shape[0] // lax.psum(1, "dp")
    return lax.dynamic_slice_in_dim(shard, lax.axis_index("dp") * part, part, 0)


def gather_with_small(left, right, vectors):
    rows = quarter(left).shape[0]
    flat = quarter(jnp.concatenate(vectors))
    cols = -(-flat.shape[0] // rows)
    tile = jnp.pad(flat, (0, rows * cols - flat.shape[0])).reshape(rows, cols)
    tile = jnp.pad(tile, ((0, 0), (0, -cols % 128)))
    joined = jnp.concatenate([quarter(left), quarter(right), tile], axis=1)
    whole = lax.all_gather(joined, ("fsdp", "dp"), axis=0, tiled=True)
    split = left.shape[1] + right.shape[1]
    groups = lax.psum(1, "fsdp")
    small = whole[:, split : split + cols].reshape(lax.psum(1, ("fsdp", "dp")), -1)[:, : flat.shape[0]]
    small = small.reshape(groups, -1)
    out, at = [], 0
    for v in vectors:
        out.append(small[:, at : at + v.shape[0]].reshape(-1))
        at += v.shape[0]
    return whole[:, : left.shape[1]], whole[:, left.shape[1] : split], out


def gather_alone(shard):
    return lax.all_gather(quarter(shard), ("fsdp", "dp"), axis=0, tiled=True)


def pack_columns(matrices, vectors):
    blocks = lax.psum(1, ("fsdp", "dp"))
    rows = matrices[0].shape[0]
    per_block = rows // blocks
    flat = jnp.concatenate([v.reshape(blocks, -1) for v in vectors], axis=1)
    small = flat.shape[1]
    small_cols = -(-small // per_block)
    flat = jnp.pad(flat, ((0, 0), (0, small_cols * per_block - small)))
    flat = flat.reshape(rows, small_cols)
    padded_cols = -(-small_cols // 128) * 128
    flat = jnp.pad(flat, ((0, 0), (0, padded_cols - small_cols)))
    parts = [m.astype(jnp.bfloat16) for m in matrices] + [flat.astype(jnp.bfloat16)]
    layout = ([m.shape[1] for m in matrices], small_cols, padded_cols, [v.shape[0] // blocks for v in vectors])
    return jnp.concatenate(parts, axis=1), layout


def unpack_columns(owned, layout):
    widths, small_cols, _, vector_sizes = layout
    groups = lax.psum(1, "dp")
    out, at = [], 0
    for w in widths:
        out.append(owned[:, at : at + w].astype(jnp.float32))
        at += w
    flat = owned[:, at : at + small_cols].reshape(groups, -1)
    vectors, at = [], 0
    for n in vector_sizes:
        vectors.append(flat[:, at : at + n].reshape(-1).astype(jnp.float32))
        at += n
    return out, vectors


def square_sums_of_block(mine, layout, last_vectors):
    widths, small_cols, _, vector_sizes = layout
    values = mine.astype(jnp.float32)
    at = sum(widths)
    flat = values[:, at : at + small_cols].reshape(-1)
    split = sum(vector_sizes[: len(vector_sizes) - last_vectors])
    end = sum(vector_sizes)
    last = jnp.sum(flat[split:end] * flat[split:end])
    rest = jnp.sum(values[:, :at] * values[:, :at]) + jnp.sum(flat[:split] * flat[:split])
    return last, rest


def sum_on_sparse_core(packed, layout):
    mine = lax.psum_scatter(packed, ("fsdp", "dp"), scatter_dimension=0, tiled=True)
    owned = lax.all_gather(mine, "dp", axis=0, tiled=True)
    return unpack_columns(owned, layout), mine


def sum_by_exchange(packed, layout, carried):
    blocks = lax.psum(1, ("fsdp", "dp"))
    received = lax.all_to_all(packed, ("fsdp", "dp"), 0, 0, tiled=True)
    mine = jnp.sum(received.reshape(blocks, -1, packed.shape[1]).astype(jnp.float32), axis=0)
    freq_part, rest_part = square_sums_of_block(mine, layout, 1)
    rest_part = rest_part + carried
    extra = jnp.zeros((mine.shape[0], 128), jnp.float32).at[0, 0].set(freq_part).at[0, 1].set(rest_part)
    owned = lax.all_gather(jnp.concatenate([mine, extra], axis=1), "dp", axis=0, tiled=True)
    partials = jnp.sum(owned[:: mine.shape[0], packed.shape[1] : packed.shape[1] + 2], axis=0)
    return unpack_columns(owned[:, : packed.shape[1]], layout), partials


def shards(
    tokens,
    image_table,
    ln1_gain,
    ln1_bias,
    qkv_weight,
    qkv_bias,
    out_weight,
    out_bias,
    ln2_gain,
    ln2_bias,
    fc1_weight,
    fc1_bias,
    fc2_weight,
    fc2_bias,
    frequencies,
    cotangent,
):
    small_local = [ln1_gain, ln1_bias, qkv_bias, out_bias, ln2_gain, ln2_bias, fc1_bias, fc2_bias, frequencies]
    g_qkv_weight, g_out_weight, small_whole = gather_with_small(qkv_weight, out_weight, small_local)
    (g_ln1_gain, g_ln1_bias, g_qkv_bias, g_out_bias, g_ln2_gain, g_ln2_bias, g_fc1_bias, g_fc2_bias,
     g_frequencies) = small_whole
    g_fc1_weight = gather_alone(fc1_weight)
    g_fc2_weight = gather_alone(fc2_weight)
    block_parameters = (
        g_ln1_gain,
        g_ln1_bias,
        g_qkv_weight,
        g_qkv_bias,
        g_out_weight,
        g_out_bias,
        g_ln2_gain,
        g_ln2_bias,
        g_fc1_weight,
        g_fc1_bias,
        g_fc2_weight,
        g_fc2_bias,
        g_frequencies,
    )
    row_count, width = tokens.shape
    bin_count = row_count // BIN
    half_head = HD // 2
    segment, grid_row, grid_col = image_layout(image_table, bin_count, BIN)
    cosine, sine = rotary_tables(block_parameters[12], grid_row, grid_col)
    input_single_precision = tokens.astype(jnp.float32)
    first_centered_normalized, first_inverse_deviation = layer_norm_forward(input_single_precision)
    first_activation = (
        first_centered_normalized * block_parameters[0].astype(jnp.float32)
        + block_parameters[1].astype(jnp.float32)
    ).astype(jnp.bfloat16)
    qkv_full = matmul(first_activation, block_parameters[2]) + block_parameters[3].astype(
        jnp.float32
    )
    q_rot = rotate(qkv_full[:, :width].reshape(row_count, H, HD), cosine, sine)
    k_rot = rotate(qkv_full[:, width : 2 * width].reshape(row_count, H, HD), cosine, sine)
    q_low = q_rot.reshape(row_count, width).astype(jnp.bfloat16)
    k_low = k_rot.reshape(row_count, width).astype(jnp.bfloat16)
    v_low = qkv_full[:, 2 * width :].astype(jnp.bfloat16)
    mixed, log_total = attention_bins(q_low, k_low, v_low, segment)
    residual_stream = (
        input_single_precision
        + matmul(mixed, block_parameters[4])
        + block_parameters[5].astype(jnp.float32)
    )
    second_centered_normalized, second_inverse_deviation = layer_norm_forward(residual_stream)
    second_activation = (
        second_centered_normalized * block_parameters[6].astype(jnp.float32)
        + block_parameters[7].astype(jnp.float32)
    ).astype(jnp.bfloat16)
    up_proj = matmul(second_activation, block_parameters[8]) + block_parameters[9].astype(
        jnp.float32
    )
    gelu_low = jax.nn.gelu(up_proj, approximate=False).astype(jnp.bfloat16)
    block_out = (
        residual_stream
        + matmul(gelu_low, block_parameters[10])
        + block_parameters[11].astype(jnp.float32)
    ).astype(jnp.bfloat16)
    output_gradient = cotangent.astype(jnp.float32)
    fc2_bias_grad = jnp.sum(output_gradient, axis=0)
    fc2_weight_grad = matmul_left_t(gelu_low, cotangent)
    d_up = (matmul_right_t(cotangent, block_parameters[10]) * gelu_slope(up_proj)).astype(
        jnp.bfloat16
    )
    fc1_bias_grad = jnp.sum(d_up.astype(jnp.float32), axis=0)
    fc1_weight_grad = matmul_left_t(second_activation, d_up)
    second_activation_gradient = matmul_right_t(d_up, block_parameters[8])
    second_norm_gain_gradient = jnp.sum(
        second_activation_gradient * second_centered_normalized, axis=0
    )
    ln2_bias_grad = jnp.sum(second_activation_gradient, axis=0)
    residual_gradient = output_gradient + layer_norm_backward(
        second_activation_gradient,
        second_centered_normalized,
        second_inverse_deviation,
        block_parameters[6].astype(jnp.float32),
    )
    d_att = residual_gradient.astype(jnp.bfloat16)
    out_bias_grad = jnp.sum(d_att.astype(jnp.float32), axis=0)
    out_weight_grad = matmul_left_t(mixed, d_att)
    d_mixed = matmul_right_t(d_att, block_parameters[4]).astype(jnp.bfloat16)
    early_packed, early_layout = pack_columns(
        [fc2_weight_grad.reshape(fc1_weight_grad.shape[0], -1), fc1_weight_grad, out_weight_grad],
        [fc2_bias_grad, fc1_bias_grad, out_bias_grad, second_norm_gain_gradient, ln2_bias_grad],
    )
    early_packed, d_mixed = lax.optimization_barrier((early_packed, d_mixed))
    (early_mats, early_vecs), early_mine = sum_on_sparse_core(early_packed, early_layout)
    d_qrot, d_krot, d_value = attention_bins_back(q_low, k_low, v_low, d_mixed, log_total, segment)
    d_qrot = d_qrot.reshape(row_count, H, HD)
    d_krot = d_krot.reshape(row_count, H, HD)
    d_theta = (
        d_qrot[..., half_head:] * q_rot[..., :half_head]
        - d_qrot[..., :half_head] * q_rot[..., half_head:]
    )
    d_theta = (
        d_theta
        + d_krot[..., half_head:] * k_rot[..., :half_head]
        - d_krot[..., :half_head] * k_rot[..., half_head:]
    )
    frequencies_grad = jnp.concatenate(
        [
            jnp.sum(grid_row[:, None, None] * d_theta, axis=0).reshape(-1),
            jnp.sum(grid_col[:, None, None] * d_theta, axis=0).reshape(-1),
        ]
    )
    d_query = rotate(d_qrot, cosine, -sine).reshape(row_count, width)
    d_key = rotate(d_krot, cosine, -sine).reshape(row_count, width)
    d_qkv = jnp.concatenate([d_query, d_key, d_value.reshape(row_count, width)], axis=1).astype(
        jnp.bfloat16
    )
    qkv_bias_grad = jnp.sum(d_qkv.astype(jnp.float32), axis=0)
    qkv_weight_grad = matmul_left_t(first_activation, d_qkv)
    first_activation_gradient = matmul_right_t(d_qkv, block_parameters[2])
    first_norm_gain_gradient = jnp.sum(
        first_activation_gradient * first_centered_normalized, axis=0
    )
    ln1_bias_grad = jnp.sum(first_activation_gradient, axis=0)
    tokens_grad = (
        residual_gradient
        + layer_norm_backward(
            first_activation_gradient,
            first_centered_normalized,
            first_inverse_deviation,
            block_parameters[0].astype(jnp.float32),
        )
    ).astype(jnp.bfloat16)
    late_packed, late_layout = pack_columns(
        [qkv_weight_grad],
        [qkv_bias_grad, first_norm_gain_gradient, ln1_bias_grad, frequencies_grad],
    )
    late_packed, tokens_grad = lax.optimization_barrier((late_packed, tokens_grad))
    _, early_sq = square_sums_of_block(early_mine, early_layout, 0)
    (late_mats, late_vecs), partials = sum_by_exchange(late_packed, late_layout, early_sq)
    freq_sq, other_sq = lax.psum((partials[0], partials[1]), "fsdp")
    fc2_weight_g = early_mats[0].reshape(fc2_weight.shape)
    fc1_weight_g = early_mats[1]
    out_weight_g = early_mats[2]
    fc2_bias_g, fc1_bias_g, out_bias_g, ln2_gain_g, ln2_bias_g = early_vecs
    qkv_weight_g = late_mats[0]
    qkv_bias_g, ln1_gain_g, ln1_bias_g, frequencies_g = late_vecs
    pieces = (
        ln1_gain_g,
        ln1_bias_g,
        qkv_weight_g,
        qkv_bias_g,
        out_weight_g,
        out_bias_g,
        ln2_gain_g,
        ln2_bias_g,
        fc1_weight_g,
        fc1_bias_g,
        fc2_weight_g,
        fc2_bias_g,
        frequencies_g,
    )
    return (
        block_out,
        tokens_grad,
        *pieces,
        jnp.sqrt(freq_sq),
        jnp.sqrt(other_sq),
    )


def solution(mesh):
    placed = (
        P(("fsdp", "dp"), None),
        P(("fsdp", "dp"), None),
        P("fsdp"),
        P("fsdp"),
        P("fsdp", None),
        P("fsdp"),
        P("fsdp", None),
        P("fsdp"),
        P("fsdp"),
        P("fsdp"),
        P("fsdp", None),
        P("fsdp"),
        P("fsdp", None),
        P("fsdp"),
        P("fsdp"),
        P(("fsdp", "dp"), None),
    )
    return jax.shard_map(
        shards,
        mesh=mesh,
        in_specs=placed,
        out_specs=(
            P(("fsdp", "dp"), None),
            P(("fsdp", "dp"), None),
            P("fsdp"),
            P("fsdp"),
            P("fsdp", None),
            P("fsdp"),
            P("fsdp", None),
            P("fsdp"),
            P("fsdp"),
            P("fsdp"),
            P("fsdp", None),
            P("fsdp"),
            P("fsdp", None),
            P("fsdp"),
            P("fsdp"),
            P(),
            P(),
        ),
        check_vma=False,
    )
```

```python
import jax
import jax.numpy as jnp
from jax import lax
from jax.experimental import pallas as pl
from jax.experimental.pallas import tpu as pltpu
from jax.sharding import PartitionSpec as P


H = 12
HD = 64
BIN = 1024
Q_BLOCK = 1024


norm_eps = 1e-06
masked_score = -1e30
inv_sqrt_two_pi = 0.3989422804014327


def matmul(left, right):
    return jnp.dot(left, right, preferred_element_type=jnp.float32)


def matmul_left_t(left, right):
    return lax.dot_general(
        left, right, (((0,), (0,)), ((), ())), preferred_element_type=jnp.float32
    )


def matmul_right_t(left, right):
    return lax.dot_general(
        left, right, (((1,), (1,)), ((), ())), preferred_element_type=jnp.float32
    )


def image_layout(image_table, bin_count, bin_rows):
    slot_count = image_table.shape[0] // bin_count
    table = image_table.reshape(bin_count, slot_count, 3)
    offset = table[:, :, 0:1]
    height = table[:, :, 1:2]
    width = table[:, :, 2:3]
    place = jnp.arange(bin_rows, dtype=jnp.int32)[None, None, :]
    inside = ((place >= offset) & (place < offset + height * width)).astype(jnp.int32)
    live = jnp.sum(inside, axis=1)
    slot_ids = jnp.arange(slot_count, dtype=jnp.int32)[None, :, None]
    segment = jnp.sum(inside * slot_ids, axis=1) + slot_count * (1 - live)
    local_place = place[:, 0, :] - jnp.sum(inside * offset, axis=1)
    grid_width = jnp.maximum(jnp.sum(inside * width, axis=1), 1)
    grid_row = local_place // grid_width * live
    grid_col = local_place % grid_width * live
    return (
        segment,
        grid_row.reshape(-1).astype(jnp.float32),
        grid_col.reshape(-1).astype(jnp.float32),
    )


def rotary_tables(frequencies, grid_row, grid_col):
    half_width = frequencies.shape[0] // 2
    freq_float = frequencies.astype(jnp.float32)
    freq_row = freq_float[:half_width].reshape(H, HD // 2)
    freq_col = freq_float[half_width:].reshape(H, HD // 2)
    theta = grid_row[:, None, None] * freq_row[None] + grid_col[:, None, None] * freq_col[None]
    return (jnp.cos(theta), jnp.sin(theta))


def rotate(heads, cosine, sine):
    half_width = heads.shape[-1] // 2
    first = heads[..., :half_width]
    second = heads[..., half_width:]
    return jnp.concatenate(
        [first * cosine - second * sine, first * sine + second * cosine], axis=-1
    )


def layer_norm_forward(values):
    center = values - jnp.mean(values, axis=-1, keepdims=True)
    inverse_deviation = lax.rsqrt(jnp.mean(center * center, axis=-1, keepdims=True) + norm_eps)
    return (center * inverse_deviation, inverse_deviation)


def layer_norm_backward(
    gradient_norm_total, centered_normalized, inverse_deviation, norm_gain_vector
):
    gain_scaled_output = gradient_norm_total * norm_gain_vector
    return inverse_deviation * (
        gain_scaled_output
        - jnp.mean(gain_scaled_output, axis=-1, keepdims=True)
        - centered_normalized
        * jnp.mean(gain_scaled_output * centered_normalized, axis=-1, keepdims=True)
    )


def gelu_slope(values):
    return (
        0.5 * (1.0 + lax.erf(values * 0.7071067811865476))
        + values * jnp.exp(-0.5 * values * values) * inv_sqrt_two_pi
    )


def _nt(a, b):
    return lax.dot_general(a, b, (((1,), (1,)), ((), ())), preferred_element_type=jnp.float32)


def _tn(a, b):
    return lax.dot_general(a, b, (((0,), (0,)), ((), ())), preferred_element_type=jnp.float32)


def _nn(a, b):
    return lax.dot_general(a, b, (((1,), (0,)), ((), ())), preferred_element_type=jnp.float32)


def build_bias(seg_r_ref, seg_c_ref, bias_ref):
    @pl.when(pl.program_id(0) == 0)
    def _():
        bias_ref[...] = jnp.where(seg_r_ref[...] == seg_c_ref[...], 0.0, masked_score).astype(jnp.float32)


def attention_forward_kernel(q_ref, k_ref, v_ref, seg_r_ref, seg_c_ref, o_ref, lse_ref, bias_ref):
    rows = q_ref.shape[0]
    scale = HD ** (-0.5)
    build_bias(seg_r_ref, seg_c_ref, bias_ref)
    for half in range(q_ref.shape[1] // HD):
        cols = slice(half * HD, (half + 1) * HD)
        k_h = k_ref[:, cols]
        v_h = v_ref[:, cols]

        def block(i, carry):
            at = pl.multiple_of(i * Q_BLOCK, Q_BLOCK)
            q_h = q_ref[pl.ds(at, Q_BLOCK), cols]
            scores = _nt(q_h, k_h) * scale + bias_ref[pl.ds(at, Q_BLOCK), :]
            top = jnp.max(scores, axis=-1, keepdims=True)
            log_total = top + jnp.log(jnp.sum(jnp.exp(scores - top), axis=-1, keepdims=True))
            probs = jnp.exp(scores - log_total).astype(jnp.bfloat16)
            o_ref[pl.ds(at, Q_BLOCK), cols] = _nn(probs, v_h).astype(o_ref.dtype)
            lse_ref[pl.ds(at, Q_BLOCK), cols] = jnp.broadcast_to(log_total, (Q_BLOCK, HD))
            return carry

        lax.fori_loop(0, rows // Q_BLOCK, block, 0)


def attention_backward_kernel(q_ref, k_ref, v_ref, d_ref, lse_ref, seg_r_ref, seg_c_ref, dq_ref, dk_ref, dv_ref, bias_ref):
    rows = q_ref.shape[0]
    scale = HD ** (-0.5)
    build_bias(seg_r_ref, seg_c_ref, bias_ref)
    for half in range(q_ref.shape[1] // HD):
        cols = slice(half * HD, (half + 1) * HD)
        k_h = k_ref[:, cols]
        v_h = v_ref[:, cols]

        def block(i, carry):
            dk_acc, dv_acc = carry
            at = pl.multiple_of(i * Q_BLOCK, Q_BLOCK)
            q_h = q_ref[pl.ds(at, Q_BLOCK), cols]
            d_h = d_ref[pl.ds(at, Q_BLOCK), cols]
            log_total = lse_ref[pl.ds(at, Q_BLOCK), pl.ds(half * HD, 1)]
            scores = _nt(q_h, k_h) * scale + bias_ref[pl.ds(at, Q_BLOCK), :]
            probs = jnp.exp(scores - log_total)
            d_probs = _nt(d_h, v_h)
            dv_acc = dv_acc + _tn(probs.astype(jnp.bfloat16), d_h)
            inner = jnp.sum(probs * d_probs, axis=-1, keepdims=True)
            d_scores = (probs * (d_probs - inner)).astype(jnp.bfloat16)
            dq_ref[pl.ds(at, Q_BLOCK), cols] = _nn(d_scores, k_h) * scale
            dk_acc = dk_acc + _tn(d_scores, q_h)
            return dk_acc, dv_acc

        zero = jnp.zeros((rows, HD), jnp.float32)
        dk_acc, dv_acc = lax.fori_loop(0, rows // Q_BLOCK, block, (zero, zero))
        dk_ref[:, cols] = dk_acc * scale
        dv_ref[:, cols] = dv_acc


def attention_forward(q, k, v, segment):
    rows, width = q.shape
    pair = 2 * HD
    seg_r = segment.reshape(rows, 1)
    seg_c = segment.reshape(1, rows)
    spec = pl.BlockSpec((rows, pair), lambda j: (0, j))
    return pl.pallas_call(
        attention_forward_kernel,
        grid=(width // pair,),
        in_specs=[spec, spec, spec, pl.BlockSpec((rows, 1), lambda j: (0, 0)), pl.BlockSpec((1, rows), lambda j: (0, 0))],
        out_specs=[spec, spec],
        out_shape=[jax.ShapeDtypeStruct((rows, width), jnp.bfloat16), jax.ShapeDtypeStruct((rows, width), jnp.float32)],
        scratch_shapes=[pltpu.VMEM((rows, rows), jnp.float32)],
        cost_estimate=pl.CostEstimate(
            flops=4 * rows * rows * width, transcendentals=2 * rows * rows * (width // HD),
            bytes_accessed=rows * width * (2 * 4 + 4)),
        name="attention_forward",
    )(q, k, v, seg_r, seg_c)


def attention_backward(q, k, v, d_mixed, log_total, segment):
    rows, width = q.shape
    pair = 2 * HD
    seg_r = segment.reshape(rows, 1)
    seg_c = segment.reshape(1, rows)
    spec = pl.BlockSpec((rows, pair), lambda j: (0, j))
    f32 = jax.ShapeDtypeStruct((rows, width), jnp.float32)
    return pl.pallas_call(
        attention_backward_kernel,
        grid=(width // pair,),
        in_specs=[spec, spec, spec, spec, spec, pl.BlockSpec((rows, 1), lambda j: (0, 0)), pl.BlockSpec((1, rows), lambda j: (0, 0))],
        out_specs=[spec, spec, spec],
        out_shape=[f32, f32, f32],
        scratch_shapes=[pltpu.VMEM((rows, rows), jnp.float32)],
        cost_estimate=pl.CostEstimate(
            flops=8 * rows * rows * width, transcendentals=rows * rows * (width // HD),
            bytes_accessed=rows * width * (2 * 4 + 4 + 12)),
        name="attention_backward",
    )(q, k, v, d_mixed, log_total, seg_r, seg_c)


def attention_bins(q_low, k_low, v_low, segment):
    outs = [attention_forward(q_low[b * BIN:(b + 1) * BIN], k_low[b * BIN:(b + 1) * BIN],
                              v_low[b * BIN:(b + 1) * BIN], segment[b]) for b in range(segment.shape[0])]
    return tuple(jnp.concatenate(parts, axis=0) for parts in zip(*outs))


def attention_bins_back(q_low, k_low, v_low, d_mixed, log_total, segment):
    outs = [attention_backward(q_low[b * BIN:(b + 1) * BIN], k_low[b * BIN:(b + 1) * BIN],
                               v_low[b * BIN:(b + 1) * BIN], d_mixed[b * BIN:(b + 1) * BIN],
                               log_total[b * BIN:(b + 1) * BIN], segment[b]) for b in range(segment.shape[0])]
    return tuple(jnp.concatenate(parts, axis=0) for parts in zip(*outs))


def quarter(shard):
    part = shard.shape[0] // lax.psum(1, "dp")
    return lax.dynamic_slice_in_dim(shard, lax.axis_index("dp") * part, part, 0)


def gather_with_small(left, right, vectors):
    rows = quarter(left).shape[0]
    flat = quarter(jnp.concatenate(vectors))
    cols = -(-flat.shape[0] // rows)
    tile = jnp.pad(flat, (0, rows * cols - flat.shape[0])).reshape(rows, cols)
    tile = jnp.pad(tile, ((0, 0), (0, -cols % 128)))
    joined = jnp.concatenate([quarter(left), quarter(right), tile], axis=1)
    whole = lax.all_gather(joined, ("fsdp", "dp"), axis=0, tiled=True)
    split = left.shape[1] + right.shape[1]
    groups = lax.psum(1, "fsdp")
    small = whole[:, split : split + cols].reshape(lax.psum(1, ("fsdp", "dp")), -1)[:, : flat.shape[0]]
    small = small.reshape(groups, -1)
    out, at = [], 0
    for v in vectors:
        out.append(small[:, at : at + v.shape[0]].reshape(-1))
        at += v.shape[0]
    return whole[:, : left.shape[1]], whole[:, left.shape[1] : split], out


def gather_alone(shard):
    return lax.all_gather(quarter(shard), ("fsdp", "dp"), axis=0, tiled=True)


def pack_columns(matrices, vectors):
    blocks = lax.psum(1, ("fsdp", "dp"))
    rows = matrices[0].shape[0]
    per_block = rows // blocks
    flat = jnp.concatenate([v.reshape(blocks, -1) for v in vectors], axis=1)
    small = flat.shape[1]
    small_cols = -(-small // per_block)
    flat = jnp.pad(flat, ((0, 0), (0, small_cols * per_block - small)))
    flat = flat.reshape(rows, small_cols)
    padded_cols = -(-small_cols // 128) * 128
    flat = jnp.pad(flat, ((0, 0), (0, padded_cols - small_cols)))
    parts = [m.astype(jnp.bfloat16) for m in matrices] + [flat.astype(jnp.bfloat16)]
    layout = ([m.shape[1] for m in matrices], small_cols, padded_cols, [v.shape[0] // blocks for v in vectors])
    return jnp.concatenate(parts, axis=1), layout


def unpack_columns(owned, layout):
    widths, small_cols, _, vector_sizes = layout
    groups = lax.psum(1, "dp")
    out, at = [], 0
    for w in widths:
        out.append(owned[:, at : at + w].astype(jnp.float32))
        at += w
    flat = owned[:, at : at + small_cols].reshape(groups, -1)
    vectors, at = [], 0
    for n in vector_sizes:
        vectors.append(flat[:, at : at + n].reshape(-1).astype(jnp.float32))
        at += n
    return out, vectors


def square_sums_of_block(mine, layout, last_vectors):
    widths, small_cols, _, vector_sizes = layout
    values = mine.astype(jnp.float32)
    at = sum(widths)
    flat = values[:, at : at + small_cols].reshape(-1)
    split = sum(vector_sizes[: len(vector_sizes) - last_vectors])
    end = sum(vector_sizes)
    last = jnp.sum(flat[split:end] * flat[split:end])
    rest = jnp.sum(values[:, :at] * values[:, :at]) + jnp.sum(flat[:split] * flat[:split])
    return last, rest


def sum_on_sparse_core(packed, layout):
    mine = lax.psum_scatter(packed, ("fsdp", "dp"), scatter_dimension=0, tiled=True)
    owned = lax.all_gather(mine, "dp", axis=0, tiled=True)
    return unpack_columns(owned, layout), mine


def sum_by_exchange(packed, layout, carried):
    blocks = lax.psum(1, ("fsdp", "dp"))
    received = lax.all_to_all(packed, ("fsdp", "dp"), 0, 0, tiled=True)
    mine = jnp.sum(received.reshape(blocks, -1, packed.shape[1]).astype(jnp.float32), axis=0)
    freq_part, rest_part = square_sums_of_block(mine, layout, 1)
    rest_part = rest_part + carried
    extra = jnp.zeros((mine.shape[0], 128), jnp.float32).at[0, 0].set(freq_part).at[0, 1].set(rest_part)
    owned = lax.all_gather(jnp.concatenate([mine, extra], axis=1), "dp", axis=0, tiled=True)
    partials = jnp.sum(owned[:: mine.shape[0], packed.shape[1] : packed.shape[1] + 2], axis=0)
    return unpack_columns(owned[:, : packed.shape[1]], layout), partials


def shards(
    tokens,
    image_table,
    ln1_gain,
    ln1_bias,
    qkv_weight,
    qkv_bias,
    out_weight,
    out_bias,
    ln2_gain,
    ln2_bias,
    fc1_weight,
    fc1_bias,
    fc2_weight,
    fc2_bias,
    frequencies,
    cotangent,
):
    small_local = [ln1_gain, ln1_bias, qkv_bias, out_bias, ln2_gain, ln2_bias, fc1_bias, fc2_bias, frequencies]
    g_qkv_weight, g_out_weight, small_whole = gather_with_small(qkv_weight, out_weight, small_local)
    (g_ln1_gain, g_ln1_bias, g_qkv_bias, g_out_bias, g_ln2_gain, g_ln2_bias, g_fc1_bias, g_fc2_bias,
     g_frequencies) = small_whole
    g_fc1_weight = gather_alone(fc1_weight)
    g_fc2_weight = gather_alone(fc2_weight)
    block_parameters = (
        g_ln1_gain,
        g_ln1_bias,
        g_qkv_weight,
        g_qkv_bias,
        g_out_weight,
        g_out_bias,
        g_ln2_gain,
        g_ln2_bias,
        g_fc1_weight,
        g_fc1_bias,
        g_fc2_weight,
        g_fc2_bias,
        g_frequencies,
    )
    row_count, width = tokens.shape
    bin_count = row_count // BIN
    half_head = HD // 2
    segment, grid_row, grid_col = image_layout(image_table, bin_count, BIN)
    cosine, sine = rotary_tables(block_parameters[12], grid_row, grid_col)
    input_single_precision = tokens.astype(jnp.float32)
    first_centered_normalized, first_inverse_deviation = layer_norm_forward(input_single_precision)
    first_activation = (
        first_centered_normalized * block_parameters[0].astype(jnp.float32)
        + block_parameters[1].astype(jnp.float32)
    ).astype(jnp.bfloat16)
    qkv_full = matmul(first_activation, block_parameters[2]) + block_parameters[3].astype(
        jnp.float32
    )
    q_rot = rotate(qkv_full[:, :width].reshape(row_count, H, HD), cosine, sine)
    k_rot = rotate(qkv_full[:, width : 2 * width].reshape(row_count, H, HD), cosine, sine)
    q_low = q_rot.reshape(row_count, width).astype(jnp.bfloat16)
    k_low = k_rot.reshape(row_count, width).astype(jnp.bfloat16)
    v_low = qkv_full[:, 2 * width :].astype(jnp.bfloat16)
    mixed, log_total = attention_bins(q_low, k_low, v_low, segment)
    residual_stream = (
        input_single_precision
        + matmul(mixed, block_parameters[4])
        + block_parameters[5].astype(jnp.float32)
    )
    second_centered_normalized, second_inverse_deviation = layer_norm_forward(residual_stream)
    second_activation = (
        second_centered_normalized * block_parameters[6].astype(jnp.float32)
        + block_parameters[7].astype(jnp.float32)
    ).astype(jnp.bfloat16)
    up_proj = matmul(second_activation, block_parameters[8]) + block_parameters[9].astype(
        jnp.float32
    )
    gelu_low = jax.nn.gelu(up_proj, approximate=False).astype(jnp.bfloat16)
    fc2_weight_grad = matmul_left_t(gelu_low, cotangent)
    fc2_recut = fc2_weight_grad.reshape(width, -1).astype(jnp.bfloat16)
    block_out = (
        residual_stream
        + matmul(gelu_low, block_parameters[10])
        + block_parameters[11].astype(jnp.float32)
    ).astype(jnp.bfloat16)
    output_gradient = cotangent.astype(jnp.float32)
    fc2_bias_grad = jnp.sum(output_gradient, axis=0)
    d_up = (matmul_right_t(cotangent, block_parameters[10]) * gelu_slope(up_proj)).astype(
        jnp.bfloat16
    )
    fc1_bias_grad = jnp.sum(d_up.astype(jnp.float32), axis=0)
    fc1_weight_grad = matmul_left_t(second_activation, d_up)
    second_activation_gradient = matmul_right_t(d_up, block_parameters[8])
    second_norm_gain_gradient = jnp.sum(
        second_activation_gradient * second_centered_normalized, axis=0
    )
    ln2_bias_grad = jnp.sum(second_activation_gradient, axis=0)
    residual_gradient = output_gradient + layer_norm_backward(
        second_activation_gradient,
        second_centered_normalized,
        second_inverse_deviation,
        block_parameters[6].astype(jnp.float32),
    )
    d_att = residual_gradient.astype(jnp.bfloat16)
    out_bias_grad = jnp.sum(d_att.astype(jnp.float32), axis=0)
    out_weight_grad = matmul_left_t(mixed, d_att)
    early_packed, early_layout = pack_columns(
        [fc2_recut, fc1_weight_grad, out_weight_grad],
        [fc2_bias_grad, fc1_bias_grad, out_bias_grad, second_norm_gain_gradient, ln2_bias_grad],
    )
    early_packed, d_att = lax.optimization_barrier((early_packed, d_att))
    d_mixed = matmul_right_t(d_att, block_parameters[4]).astype(jnp.bfloat16)
    (early_mats, early_vecs), early_mine = sum_on_sparse_core(early_packed, early_layout)
    d_qrot, d_krot, d_value = attention_bins_back(q_low, k_low, v_low, d_mixed, log_total, segment)
    d_qrot = d_qrot.reshape(row_count, H, HD)
    d_krot = d_krot.reshape(row_count, H, HD)
    d_theta = (
        d_qrot[..., half_head:] * q_rot[..., :half_head]
        - d_qrot[..., :half_head] * q_rot[..., half_head:]
    )
    d_theta = (
        d_theta
        + d_krot[..., half_head:] * k_rot[..., :half_head]
        - d_krot[..., :half_head] * k_rot[..., half_head:]
    )
    frequencies_grad = jnp.concatenate(
        [
            jnp.sum(grid_row[:, None, None] * d_theta, axis=0).reshape(-1),
            jnp.sum(grid_col[:, None, None] * d_theta, axis=0).reshape(-1),
        ]
    )
    d_query = rotate(d_qrot, cosine, -sine).reshape(row_count, width)
    d_key = rotate(d_krot, cosine, -sine).reshape(row_count, width)
    d_qkv = jnp.concatenate([d_query, d_key, d_value.reshape(row_count, width)], axis=1).astype(
        jnp.bfloat16
    )
    qkv_bias_grad = jnp.sum(d_qkv.astype(jnp.float32), axis=0)
    qkv_weight_grad = matmul_left_t(first_activation, d_qkv)
    first_activation_gradient = matmul_right_t(d_qkv, block_parameters[2])
    first_norm_gain_gradient = jnp.sum(
        first_activation_gradient * first_centered_normalized, axis=0
    )
    ln1_bias_grad = jnp.sum(first_activation_gradient, axis=0)
    tokens_grad = (
        residual_gradient
        + layer_norm_backward(
            first_activation_gradient,
            first_centered_normalized,
            first_inverse_deviation,
            block_parameters[0].astype(jnp.float32),
        )
    ).astype(jnp.bfloat16)
    late_packed, late_layout = pack_columns(
        [qkv_weight_grad],
        [qkv_bias_grad, first_norm_gain_gradient, ln1_bias_grad, frequencies_grad],
    )
    late_packed, tokens_grad = lax.optimization_barrier((late_packed, tokens_grad))
    _, early_sq = square_sums_of_block(early_mine, early_layout, 0)
    (late_mats, late_vecs), partials = sum_by_exchange(late_packed, late_layout, early_sq)
    freq_sq, other_sq = lax.psum((partials[0], partials[1]), "fsdp")
    fc2_weight_g = early_mats[0].reshape(fc2_weight.shape)
    fc1_weight_g = early_mats[1]
    out_weight_g = early_mats[2]
    fc2_bias_g, fc1_bias_g, out_bias_g, ln2_gain_g, ln2_bias_g = early_vecs
    qkv_weight_g = late_mats[0]
    qkv_bias_g, ln1_gain_g, ln1_bias_g, frequencies_g = late_vecs
    pieces = (
        ln1_gain_g,
        ln1_bias_g,
        qkv_weight_g,
        qkv_bias_g,
        out_weight_g,
        out_bias_g,
        ln2_gain_g,
        ln2_bias_g,
        fc1_weight_g,
        fc1_bias_g,
        fc2_weight_g,
        fc2_bias_g,
        frequencies_g,
    )
    return (
        block_out,
        tokens_grad,
        *pieces,
        jnp.sqrt(freq_sq),
        jnp.sqrt(other_sq),
    )


def solution(mesh):
    placed = (
        P(("fsdp", "dp"), None),
        P(("fsdp", "dp"), None),
        P("fsdp"),
        P("fsdp"),
        P("fsdp", None),
        P("fsdp"),
        P("fsdp", None),
        P("fsdp"),
        P("fsdp"),
        P("fsdp"),
        P("fsdp", None),
        P("fsdp"),
        P("fsdp", None),
        P("fsdp"),
        P("fsdp"),
        P(("fsdp", "dp"), None),
    )
    return jax.shard_map(
        shards,
        mesh=mesh,
        in_specs=placed,
        out_specs=(
            P(("fsdp", "dp"), None),
            P(("fsdp", "dp"), None),
            P("fsdp"),
            P("fsdp"),
            P("fsdp", None),
            P("fsdp"),
            P("fsdp", None),
            P("fsdp"),
            P("fsdp"),
            P("fsdp"),
            P("fsdp", None),
            P("fsdp"),
            P("fsdp", None),
            P("fsdp"),
            P("fsdp"),
            P(),
            P(),
        ),
        check_vma=False,
    )
```

```python
import jax
import jax.numpy as jnp
from jax import lax
from jax.experimental import pallas as pl
from jax.experimental.pallas import tpu as pltpu
from jax.sharding import PartitionSpec as P


H = 12
HD = 64
BIN = 1024
Q_BLOCK = 1024


norm_eps = 1e-06
masked_score = -1e30
inv_sqrt_two_pi = 0.3989422804014327


def matmul(left, right):
    return jnp.dot(left, right, preferred_element_type=jnp.float32)


def matmul_left_t(left, right):
    return lax.dot_general(
        left, right, (((0,), (0,)), ((), ())), preferred_element_type=jnp.float32
    )


def matmul_right_t(left, right):
    return lax.dot_general(
        left, right, (((1,), (1,)), ((), ())), preferred_element_type=jnp.float32
    )


def image_layout(image_table, bin_count, bin_rows):
    slot_count = image_table.shape[0] // bin_count
    table = image_table.reshape(bin_count, slot_count, 3)
    offset = table[:, :, 0:1]
    height = table[:, :, 1:2]
    width = table[:, :, 2:3]
    place = jnp.arange(bin_rows, dtype=jnp.int32)[None, None, :]
    inside = ((place >= offset) & (place < offset + height * width)).astype(jnp.int32)
    live = jnp.sum(inside, axis=1)
    slot_ids = jnp.arange(slot_count, dtype=jnp.int32)[None, :, None]
    segment = jnp.sum(inside * slot_ids, axis=1) + slot_count * (1 - live)
    local_place = place[:, 0, :] - jnp.sum(inside * offset, axis=1)
    grid_width = jnp.maximum(jnp.sum(inside * width, axis=1), 1)
    grid_row = local_place // grid_width * live
    grid_col = local_place % grid_width * live
    return (
        segment,
        grid_row.reshape(-1).astype(jnp.float32),
        grid_col.reshape(-1).astype(jnp.float32),
    )


def rotary_tables(frequencies, grid_row, grid_col):
    half_width = frequencies.shape[0] // 2
    freq_float = frequencies.astype(jnp.float32)
    freq_row = freq_float[:half_width].reshape(H, HD // 2)
    freq_col = freq_float[half_width:].reshape(H, HD // 2)
    theta = grid_row[:, None, None] * freq_row[None] + grid_col[:, None, None] * freq_col[None]
    return (jnp.cos(theta), jnp.sin(theta))


def rotate(heads, cosine, sine):
    half_width = heads.shape[-1] // 2
    first = heads[..., :half_width]
    second = heads[..., half_width:]
    return jnp.concatenate(
        [first * cosine - second * sine, first * sine + second * cosine], axis=-1
    )


def layer_norm_forward(values):
    center = values - jnp.mean(values, axis=-1, keepdims=True)
    inverse_deviation = lax.rsqrt(jnp.mean(center * center, axis=-1, keepdims=True) + norm_eps)
    return (center * inverse_deviation, inverse_deviation)


def layer_norm_backward(
    gradient_norm_total, centered_normalized, inverse_deviation, norm_gain_vector
):
    gain_scaled_output = gradient_norm_total * norm_gain_vector
    return inverse_deviation * (
        gain_scaled_output
        - jnp.mean(gain_scaled_output, axis=-1, keepdims=True)
        - centered_normalized
        * jnp.mean(gain_scaled_output * centered_normalized, axis=-1, keepdims=True)
    )


def gelu_slope(values):
    return (
        0.5 * (1.0 + lax.erf(values * 0.7071067811865476))
        + values * jnp.exp(-0.5 * values * values) * inv_sqrt_two_pi
    )


def _nt(a, b):
    return lax.dot_general(a, b, (((1,), (1,)), ((), ())), preferred_element_type=jnp.float32)


def _tn(a, b):
    return lax.dot_general(a, b, (((0,), (0,)), ((), ())), preferred_element_type=jnp.float32)


def _nn(a, b):
    return lax.dot_general(a, b, (((1,), (0,)), ((), ())), preferred_element_type=jnp.float32)


def build_bias(seg_r_ref, seg_c_ref, bias_ref):
    @pl.when(pl.program_id(0) == 0)
    def _():
        bias_ref[...] = jnp.where(seg_r_ref[...] == seg_c_ref[...], 0.0, masked_score).astype(jnp.float32)


def attention_forward_kernel(q_ref, k_ref, v_ref, seg_r_ref, seg_c_ref, o_ref, lse_ref, bias_ref):
    rows = q_ref.shape[0]
    scale = HD ** (-0.5)
    build_bias(seg_r_ref, seg_c_ref, bias_ref)
    for half in range(q_ref.shape[1] // HD):
        cols = slice(half * HD, (half + 1) * HD)
        k_h = k_ref[:, cols]
        v_h = v_ref[:, cols]

        def block(i, carry):
            at = pl.multiple_of(i * Q_BLOCK, Q_BLOCK)
            q_h = q_ref[pl.ds(at, Q_BLOCK), cols]
            scores = _nt(q_h, k_h) * scale + bias_ref[pl.ds(at, Q_BLOCK), :]
            top = jnp.max(scores, axis=-1, keepdims=True)
            log_total = top + jnp.log(jnp.sum(jnp.exp(scores - top), axis=-1, keepdims=True))
            probs = jnp.exp(scores - log_total).astype(jnp.bfloat16)
            o_ref[pl.ds(at, Q_BLOCK), cols] = _nn(probs, v_h).astype(o_ref.dtype)
            lse_ref[pl.ds(at, Q_BLOCK), cols] = jnp.broadcast_to(log_total, (Q_BLOCK, HD))
            return carry

        lax.fori_loop(0, rows // Q_BLOCK, block, 0)


def attention_backward_kernel(q_ref, k_ref, v_ref, d_ref, lse_ref, seg_r_ref, seg_c_ref, dq_ref, dk_ref, dv_ref, bias_ref):
    rows = q_ref.shape[0]
    scale = HD ** (-0.5)
    build_bias(seg_r_ref, seg_c_ref, bias_ref)
    for half in range(q_ref.shape[1] // HD):
        cols = slice(half * HD, (half + 1) * HD)
        k_h = k_ref[:, cols]
        v_h = v_ref[:, cols]

        def block(i, carry):
            dk_acc, dv_acc = carry
            at = pl.multiple_of(i * Q_BLOCK, Q_BLOCK)
            q_h = q_ref[pl.ds(at, Q_BLOCK), cols]
            d_h = d_ref[pl.ds(at, Q_BLOCK), cols]
            log_total = lse_ref[pl.ds(at, Q_BLOCK), pl.ds(half * HD, 1)]
            scores = _nt(q_h, k_h) * scale + bias_ref[pl.ds(at, Q_BLOCK), :]
            probs = jnp.exp(scores - log_total)
            d_probs = _nt(d_h, v_h)
            dv_acc = dv_acc + _tn(probs.astype(jnp.bfloat16), d_h)
            inner = jnp.sum(probs * d_probs, axis=-1, keepdims=True)
            d_scores = (probs * (d_probs - inner)).astype(jnp.bfloat16)
            dq_ref[pl.ds(at, Q_BLOCK), cols] = _nn(d_scores, k_h) * scale
            dk_acc = dk_acc + _tn(d_scores, q_h)
            return dk_acc, dv_acc

        zero = jnp.zeros((rows, HD), jnp.float32)
        dk_acc, dv_acc = lax.fori_loop(0, rows // Q_BLOCK, block, (zero, zero))
        dk_ref[:, cols] = dk_acc * scale
        dv_ref[:, cols] = dv_acc


def attention_forward(q, k, v, segment):
    rows, width = q.shape
    pair = 2 * HD
    seg_r = segment.reshape(rows, 1)
    seg_c = segment.reshape(1, rows)
    spec = pl.BlockSpec((rows, pair), lambda j: (0, j))
    return pl.pallas_call(
        attention_forward_kernel,
        grid=(width // pair,),
        in_specs=[spec, spec, spec, pl.BlockSpec((rows, 1), lambda j: (0, 0)), pl.BlockSpec((1, rows), lambda j: (0, 0))],
        out_specs=[spec, spec],
        out_shape=[jax.ShapeDtypeStruct((rows, width), jnp.bfloat16), jax.ShapeDtypeStruct((rows, width), jnp.float32)],
        scratch_shapes=[pltpu.VMEM((rows, rows), jnp.float32)],
        cost_estimate=pl.CostEstimate(
            flops=4 * rows * rows * width, transcendentals=2 * rows * rows * (width // HD),
            bytes_accessed=rows * width * (2 * 4 + 4)),
        name="attention_forward",
    )(q, k, v, seg_r, seg_c)


def attention_backward(q, k, v, d_mixed, log_total, segment):
    rows, width = q.shape
    pair = 2 * HD
    seg_r = segment.reshape(rows, 1)
    seg_c = segment.reshape(1, rows)
    spec = pl.BlockSpec((rows, pair), lambda j: (0, j))
    f32 = jax.ShapeDtypeStruct((rows, width), jnp.float32)
    return pl.pallas_call(
        attention_backward_kernel,
        grid=(width // pair,),
        in_specs=[spec, spec, spec, spec, spec, pl.BlockSpec((rows, 1), lambda j: (0, 0)), pl.BlockSpec((1, rows), lambda j: (0, 0))],
        out_specs=[spec, spec, spec],
        out_shape=[f32, f32, f32],
        scratch_shapes=[pltpu.VMEM((rows, rows), jnp.float32)],
        cost_estimate=pl.CostEstimate(
            flops=8 * rows * rows * width, transcendentals=rows * rows * (width // HD),
            bytes_accessed=rows * width * (2 * 4 + 4 + 12)),
        name="attention_backward",
    )(q, k, v, d_mixed, log_total, seg_r, seg_c)


def attention_bins(q_low, k_low, v_low, segment):
    outs = [attention_forward(q_low[b * BIN:(b + 1) * BIN], k_low[b * BIN:(b + 1) * BIN],
                              v_low[b * BIN:(b + 1) * BIN], segment[b]) for b in range(segment.shape[0])]
    return tuple(jnp.concatenate(parts, axis=0) for parts in zip(*outs))


def attention_bins_back(q_low, k_low, v_low, d_mixed, log_total, segment):
    outs = [attention_backward(q_low[b * BIN:(b + 1) * BIN], k_low[b * BIN:(b + 1) * BIN],
                               v_low[b * BIN:(b + 1) * BIN], d_mixed[b * BIN:(b + 1) * BIN],
                               log_total[b * BIN:(b + 1) * BIN], segment[b]) for b in range(segment.shape[0])]
    return tuple(jnp.concatenate(parts, axis=0) for parts in zip(*outs))


def quarter(shard):
    part = shard.shape[0] // lax.psum(1, "dp")
    return lax.dynamic_slice_in_dim(shard, lax.axis_index("dp") * part, part, 0)


def gather_with_small(left, right, vectors):
    rows = quarter(left).shape[0]
    flat = quarter(jnp.concatenate(vectors))
    cols = -(-flat.shape[0] // rows)
    tile = jnp.pad(flat, (0, rows * cols - flat.shape[0])).reshape(rows, cols)
    tile = jnp.pad(tile, ((0, 0), (0, -cols % 128)))
    joined = jnp.concatenate([quarter(left), quarter(right), tile], axis=1)
    whole = lax.all_gather(joined, ("fsdp", "dp"), axis=0, tiled=True)
    split = left.shape[1] + right.shape[1]
    groups = lax.psum(1, "fsdp")
    small = whole[:, split : split + cols].reshape(lax.psum(1, ("fsdp", "dp")), -1)[:, : flat.shape[0]]
    small = small.reshape(groups, -1)
    out, at = [], 0
    for v in vectors:
        out.append(small[:, at : at + v.shape[0]].reshape(-1))
        at += v.shape[0]
    return whole[:, : left.shape[1]], whole[:, left.shape[1] : split], out


def gather_alone(shard):
    return lax.all_gather(quarter(shard), ("fsdp", "dp"), axis=0, tiled=True)


def pack_columns(matrices, vectors):
    blocks = lax.psum(1, ("fsdp", "dp"))
    rows = matrices[0].shape[0]
    per_block = rows // blocks
    flat = jnp.concatenate([v.reshape(blocks, -1) for v in vectors], axis=1)
    small = flat.shape[1]
    small_cols = -(-small // per_block)
    flat = jnp.pad(flat, ((0, 0), (0, small_cols * per_block - small)))
    flat = flat.reshape(rows, small_cols)
    padded_cols = -(-small_cols // 128) * 128
    flat = jnp.pad(flat, ((0, 0), (0, padded_cols - small_cols)))
    parts = [m.astype(jnp.bfloat16) for m in matrices] + [flat.astype(jnp.bfloat16)]
    layout = ([m.shape[1] for m in matrices], small_cols, padded_cols, [v.shape[0] // blocks for v in vectors])
    return jnp.concatenate(parts, axis=1), layout


def unpack_columns(owned, layout):
    widths, small_cols, _, vector_sizes = layout
    groups = lax.psum(1, "dp")
    out, at = [], 0
    for w in widths:
        out.append(owned[:, at : at + w].astype(jnp.float32))
        at += w
    flat = owned[:, at : at + small_cols].reshape(groups, -1)
    vectors, at = [], 0
    for n in vector_sizes:
        vectors.append(flat[:, at : at + n].reshape(-1).astype(jnp.float32))
        at += n
    return out, vectors


def square_sums_of_block(mine, layout, last_vectors):
    widths, small_cols, _, vector_sizes = layout
    values = mine.astype(jnp.float32)
    at = sum(widths)
    flat = values[:, at : at + small_cols].reshape(-1)
    split = sum(vector_sizes[: len(vector_sizes) - last_vectors])
    end = sum(vector_sizes)
    last = jnp.sum(flat[split:end] * flat[split:end])
    rest = jnp.sum(values[:, :at] * values[:, :at]) + jnp.sum(flat[:split] * flat[:split])
    return last, rest


def sum_on_sparse_core(packed, layout):
    mine = lax.psum_scatter(packed, ("fsdp", "dp"), scatter_dimension=0, tiled=True)
    owned = lax.all_gather(mine, "dp", axis=0, tiled=True)
    return unpack_columns(owned, layout), mine


def sum_by_exchange(packed, layout, carried):
    blocks = lax.psum(1, ("fsdp", "dp"))
    received = lax.all_to_all(packed, ("fsdp", "dp"), 0, 0, tiled=True)
    mine = jnp.sum(received.reshape(blocks, -1, packed.shape[1]).astype(jnp.float32), axis=0)
    freq_part, rest_part = square_sums_of_block(mine, layout, 1)
    rest_part = rest_part + carried
    pair = jnp.stack([freq_part, rest_part])
    high = pair.astype(jnp.bfloat16)
    low = (pair - high.astype(jnp.float32)).astype(jnp.bfloat16)
    extra = jnp.zeros((mine.shape[0], 128), jnp.bfloat16).at[0, 0:2].set(high).at[0, 2:4].set(low)
    owned = lax.all_gather(
        jnp.concatenate([mine.astype(jnp.bfloat16), extra], axis=1), "dp", axis=0, tiled=True
    )
    tile = owned[:: mine.shape[0], packed.shape[1] : packed.shape[1] + 4].astype(jnp.float32)
    partials = jnp.sum(tile[:, 0:2] + tile[:, 2:4], axis=0)
    return unpack_columns(owned[:, : packed.shape[1]], layout), partials


def shards(
    tokens,
    image_table,
    ln1_gain,
    ln1_bias,
    qkv_weight,
    qkv_bias,
    out_weight,
    out_bias,
    ln2_gain,
    ln2_bias,
    fc1_weight,
    fc1_bias,
    fc2_weight,
    fc2_bias,
    frequencies,
    cotangent,
):
    small_local = [ln1_gain, ln1_bias, qkv_bias, out_bias, ln2_gain, ln2_bias, fc1_bias, fc2_bias, frequencies]
    g_qkv_weight, g_out_weight, small_whole = gather_with_small(qkv_weight, out_weight, small_local)
    (g_ln1_gain, g_ln1_bias, g_qkv_bias, g_out_bias, g_ln2_gain, g_ln2_bias, g_fc1_bias, g_fc2_bias,
     g_frequencies) = small_whole
    g_fc1_weight = gather_alone(fc1_weight)
    g_fc2_weight = gather_alone(fc2_weight)
    block_parameters = (
        g_ln1_gain,
        g_ln1_bias,
        g_qkv_weight,
        g_qkv_bias,
        g_out_weight,
        g_out_bias,
        g_ln2_gain,
        g_ln2_bias,
        g_fc1_weight,
        g_fc1_bias,
        g_fc2_weight,
        g_fc2_bias,
        g_frequencies,
    )
    row_count, width = tokens.shape
    bin_count = row_count // BIN
    half_head = HD // 2
    segment, grid_row, grid_col = image_layout(image_table, bin_count, BIN)
    cosine, sine = rotary_tables(block_parameters[12], grid_row, grid_col)
    input_single_precision = tokens.astype(jnp.float32)
    first_centered_normalized, first_inverse_deviation = layer_norm_forward(input_single_precision)
    first_activation = (
        first_centered_normalized * block_parameters[0].astype(jnp.float32)
        + block_parameters[1].astype(jnp.float32)
    ).astype(jnp.bfloat16)
    qkv_full = matmul(first_activation, block_parameters[2]) + block_parameters[3].astype(
        jnp.float32
    )
    q_rot = rotate(qkv_full[:, :width].reshape(row_count, H, HD), cosine, sine)
    k_rot = rotate(qkv_full[:, width : 2 * width].reshape(row_count, H, HD), cosine, sine)
    q_low = q_rot.reshape(row_count, width).astype(jnp.bfloat16)
    k_low = k_rot.reshape(row_count, width).astype(jnp.bfloat16)
    v_low = qkv_full[:, 2 * width :].astype(jnp.bfloat16)
    mixed, log_total = attention_bins(q_low, k_low, v_low, segment)
    residual_stream = (
        input_single_precision
        + matmul(mixed, block_parameters[4])
        + block_parameters[5].astype(jnp.float32)
    )
    second_centered_normalized, second_inverse_deviation = layer_norm_forward(residual_stream)
    second_activation = (
        second_centered_normalized * block_parameters[6].astype(jnp.float32)
        + block_parameters[7].astype(jnp.float32)
    ).astype(jnp.bfloat16)
    up_proj = matmul(second_activation, block_parameters[8]) + block_parameters[9].astype(
        jnp.float32
    )
    gelu_low = jax.nn.gelu(up_proj, approximate=False).astype(jnp.bfloat16)
    fc2_weight_grad = matmul_left_t(gelu_low, cotangent)
    fc2_recut = fc2_weight_grad.reshape(width, -1).astype(jnp.bfloat16)
    block_out = (
        residual_stream
        + matmul(gelu_low, block_parameters[10])
        + block_parameters[11].astype(jnp.float32)
    ).astype(jnp.bfloat16)
    output_gradient = cotangent.astype(jnp.float32)
    fc2_bias_grad = jnp.sum(output_gradient, axis=0)
    d_up = (matmul_right_t(cotangent, block_parameters[10]) * gelu_slope(up_proj)).astype(
        jnp.bfloat16
    )
    fc1_bias_grad = jnp.sum(d_up.astype(jnp.float32), axis=0)
    fc1_weight_grad = matmul_left_t(second_activation, d_up)
    second_activation_gradient = matmul_right_t(d_up, block_parameters[8])
    second_norm_gain_gradient = jnp.sum(
        second_activation_gradient * second_centered_normalized, axis=0
    )
    ln2_bias_grad = jnp.sum(second_activation_gradient, axis=0)
    residual_gradient = output_gradient + layer_norm_backward(
        second_activation_gradient,
        second_centered_normalized,
        second_inverse_deviation,
        block_parameters[6].astype(jnp.float32),
    )
    d_att = residual_gradient.astype(jnp.bfloat16)
    out_bias_grad = jnp.sum(d_att.astype(jnp.float32), axis=0)
    out_weight_grad = matmul_left_t(mixed, d_att)
    d_mixed = matmul_right_t(d_att, block_parameters[4]).astype(jnp.bfloat16)
    early_packed, early_layout = pack_columns(
        [fc2_recut, fc1_weight_grad, out_weight_grad],
        [fc2_bias_grad, fc1_bias_grad, out_bias_grad, second_norm_gain_gradient, ln2_bias_grad],
    )
    early_packed, d_mixed = lax.optimization_barrier((early_packed, d_mixed))
    (early_mats, early_vecs), early_mine = sum_on_sparse_core(early_packed, early_layout)
    d_qrot, d_krot, d_value = attention_bins_back(q_low, k_low, v_low, d_mixed, log_total, segment)
    d_qrot = d_qrot.reshape(row_count, H, HD)
    d_krot = d_krot.reshape(row_count, H, HD)
    d_theta = (
        d_qrot[..., half_head:] * q_rot[..., :half_head]
        - d_qrot[..., :half_head] * q_rot[..., half_head:]
    )
    d_theta = (
        d_theta
        + d_krot[..., half_head:] * k_rot[..., :half_head]
        - d_krot[..., :half_head] * k_rot[..., half_head:]
    )
    frequencies_grad = jnp.concatenate(
        [
            jnp.sum(grid_row[:, None, None] * d_theta, axis=0).reshape(-1),
            jnp.sum(grid_col[:, None, None] * d_theta, axis=0).reshape(-1),
        ]
    )
    d_query = rotate(d_qrot, cosine, -sine).reshape(row_count, width)
    d_key = rotate(d_krot, cosine, -sine).reshape(row_count, width)
    d_qkv = jnp.concatenate([d_query, d_key, d_value.reshape(row_count, width)], axis=1).astype(
        jnp.bfloat16
    )
    qkv_bias_grad = jnp.sum(d_qkv.astype(jnp.float32), axis=0)
    qkv_weight_grad = matmul_left_t(first_activation, d_qkv)
    first_activation_gradient = matmul_right_t(d_qkv, block_parameters[2])
    first_norm_gain_gradient = jnp.sum(
        first_activation_gradient * first_centered_normalized, axis=0
    )
    ln1_bias_grad = jnp.sum(first_activation_gradient, axis=0)
    tokens_grad = (
        residual_gradient
        + layer_norm_backward(
            first_activation_gradient,
            first_centered_normalized,
            first_inverse_deviation,
            block_parameters[0].astype(jnp.float32),
        )
    ).astype(jnp.bfloat16)
    late_packed, late_layout = pack_columns(
        [qkv_weight_grad],
        [qkv_bias_grad, first_norm_gain_gradient, ln1_bias_grad, frequencies_grad],
    )
    late_packed, tokens_grad = lax.optimization_barrier((late_packed, tokens_grad))
    _, early_sq = square_sums_of_block(early_mine, early_layout, 0)
    (late_mats, late_vecs), partials = sum_by_exchange(late_packed, late_layout, early_sq)
    freq_sq, other_sq = lax.psum((partials[0], partials[1]), "fsdp")
    fc2_weight_g = early_mats[0].reshape(fc2_weight.shape)
    fc1_weight_g = early_mats[1]
    out_weight_g = early_mats[2]
    fc2_bias_g, fc1_bias_g, out_bias_g, ln2_gain_g, ln2_bias_g = early_vecs
    qkv_weight_g = late_mats[0]
    qkv_bias_g, ln1_gain_g, ln1_bias_g, frequencies_g = late_vecs
    pieces = (
        ln1_gain_g,
        ln1_bias_g,
        qkv_weight_g,
        qkv_bias_g,
        out_weight_g,
        out_bias_g,
        ln2_gain_g,
        ln2_bias_g,
        fc1_weight_g,
        fc1_bias_g,
        fc2_weight_g,
        fc2_bias_g,
        frequencies_g,
    )
    return (
        block_out,
        tokens_grad,
        *pieces,
        jnp.sqrt(freq_sq),
        jnp.sqrt(other_sq),
    )


def solution(mesh):
    placed = (
        P(("fsdp", "dp"), None),
        P(("fsdp", "dp"), None),
        P("fsdp"),
        P("fsdp"),
        P("fsdp", None),
        P("fsdp"),
        P("fsdp", None),
        P("fsdp"),
        P("fsdp"),
        P("fsdp"),
        P("fsdp", None),
        P("fsdp"),
        P("fsdp", None),
        P("fsdp"),
        P("fsdp"),
        P(("fsdp", "dp"), None),
    )
    return jax.shard_map(
        shards,
        mesh=mesh,
        in_specs=placed,
        out_specs=(
            P(("fsdp", "dp"), None),
            P(("fsdp", "dp"), None),
            P("fsdp"),
            P("fsdp"),
            P("fsdp", None),
            P("fsdp"),
            P("fsdp", None),
            P("fsdp"),
            P("fsdp"),
            P("fsdp"),
            P("fsdp", None),
            P("fsdp"),
            P("fsdp", None),
            P("fsdp"),
            P("fsdp"),
            P(),
            P(),
        ),
        check_vma=False,
    )
```
